32 devices in a mesh: blk: 8 (over y, x, core), rep: 4 (over z).
Axes of the slice: x: 2, y: 2, z: 4, core: 2. Of those that a mesh axis runs over, the one named last changes fastest.
Arguments:
- picture_averaged_features: bfloat16 [4, 512, 1152], P('rep', 'blk'), may hold values from -0.23925781 to 0.23925781
- caption_averaged_features: bfloat16 [4, 512, 1152], P('rep', 'blk'), may hold values from -0.23925781 to 0.23925781
- picture_rescale_factor: float32 [1152], replicated, may hold values from 0.1 to 1.9
- caption_rescale_factor: float32 [1152], replicated, may hold values from 0.1 to 1.9
- exponent_of_sharpness: float32 [1], replicated, may hold values from 1.8 to 2.6
- score_shift_term: float32 [1], replicated, may hold values from -8 to -4
- objective_multiplier: float32 [1], replicated, may hold values from 512 to 2048
- matching_caption_index: int32 [4, 512], P('rep'), may hold values from 0 to 511, each once within a row
- genuine_entry_counts: int32 [4, 8], P('rep'), may hold values from 1 to 64, 384 in all within a row
Outputs:
- image_grad: bfloat16 [4, 512, 1152], P('rep', 'blk')
- text_grad: bfloat16 [4, 512, 1152], P('rep', 'blk')
- gain_grads: float32 [2, 1152], replicated
- group_loss: float32 [4], P('rep')
The draws below stay inside these ranges and needn't reach their ends.
Inputs may be any that keep to these rules, and one draw needn't show every extreme that they name: `matching_caption_index`: each group's row of positives is a permutation of 0 to 511. `genuine_entry_counts`: each group's counts sum to 384, and some block of every group is full.
All inputs are finite; a program needn't handle non-finite values.
Results may differ from the reference program's by a relative error of at most 0.0058.
Values may be sent and summed in bfloat16 or wider, within the bound.
No kernel may reach another device: no remote copies, remote signals or barrier semaphores. Data moves between devices by JAX's collectives and lax.ppermute only.
A program may use at most 64 MiB of HBM per device.

```python
import math
import jax
import jax.numpy as jnp
import numpy as np
from jax import lax

D = 1152
B_DEV = 64
NB = 512
GROUPS = 4
N_BLK = 8


def shard_levels(own_key, dims, shards, least, largest):
    level, own = 1.0, jax.random.fold_in(own_key, 6)
    for dim, blocks in shards:
        heights = jnp.exp(jax.random.uniform(jax.random.fold_in(own, dim), (blocks,), jnp.float32, least / len(shards), largest / len(shards)))
        level = level * jnp.repeat(heights, dims[dim] // blocks).reshape([-1 if axis == dim else 1 for axis in range(len(dims))])
    return level


def length_profile(amount, total, reach, slope):
    portions = [(1 << 20) // math.isqrt(grade ** slope) + 1 for grade in range(2, amount + 1)]
    spare, counts = total - reach - (amount - 1), [1] * (amount - 1)
    while spare > 0:
        candidates = [i for i in range(amount - 1) if counts[i] < reach]
        whole, budget = sum([portions[i] for i in candidates]), spare
        for i in candidates:
            more = min(reach - counts[i], max(1, budget * portions[i] // whole), spare)
            counts[i] = counts[i] + more
            spare = spare - more
    return np.array([reach] + counts)


def uneven_parts(stream_key, number_of, total, limit, skew):
    if number_of == 2:
        one = jax.random.randint(stream_key, (), max(1, total - limit), min(limit, total - 1) + 1)
        return jnp.stack([one, total - one])
    lengths = jnp.asarray(length_profile(number_of, total, limit, skew), jnp.int32)
    couples = (number_of - 1) // 2
    donor, sink = lengths[1:1 + 2 * couples:2], lengths[2:2 + 2 * couples:2]
    room = jnp.minimum(donor - 1, limit - sink)
    shifted = jax.random.randint(jax.random.fold_in(stream_key, 1), (couples,), 0, 1 << 20) % (room + 1)
    lengths = lengths.at[1:1 + 2 * couples:2].set(donor - shifted).at[2:2 + 2 * couples:2].set(sink + shifted)
    return lengths[jax.random.permutation(jax.random.fold_in(stream_key, 2), number_of)]


def scatter_about(key, extent, spread, bound, split=(), dtype=jnp.bfloat16):
    level = shard_levels(key, extent, split, -0.22, 0.18) if split else 1.0
    drawn = jax.random.normal(key, extent, jnp.float32) * spread * level
    return jnp.minimum(jnp.maximum(drawn, -bound), bound).astype(dtype)


def setup_inputs(seed: int = 0) -> dict:
    seeds = jax.random.split(jax.random.key(seed), 10)
    picture_averaged_features = scatter_about(seeds[0], (GROUPS, NB, D), 0.04, 0.23925781, ((0, 4), (1, 8)))
    caption_averaged_features = scatter_about(seeds[1], (GROUPS, NB, D), 0.04, 0.23925781, ((0, 4), (1, 8)))
    picture_rescale_factor = jnp.clip(1.0 + 0.18 * jax.random.normal(seeds[2], (D,), jnp.float32), 0.1, 1.9)
    caption_rescale_factor = jnp.clip(1.0 + 0.18 * jax.random.normal(seeds[3], (D,), jnp.float32), 0.1, 1.9)
    exponent_of_sharpness = jnp.clip(jax.random.uniform(seeds[4], (1,), jnp.float32, 1.8, 2.6), 1.8, 2.6)
    score_shift_term = jnp.clip(jax.random.uniform(seeds[5], (1,), jnp.float32, -8.0, -4.0), -8.0, -4.0)
    objective_multiplier = jnp.clip(jnp.exp(jax.random.uniform(seeds[6], (1,), jnp.float32, math.log(512.0), math.log(2048.0))), 512.0, 2048.0)
    matching_caption_index = jax.vmap(lambda own: jax.random.permutation(own, NB))(jax.random.split(seeds[7], GROUPS)).reshape((GROUPS, NB)).astype(jnp.int32)
    genuine_entry_counts = jax.vmap(lambda own: uneven_parts(own, N_BLK, 3 * NB // 4, B_DEV, 1))(jax.random.split(seeds[8], GROUPS)).reshape((GROUPS, N_BLK)).astype(jnp.int32)
    return dict(picture_averaged_features=picture_averaged_features, caption_averaged_features=caption_averaged_features, picture_rescale_factor=picture_rescale_factor, caption_rescale_factor=caption_rescale_factor, exponent_of_sharpness=exponent_of_sharpness, score_shift_term=score_shift_term, objective_multiplier=objective_multiplier, matching_caption_index=matching_caption_index, genuine_entry_counts=genuine_entry_counts)


epsilon = 1e-06

def embed_rows(pooled, gain):
    values = pooled.astype(jnp.float32)
    centred = values - lax.optimization_barrier(jnp.mean(values, axis=-1, keepdims=True))
    inverse = lax.rsqrt(lax.optimization_barrier(jnp.mean(centred * centred, axis=-1, keepdims=True)) + epsilon)
    normed = centred * inverse
    scaled = normed * gain
    inv_length = lax.rsqrt(lax.optimization_barrier(jnp.sum(scaled * scaled, axis=-1, keepdims=True)) + epsilon)
    return (scaled * inv_length, normed, inverse, inv_length)

def embed_back(direction, unit_rows, normed, inverse, inv_length, gain):
    tangent = (direction - unit_rows * lax.optimization_barrier(jnp.sum(unit_rows * direction, axis=-1, keepdims=True))) * inv_length
    gain_part = lax.optimization_barrier(jnp.sum(tangent * normed, axis=0))
    scaled = tangent * gain
    gradient = (scaled - lax.optimization_barrier(jnp.mean(scaled, axis=-1, keepdims=True)) - normed * lax.optimization_barrier(jnp.mean(scaled * normed, axis=-1, keepdims=True))) * inverse
    return (gradient, gain_part)

def reference(picture_averaged_features, caption_averaged_features, picture_rescale_factor, caption_rescale_factor, exponent_of_sharpness, score_shift_term, objective_multiplier, matching_caption_index, genuine_entry_counts):
    score_sharpness_factor = jnp.exp(exponent_of_sharpness[0])
    score_shift_amount = score_shift_term[0]
    within = (jnp.arange(NB) % B_DEV).astype(jnp.int32)
    owner = (jnp.arange(NB) // B_DEV).astype(jnp.int32)
    columns = jnp.arange(NB).astype(jnp.int32)

    def one_group(inputs):
        image_rows, text_rows, partner, block_counts = inputs
        image_unit_rows, image_normalized, image_inverse_length, image_length = embed_rows(image_rows, picture_rescale_factor)
        text_unit_rows, text_normalized, text_inverse_length, text_length = embed_rows(text_rows, caption_rescale_factor)
        picture_feature_entries = image_unit_rows.astype(jnp.bfloat16)
        caption_feature_entries = text_unit_rows.astype(jnp.bfloat16)
        real_rows = within < block_counts[owner]
        real_count = jnp.sum(block_counts).astype(jnp.float32)
        angle_similarity_table = jnp.dot(picture_feature_entries, caption_feature_entries.T, preferred_element_type=jnp.float32)
        score_similarity_table = score_sharpness_factor * angle_similarity_table + score_shift_amount
        labels = jnp.where(partner[:, None] == columns[None, :], 1.0, -1.0).astype(jnp.float32)
        kept_pairs = real_rows[:, None] & real_rows[None, :]
        margin = -labels * score_similarity_table
        loss_sum = jnp.sum(jnp.where(kept_pairs, jax.nn.softplus(margin), 0.0)) / real_count
        couple_importance_factor = (jnp.where(kept_pairs, -labels * jax.nn.sigmoid(margin), 0.0) * (objective_multiplier[0] / real_count)).astype(jnp.bfloat16)
        picture_heading_vector = score_sharpness_factor * jnp.dot(couple_importance_factor, caption_feature_entries, preferred_element_type=jnp.float32)
        caption_heading_vector = score_sharpness_factor * jnp.dot(couple_importance_factor.T, picture_feature_entries, preferred_element_type=jnp.float32)
        image_gradient, image_part = embed_back(picture_heading_vector, image_unit_rows, image_normalized, image_inverse_length, image_length, picture_rescale_factor)
        text_gradient, text_part = embed_back(caption_heading_vector, text_unit_rows, text_normalized, text_inverse_length, text_length, caption_rescale_factor)
        return (image_gradient.astype(jnp.bfloat16), text_gradient.astype(jnp.bfloat16), jnp.stack([image_part, text_part]), loss_sum)
    image_grad, text_grad, gain_parts, losses = lax.map(one_group, (picture_averaged_features, caption_averaged_features, matching_caption_index, genuine_entry_counts))
    return (image_grad, text_grad, lax.optimization_barrier(jnp.sum(gain_parts, axis=0)), losses)
```

```python
import jax
import jax.numpy as jnp
from jax import lax
from jax.sharding import PartitionSpec as P

epsilon = 1e-06


def embed_rows(pooled, gain):
    values = pooled.astype(jnp.float32)
    centred = values - jnp.mean(values, axis=-1, keepdims=True)
    inverse = lax.rsqrt(jnp.mean(centred * centred, axis=-1, keepdims=True) + epsilon)
    normed = centred * inverse
    scaled = normed * gain
    inv_length = lax.rsqrt(jnp.sum(scaled * scaled, axis=-1, keepdims=True) + epsilon)
    return (scaled * inv_length, normed, inverse, inv_length)


def embed_back(direction, unit_rows, normed, inverse, inv_length, gain):
    tangent = (
        direction - unit_rows * jnp.sum(unit_rows * direction, axis=-1, keepdims=True)
    ) * inv_length
    gain_part = jnp.sum(tangent * normed, axis=0)
    scaled = tangent * gain
    gradient = (
        scaled
        - jnp.mean(scaled, axis=-1, keepdims=True)
        - normed * jnp.mean(scaled * normed, axis=-1, keepdims=True)
    ) * inverse
    return (gradient, gain_part)


def pair_weights(scores, labels_pos, kept, score_sharpness_factor, score_shift_amount, grad_factor):
    score_similarity_table = score_sharpness_factor * scores + score_shift_amount
    labels = jnp.where(labels_pos, 1.0, -1.0).astype(jnp.float32)
    margin = -labels * score_similarity_table
    loss_sum = jnp.sum(jnp.where(kept, jax.nn.softplus(margin), 0.0))
    weights = jnp.where(kept, -labels * jax.nn.sigmoid(margin), 0.0) * grad_factor
    return loss_sum, weights.astype(jnp.bfloat16)


def shards(
    picture_averaged_features,
    caption_averaged_features,
    picture_rescale_factor,
    caption_rescale_factor,
    exponent_of_sharpness,
    score_shift_term,
    objective_multiplier,
    matching_caption_index,
    genuine_entry_counts,
):
    block_rows = picture_averaged_features.shape[1]
    members = lax.axis_size("blk")
    own_block = lax.axis_index("blk")
    group_rows = block_rows * members
    image_unit_rows, image_normalized, image_inverse_length, image_length = embed_rows(
        picture_averaged_features[0], picture_rescale_factor
    )
    text_unit_rows, text_normalized, text_inverse_length, text_length = embed_rows(
        caption_averaged_features[0], caption_rescale_factor
    )
    picture_feature_entries = image_unit_rows.astype(jnp.bfloat16)
    caption_feature_entries = text_unit_rows.astype(jnp.bfloat16)
    block_counts = genuine_entry_counts[0]
    partner = matching_caption_index[0]
    real_count = jnp.sum(block_counts).astype(jnp.float32)
    score_sharpness_factor = jnp.exp(exponent_of_sharpness[0])
    score_shift_amount = score_shift_term[0]
    grad_factor = objective_multiplier[0] / real_count

    both = jnp.stack([picture_feature_entries, caption_feature_entries])
    gathered = lax.all_gather(both, "blk", axis=1, tiled=True)
    image_all = gathered[0]
    text_all = gathered[1]

    rows = jnp.arange(group_rows, dtype=jnp.int32)
    real_all = (rows % block_rows) < block_counts[rows // block_rows]
    own_rows = jnp.arange(block_rows, dtype=jnp.int32)
    real_own = own_rows < lax.dynamic_index_in_dim(block_counts, own_block, keepdims=False)
    own_start = own_block * block_rows
    own_partner = lax.dynamic_slice_in_dim(partner, own_start, block_rows)

    row_scores = lax.dot_general(
        picture_feature_entries, text_all, (((1,), (1,)), ((), ())),
        preferred_element_type=jnp.float32,
    )
    row_pos = own_partner[:, None] == rows[None, :]
    row_kept = real_own[:, None] & real_all[None, :]
    loss_sum, row_weights = pair_weights(
        row_scores, row_pos, row_kept, score_sharpness_factor, score_shift_amount, grad_factor
    )
    image_direction = jnp.dot(row_weights, text_all, preferred_element_type=jnp.float32)

    col_scores = lax.dot_general(
        image_all, caption_feature_entries, (((1,), (1,)), ((), ())),
        preferred_element_type=jnp.float32,
    )
    col_pos = partner[:, None] == (own_start + own_rows)[None, :]
    col_kept = real_all[:, None] & real_own[None, :]
    unused, col_weights = pair_weights(
        col_scores, col_pos, col_kept, score_sharpness_factor, score_shift_amount, grad_factor
    )
    text_direction = lax.dot_general(
        col_weights, image_all, (((0,), (0,)), ((), ())),
        preferred_element_type=jnp.float32,
    )

    image_gradient, image_part = embed_back(
        score_sharpness_factor * image_direction,
        image_unit_rows,
        image_normalized,
        image_inverse_length,
        image_length,
        picture_rescale_factor,
    )
    text_gradient, text_part = embed_back(
        score_sharpness_factor * text_direction,
        text_unit_rows,
        text_normalized,
        text_inverse_length,
        text_length,
        caption_rescale_factor,
    )
    replicas = lax.axis_size("rep")
    group_index = lax.axis_index("rep")
    loss_vector = jnp.where(
        jnp.arange(replicas, dtype=jnp.int32) == group_index, loss_sum / real_count, 0.0
    )
    width = image_part.shape[0]
    flat = jnp.concatenate([image_part, text_part, loss_vector])
    total = lax.psum(flat, ("blk", "rep"))
    gain_grads = total[: 2 * width].reshape(2, width)
    group_loss = lax.dynamic_slice_in_dim(total[2 * width:], group_index, 1)
    return (
        image_gradient.astype(jnp.bfloat16)[None],
        text_gradient.astype(jnp.bfloat16)[None],
        gain_grads,
        group_loss,
    )


def solution(mesh):
    placed = (
        P("rep", "blk", None),
        P("rep", "blk", None),
        P(),
        P(),
        P(),
        P(),
        P(),
        P("rep", None),
        P("rep", None),
    )
    return jax.shard_map(
        shards,
        mesh=mesh,
        in_specs=placed,
        out_specs=(P("rep", "blk", None), P("rep", "blk", None), P(), P("rep")),
        check_vma=False,
    )
```

```python
import jax
import jax.numpy as jnp
from jax import lax
from jax.sharding import PartitionSpec as P

epsilon = 1e-06


def xor_swap(value, axis, bit):
    count = lax.axis_size(axis)
    return lax.ppermute(value, axis, [(source, source ^ bit) for source in range(count)])


def power_of_two(count):
    return count > 1 and count & (count - 1) == 0


def gather_blocks(both, axis):
    count = lax.axis_size(axis)
    rows = both.shape[1]
    if not power_of_two(count) or count < 4 or rows % 2:
        gathered = lax.all_gather(both, axis, axis=1, tiled=False)
        return gathered, list(range(count)), [0] * count, True
    chip_bits = [1 << b for b in range(1, count.bit_length() - 1)]
    half = rows // 2
    halves = [
        [both[:, None, :half], [0], chip_bits],
        [both[:, None, half:], [0], chip_bits[::-1]],
    ]
    for step in range(len(chip_bits)):
        for held in halves:
            bit = held[2][step]
            held[0] = jnp.concatenate([held[0], xor_swap(held[0], axis, bit)], axis=1)
            held[1] = held[1] + [mask ^ bit for mask in held[1]]
    for held in halves:
        held[0] = jnp.concatenate([held[0], xor_swap(held[0], axis, 1)], axis=1)
        held[1] = held[1] + [mask ^ 1 for mask in held[1]]
    gathered = jnp.concatenate([halves[0][0], halves[1][0]], axis=1)
    masks = halves[0][1] + halves[1][1]
    offsets = [0] * count + [half] * count
    return gathered, masks, offsets, False


def all_sum(value, axes):
    for axis in axes:
        count = lax.axis_size(axis)
        if not power_of_two(count):
            value = lax.psum(value, axis)
            continue
        bit = 1
        while bit < count:
            value = value + xor_swap(value, axis, bit)
            bit *= 2
    return value


def embed_rows(pooled, gain):
    values = pooled.astype(jnp.float32)
    centred = values - jnp.mean(values, axis=-1, keepdims=True)
    inverse = lax.rsqrt(jnp.mean(centred * centred, axis=-1, keepdims=True) + epsilon)
    normed = centred * inverse
    scaled = normed * gain
    inv_length = lax.rsqrt(jnp.sum(scaled * scaled, axis=-1, keepdims=True) + epsilon)
    return (scaled * inv_length, normed, inverse, inv_length)


def embed_back(direction, unit_rows, normed, inverse, inv_length, gain):
    tangent = (
        direction - unit_rows * jnp.sum(unit_rows * direction, axis=-1, keepdims=True)
    ) * inv_length
    gain_part = jnp.sum(tangent * normed, axis=0)
    scaled = tangent * gain
    gradient = (
        scaled
        - jnp.mean(scaled, axis=-1, keepdims=True)
        - normed * jnp.mean(scaled * normed, axis=-1, keepdims=True)
    ) * inverse
    return (gradient, gain_part)


def pair_weights(scores, labels_pos, kept, score_sharpness_factor, score_shift_amount, grad_factor):
    score_similarity_table = score_sharpness_factor * scores + score_shift_amount
    labels = jnp.where(labels_pos, 1.0, -1.0).astype(jnp.float32)
    margin = -labels * score_similarity_table
    loss_sum = jnp.sum(jnp.where(kept, jax.nn.softplus(margin), 0.0))
    weights = jnp.where(kept, -labels * jax.nn.sigmoid(margin), 0.0) * grad_factor
    return loss_sum, weights.astype(jnp.bfloat16)


def shards(
    picture_averaged_features,
    caption_averaged_features,
    picture_rescale_factor,
    caption_rescale_factor,
    exponent_of_sharpness,
    score_shift_term,
    objective_multiplier,
    matching_caption_index,
    genuine_entry_counts,
):
    block_rows = picture_averaged_features.shape[1]
    own_block = lax.axis_index("blk")
    image_unit_rows, image_normalized, image_inverse_length, image_length = embed_rows(
        picture_averaged_features[0], picture_rescale_factor
    )
    text_unit_rows, text_normalized, text_inverse_length, text_length = embed_rows(
        caption_averaged_features[0], caption_rescale_factor
    )
    picture_feature_entries = image_unit_rows.astype(jnp.bfloat16)
    caption_feature_entries = text_unit_rows.astype(jnp.bfloat16)
    block_counts = genuine_entry_counts[0]
    partner = matching_caption_index[0]
    real_count = jnp.sum(block_counts).astype(jnp.float32)
    score_sharpness_factor = jnp.exp(exponent_of_sharpness[0])
    score_shift_amount = score_shift_term[0]
    grad_factor = objective_multiplier[0] / real_count

    both = jnp.stack([picture_feature_entries, caption_feature_entries])
    gathered, masks, offsets, natural = gather_blocks(both, "blk")
    positions = gathered.shape[1]
    piece = gathered.shape[2]
    image_all = gathered[0].reshape(positions * piece, -1)
    text_all = gathered[1].reshape(positions * piece, -1)
    if natural:
        held_block = jnp.arange(positions, dtype=jnp.int32)
    else:
        held_block = own_block ^ jnp.asarray(masks, jnp.int32)
    first_row = jnp.asarray(offsets, jnp.int32)[:, None] + jnp.arange(piece, dtype=jnp.int32)[None, :]
    rows = (held_block[:, None] * block_rows + first_row).reshape(-1)
    real_all = (first_row < block_counts[held_block][:, None]).reshape(-1)
    own_rows = jnp.arange(block_rows, dtype=jnp.int32)
    real_own = own_rows < lax.dynamic_index_in_dim(block_counts, own_block, keepdims=False)
    own_start = own_block * block_rows
    own_partner = lax.dynamic_slice_in_dim(partner, own_start, block_rows)
    held_partner = partner[rows]

    row_scores = lax.dot_general(
        picture_feature_entries, text_all, (((1,), (1,)), ((), ())),
        preferred_element_type=jnp.float32,
    )
    row_pos = own_partner[:, None] == rows[None, :]
    row_kept = real_own[:, None] & real_all[None, :]
    loss_sum, row_weights = pair_weights(
        row_scores, row_pos, row_kept, score_sharpness_factor, score_shift_amount, grad_factor
    )
    image_direction = jnp.dot(row_weights, text_all, preferred_element_type=jnp.float32)

    col_scores = lax.dot_general(
        image_all, caption_feature_entries, (((1,), (1,)), ((), ())),
        preferred_element_type=jnp.float32,
    )
    col_pos = held_partner[:, None] == (own_start + own_rows)[None, :]
    col_kept = real_all[:, None] & real_own[None, :]
    unused, col_weights = pair_weights(
        col_scores, col_pos, col_kept, score_sharpness_factor, score_shift_amount, grad_factor
    )
    text_direction = lax.dot_general(
        col_weights, image_all, (((0,), (0,)), ((), ())),
        preferred_element_type=jnp.float32,
    )

    image_gradient, image_part = embed_back(
        score_sharpness_factor * image_direction,
        image_unit_rows,
        image_normalized,
        image_inverse_length,
        image_length,
        picture_rescale_factor,
    )
    text_gradient, text_part = embed_back(
        score_sharpness_factor * text_direction,
        text_unit_rows,
        text_normalized,
        text_inverse_length,
        text_length,
        caption_rescale_factor,
    )
    replicas = lax.axis_size("rep")
    group_index = lax.axis_index("rep")
    loss_vector = jnp.where(
        jnp.arange(replicas, dtype=jnp.int32) == group_index, loss_sum / real_count, 0.0
    )
    width = image_part.shape[0]
    flat = jnp.concatenate([image_part, text_part, loss_vector])
    total = all_sum(flat, ("blk", "rep"))
    gain_grads = total[: 2 * width].reshape(2, width)
    group_loss = lax.dynamic_slice_in_dim(total[2 * width:], group_index, 1)
    return (
        image_gradient.astype(jnp.bfloat16)[None],
        text_gradient.astype(jnp.bfloat16)[None],
        gain_grads,
        group_loss,
    )


def solution(mesh):
    placed = (
        P("rep", "blk", None),
        P("rep", "blk", None),
        P(),
        P(),
        P(),
        P(),
        P(),
        P("rep", None),
        P("rep", None),
    )
    return jax.shard_map(
        shards,
        mesh=mesh,
        in_specs=placed,
        out_specs=(P("rep", "blk", None), P("rep", "blk", None), P(), P("rep")),
        check_vma=False,
    )
```

```python
import jax
import jax.numpy as jnp
from jax import lax
from jax.sharding import PartitionSpec as P

epsilon = 1e-06


def xor_swap(value, axis, bit):
    count = lax.axis_size(axis)
    return lax.ppermute(value, axis, [(source, source ^ bit) for source in range(count)])


def power_of_two(count):
    return count > 1 and count & (count - 1) == 0


def gather_blocks(both, axis):
    count = lax.axis_size(axis)
    rows = both.shape[1]
    if not power_of_two(count) or count < 4 or rows % 2:
        gathered = lax.all_gather(both, axis, axis=1, tiled=False)
        return gathered, list(range(count)), [0] * count, True
    chip_bits = [1 << b for b in range(1, count.bit_length() - 1)]
    half = rows // 2
    orders = (chip_bits + [1], chip_bits[::-1] + [1])
    pieces = ([both[:, :half]], [both[:, half:]])
    held = ([0], [0])
    for step in range(len(chip_bits) + 1):
        sent = [xor_swap(tuple(pieces[h]), axis, orders[h][step]) for h in range(2)]
        for h in range(2):
            bit = orders[h][step]
            pieces[h].extend(sent[h])
            held[h].extend([mask ^ bit for mask in held[h]])
    gathered = jnp.stack(pieces[0] + pieces[1], axis=1)
    masks = held[0] + held[1]
    offsets = [0] * count + [half] * count
    return gathered, masks, offsets, False


def all_sum(value, axes):
    for axis in axes:
        count = lax.axis_size(axis)
        if not power_of_two(count):
            value = lax.psum(value, axis)
            continue
        bit = 1
        while bit < count:
            value = value + xor_swap(value, axis, bit)
            bit *= 2
    return value


def embed_rows(pooled, gain):
    values = pooled.astype(jnp.float32)
    centred = values - jnp.mean(values, axis=-1, keepdims=True)
    inverse = lax.rsqrt(jnp.mean(centred * centred, axis=-1, keepdims=True) + epsilon)
    normed = centred * inverse
    scaled = normed * gain
    inv_length = lax.rsqrt(jnp.sum(scaled * scaled, axis=-1, keepdims=True) + epsilon)
    return (scaled * inv_length, normed, inverse, inv_length)


def embed_back(direction, unit_rows, normed, inverse, inv_length, gain):
    tangent = (
        direction - unit_rows * jnp.sum(unit_rows * direction, axis=-1, keepdims=True)
    ) * inv_length
    gain_part = jnp.sum(tangent * normed, axis=0)
    scaled = tangent * gain
    gradient = (
        scaled
        - jnp.mean(scaled, axis=-1, keepdims=True)
        - normed * jnp.mean(scaled * normed, axis=-1, keepdims=True)
    ) * inverse
    return (gradient, gain_part)


def pair_weights(scores, labels_pos, kept, score_sharpness_factor, score_shift_amount, grad_factor):
    score_similarity_table = score_sharpness_factor * scores + score_shift_amount
    labels = jnp.where(labels_pos, 1.0, -1.0).astype(jnp.float32)
    margin = -labels * score_similarity_table
    loss_sum = jnp.sum(jnp.where(kept, jax.nn.softplus(margin), 0.0))
    weights = jnp.where(kept, -labels * jax.nn.sigmoid(margin), 0.0) * grad_factor
    return loss_sum, weights.astype(jnp.bfloat16)


def shards(
    picture_averaged_features,
    caption_averaged_features,
    picture_rescale_factor,
    caption_rescale_factor,
    exponent_of_sharpness,
    score_shift_term,
    objective_multiplier,
    matching_caption_index,
    genuine_entry_counts,
):
    block_rows = picture_averaged_features.shape[1]
    own_block = lax.axis_index("blk")
    image_unit_rows, image_normalized, image_inverse_length, image_length = embed_rows(
        picture_averaged_features[0], picture_rescale_factor
    )
    text_unit_rows, text_normalized, text_inverse_length, text_length = embed_rows(
        caption_averaged_features[0], caption_rescale_factor
    )
    picture_feature_entries = image_unit_rows.astype(jnp.bfloat16)
    caption_feature_entries = text_unit_rows.astype(jnp.bfloat16)
    block_counts = genuine_entry_counts[0]
    partner = matching_caption_index[0]
    real_count = jnp.sum(block_counts).astype(jnp.float32)
    score_sharpness_factor = jnp.exp(exponent_of_sharpness[0])
    score_shift_amount = score_shift_term[0]
    grad_factor = objective_multiplier[0] / real_count

    both = jnp.stack([picture_feature_entries, caption_feature_entries])
    gathered, masks, offsets, natural = gather_blocks(both, "blk")
    positions = gathered.shape[1]
    piece = gathered.shape[2]
    image_all = gathered[0].reshape(positions * piece, -1)
    text_all = gathered[1].reshape(positions * piece, -1)
    if natural:
        held_block = jnp.arange(positions, dtype=jnp.int32)
    else:
        held_block = own_block ^ jnp.asarray(masks, jnp.int32)
    first_row = jnp.asarray(offsets, jnp.int32)[:, None] + jnp.arange(piece, dtype=jnp.int32)[None, :]
    rows = (held_block[:, None] * block_rows + first_row).reshape(-1)
    real_all = (first_row < block_counts[held_block][:, None]).reshape(-1)
    own_rows = jnp.arange(block_rows, dtype=jnp.int32)
    real_own = own_rows < lax.dynamic_index_in_dim(block_counts, own_block, keepdims=False)
    own_start = own_block * block_rows
    own_partner = lax.dynamic_slice_in_dim(partner, own_start, block_rows)
    held_partner = partner[rows]

    row_scores = lax.dot_general(
        picture_feature_entries, text_all, (((1,), (1,)), ((), ())),
        preferred_element_type=jnp.float32,
    )
    row_pos = own_partner[:, None] == rows[None, :]
    row_kept = real_own[:, None] & real_all[None, :]
    loss_sum, row_weights = pair_weights(
        row_scores, row_pos, row_kept, score_sharpness_factor, score_shift_amount, grad_factor
    )
    image_direction = jnp.dot(row_weights, text_all, preferred_element_type=jnp.float32)

    col_scores = lax.dot_general(
        image_all, caption_feature_entries, (((1,), (1,)), ((), ())),
        preferred_element_type=jnp.float32,
    )
    col_pos = held_partner[:, None] == (own_start + own_rows)[None, :]
    col_kept = real_all[:, None] & real_own[None, :]
    unused, col_weights = pair_weights(
        col_scores, col_pos, col_kept, score_sharpness_factor, score_shift_amount, grad_factor
    )
    text_direction = lax.dot_general(
        col_weights, image_all, (((0,), (0,)), ((), ())),
        preferred_element_type=jnp.float32,
    )

    image_gradient, image_part = embed_back(
        score_sharpness_factor * image_direction,
        image_unit_rows,
        image_normalized,
        image_inverse_length,
        image_length,
        picture_rescale_factor,
    )
    text_gradient, text_part = embed_back(
        score_sharpness_factor * text_direction,
        text_unit_rows,
        text_normalized,
        text_inverse_length,
        text_length,
        caption_rescale_factor,
    )
    replicas = lax.axis_size("rep")
    group_index = lax.axis_index("rep")
    loss_vector = jnp.where(
        jnp.arange(replicas, dtype=jnp.int32) == group_index, loss_sum / real_count, 0.0
    )
    width = image_part.shape[0]
    flat = jnp.concatenate([image_part, text_part, loss_vector])
    total = all_sum(flat, ("blk", "rep"))
    gain_grads = total[: 2 * width].reshape(2, width)
    group_loss = lax.dynamic_slice_in_dim(total[2 * width:], group_index, 1)
    return (
        image_gradient.astype(jnp.bfloat16)[None],
        text_gradient.astype(jnp.bfloat16)[None],
        gain_grads,
        group_loss,
    )


def solution(mesh):
    placed = (
        P("rep", "blk", None),
        P("rep", "blk", None),
        P(),
        P(),
        P(),
        P(),
        P(),
        P("rep", None),
        P("rep", None),
    )
    return jax.shard_map(
        shards,
        mesh=mesh,
        in_specs=placed,
        out_specs=(P("rep", "blk", None), P("rep", "blk", None), P(), P("rep")),
        check_vma=False,
    )
```

```python
import jax
import jax.numpy as jnp
from jax import lax
from jax.sharding import PartitionSpec as P

epsilon = 1e-06


def xor_swap(value, axis, bit):
    count = lax.axis_size(axis)
    return lax.ppermute(value, axis, [(source, source ^ bit) for source in range(count)])


def power_of_two(count):
    return count > 1 and count & (count - 1) == 0


def gather_blocks(both, axis):
    count = lax.axis_size(axis)
    rows = both.shape[1]
    if not power_of_two(count) or count < 4 or rows % 2:
        gathered = lax.all_gather(both, axis, axis=1, tiled=False)
        return gathered, list(range(count)), [0] * count, True
    chip_bits = [1 << b for b in range(1, count.bit_length() - 1)]
    half = rows // 2
    orders = (chip_bits, chip_bits[::-1])
    routed = ([both[:, :half]], [both[:, half:]])
    routed_masks = ([0], [0])
    fresh = ([0], [0])
    shared = ([], [])
    shared_masks = ([], [])
    for step in range(len(chip_bits) + 1):
        last = step == len(chip_bits)
        sent = [None, None]
        if not last:
            sent = [xor_swap(tuple(routed[h]), axis, orders[h][step]) for h in range(2)]
        across = [xor_swap(tuple(routed[h][i] for i in fresh[h]), axis, 1) for h in range(2)]
        for h in range(2):
            shared[h].extend(across[h])
            shared_masks[h].extend([routed_masks[h][i] ^ 1 for i in fresh[h]])
            if not last:
                bit = orders[h][step]
                fresh[h][:] = list(range(len(routed[h]), 2 * len(routed[h])))
                routed[h].extend(sent[h])
                routed_masks[h].extend([mask ^ bit for mask in routed_masks[h]])
    gathered = jnp.stack(routed[0] + shared[0] + routed[1] + shared[1], axis=1)
    masks = routed_masks[0] + shared_masks[0] + routed_masks[1] + shared_masks[1]
    offsets = [0] * count + [half] * count
    return gathered, masks, offsets, False


def all_sum(value, axes):
    for axis in axes:
        count = lax.axis_size(axis)
        if not power_of_two(count):
            value = lax.psum(value, axis)
            continue
        bit = 1
        while bit < count:
            value = value + xor_swap(value, axis, bit)
            bit *= 2
    return value


def embed_rows(pooled, gain):
    values = pooled.astype(jnp.float32)
    centred = values - jnp.mean(values, axis=-1, keepdims=True)
    inverse = lax.rsqrt(jnp.mean(centred * centred, axis=-1, keepdims=True) + epsilon)
    normed = centred * inverse
    scaled = normed * gain
    inv_length = lax.rsqrt(jnp.sum(scaled * scaled, axis=-1, keepdims=True) + epsilon)
    return (scaled * inv_length, normed, inverse, inv_length)


def embed_back(direction, unit_rows, normed, inverse, inv_length, gain):
    tangent = (
        direction - unit_rows * jnp.sum(unit_rows * direction, axis=-1, keepdims=True)
    ) * inv_length
    gain_part = jnp.sum(tangent * normed, axis=0)
    scaled = tangent * gain
    gradient = (
        scaled
        - jnp.mean(scaled, axis=-1, keepdims=True)
        - normed * jnp.mean(scaled * normed, axis=-1, keepdims=True)
    ) * inverse
    return (gradient, gain_part)


def pair_weights(scores, labels_pos, kept, score_sharpness_factor, score_shift_amount, grad_factor):
    score_similarity_table = score_sharpness_factor * scores + score_shift_amount
    labels = jnp.where(labels_pos, 1.0, -1.0).astype(jnp.float32)
    margin = -labels * score_similarity_table
    loss_sum = jnp.sum(jnp.where(kept, jax.nn.softplus(margin), 0.0))
    weights = jnp.where(kept, -labels * jax.nn.sigmoid(margin), 0.0) * grad_factor
    return loss_sum, weights.astype(jnp.bfloat16)


def shards(
    picture_averaged_features,
    caption_averaged_features,
    picture_rescale_factor,
    caption_rescale_factor,
    exponent_of_sharpness,
    score_shift_term,
    objective_multiplier,
    matching_caption_index,
    genuine_entry_counts,
):
    block_rows = picture_averaged_features.shape[1]
    own_block = lax.axis_index("blk")
    image_unit_rows, image_normalized, image_inverse_length, image_length = embed_rows(
        picture_averaged_features[0], picture_rescale_factor
    )
    text_unit_rows, text_normalized, text_inverse_length, text_length = embed_rows(
        caption_averaged_features[0], caption_rescale_factor
    )
    picture_feature_entries = image_unit_rows.astype(jnp.bfloat16)
    caption_feature_entries = text_unit_rows.astype(jnp.bfloat16)
    block_counts = genuine_entry_counts[0]
    partner = matching_caption_index[0]
    real_count = jnp.sum(block_counts).astype(jnp.float32)
    score_sharpness_factor = jnp.exp(exponent_of_sharpness[0])
    score_shift_amount = score_shift_term[0]
    grad_factor = objective_multiplier[0] / real_count

    both = jnp.stack([picture_feature_entries, caption_feature_entries])
    gathered, masks, offsets, natural = gather_blocks(both, "blk")
    positions = gathered.shape[1]
    piece = gathered.shape[2]
    image_all = gathered[0].reshape(positions * piece, -1)
    text_all = gathered[1].reshape(positions * piece, -1)
    if natural:
        held_block = jnp.arange(positions, dtype=jnp.int32)
    else:
        held_block = own_block ^ jnp.asarray(masks, jnp.int32)
    first_row = jnp.asarray(offsets, jnp.int32)[:, None] + jnp.arange(piece, dtype=jnp.int32)[None, :]
    rows = (held_block[:, None] * block_rows + first_row).reshape(-1)
    real_all = (first_row < block_counts[held_block][:, None]).reshape(-1)
    own_rows = jnp.arange(block_rows, dtype=jnp.int32)
    real_own = own_rows < lax.dynamic_index_in_dim(block_counts, own_block, keepdims=False)
    own_start = own_block * block_rows
    own_partner = lax.dynamic_slice_in_dim(partner, own_start, block_rows)
    own_texts = own_start + own_rows
    matched_image = jnp.sum(
        jnp.where(partner[:, None] == own_texts[None, :], jnp.arange(partner.shape[0], dtype=jnp.int32)[:, None], 0),
        axis=0,
    )

    row_scores = lax.dot_general(
        picture_feature_entries, text_all, (((1,), (1,)), ((), ())),
        preferred_element_type=jnp.float32,
    )
    row_pos = own_partner[:, None] == rows[None, :]
    row_kept = real_own[:, None] & real_all[None, :]
    loss_sum, row_weights = pair_weights(
        row_scores, row_pos, row_kept, score_sharpness_factor, score_shift_amount, grad_factor
    )
    image_direction = jnp.dot(row_weights, text_all, preferred_element_type=jnp.float32)

    col_scores = lax.dot_general(
        image_all, caption_feature_entries, (((1,), (1,)), ((), ())),
        preferred_element_type=jnp.float32,
    )
    col_pos = rows[:, None] == matched_image[None, :]
    col_kept = real_all[:, None] & real_own[None, :]
    unused, col_weights = pair_weights(
        col_scores, col_pos, col_kept, score_sharpness_factor, score_shift_amount, grad_factor
    )
    text_direction = lax.dot_general(
        col_weights, image_all, (((0,), (0,)), ((), ())),
        preferred_element_type=jnp.float32,
    )

    image_gradient, image_part = embed_back(
        score_sharpness_factor * image_direction,
        image_unit_rows,
        image_normalized,
        image_inverse_length,
        image_length,
        picture_rescale_factor,
    )
    text_gradient, text_part = embed_back(
        score_sharpness_factor * text_direction,
        text_unit_rows,
        text_normalized,
        text_inverse_length,
        text_length,
        caption_rescale_factor,
    )
    replicas = lax.axis_size("rep")
    group_index = lax.axis_index("rep")
    loss_vector = jnp.where(
        jnp.arange(replicas, dtype=jnp.int32) == group_index, loss_sum / real_count, 0.0
    )
    width = image_part.shape[0]
    flat = jnp.concatenate([image_part, text_part, loss_vector])
    total = all_sum(flat, ("blk", "rep"))
    gain_grads = total[: 2 * width].reshape(2, width)
    group_loss = lax.dynamic_slice_in_dim(total[2 * width:], group_index, 1)
    return (
        image_gradient.astype(jnp.bfloat16)[None],
        text_gradient.astype(jnp.bfloat16)[None],
        gain_grads,
        group_loss,
    )


def solution(mesh):
    placed = (
        P("rep", "blk", None),
        P("rep", "blk", None),
        P(),
        P(),
        P(),
        P(),
        P(),
        P("rep", None),
        P("rep", None),
    )
    return jax.shard_map(
        shards,
        mesh=mesh,
        in_specs=placed,
        out_specs=(P("rep", "blk", None), P("rep", "blk", None), P(), P("rep")),
        check_vma=False,
    )
```

```python
import jax
import jax.numpy as jnp
from jax import lax
from jax.sharding import PartitionSpec as P
from jax.experimental import pallas as pl
from jax.experimental.pallas import tpu as pltpu

epsilon = 1e-06


def xor_swap(value, axis, bit):
    count = lax.axis_size(axis)
    return lax.ppermute(value, axis, [(source, source ^ bit) for source in range(count)])


def power_of_two(count):
    return count > 1 and count & (count - 1) == 0


def gather_blocks(both, axis):
    count = lax.axis_size(axis)
    rows = both.shape[1]
    if not power_of_two(count) or count < 4 or rows % 2:
        gathered = lax.all_gather(both, axis, axis=1, tiled=False)
        return gathered, list(range(count)), [0] * count, True
    chip_bits = [1 << b for b in range(1, count.bit_length() - 1)]
    half = rows // 2
    orders = (chip_bits, chip_bits[::-1])
    routed = ([both[:, :half]], [both[:, half:]])
    routed_masks = ([0], [0])
    fresh = ([0], [0])
    shared = ([], [])
    shared_masks = ([], [])
    for step in range(len(chip_bits) + 1):
        last = step == len(chip_bits)
        sent = [None, None]
        if not last:
            sent = [xor_swap(tuple(routed[h]), axis, orders[h][step]) for h in range(2)]
        across = [xor_swap(tuple(routed[h][i] for i in fresh[h]), axis, 1) for h in range(2)]
        for h in range(2):
            shared[h].extend(across[h])
            shared_masks[h].extend([routed_masks[h][i] ^ 1 for i in fresh[h]])
            if not last:
                bit = orders[h][step]
                fresh[h][:] = list(range(len(routed[h]), 2 * len(routed[h])))
                routed[h].extend(sent[h])
                routed_masks[h].extend([mask ^ bit for mask in routed_masks[h]])
    gathered = jnp.stack(routed[0] + shared[0] + routed[1] + shared[1], axis=1)
    masks = routed_masks[0] + shared_masks[0] + routed_masks[1] + shared_masks[1]
    offsets = [0] * count + [half] * count
    return gathered, masks, offsets, False


def all_sum(value, axes):
    for axis in axes:
        count = lax.axis_size(axis)
        if not power_of_two(count):
            value = lax.psum(value, axis)
            continue
        bit = 1
        while bit < count:
            value = value + xor_swap(value, axis, bit)
            bit *= 2
    return value


def embed_kernel(picture_ref, caption_ref, picture_gain_ref, caption_gain_ref, out_ref):
    towers = ((picture_ref, picture_gain_ref), (caption_ref, caption_gain_ref))
    for tower, (pooled_ref, gain_ref) in enumerate(towers):
        values = pooled_ref[...].astype(jnp.float32)
        centred = values - jnp.mean(values, axis=-1, keepdims=True)
        inverse = lax.rsqrt(jnp.mean(centred * centred, axis=-1, keepdims=True) + epsilon)
        scaled = centred * inverse * gain_ref[...]
        inv_length = lax.rsqrt(jnp.sum(scaled * scaled, axis=-1, keepdims=True) + epsilon)
        out_ref[tower] = (scaled * inv_length).astype(out_ref.dtype)


def embed_both(picture, caption, picture_gain, caption_gain):
    rows, width = picture.shape
    vmem = pltpu.MemorySpace.VMEM
    return pl.pallas_call(
        embed_kernel,
        out_shape=jax.ShapeDtypeStruct((2, rows, width), jnp.bfloat16),
        in_specs=[pl.BlockSpec(memory_space=vmem)] * 4,
        out_specs=pl.BlockSpec(memory_space=vmem),
    )(picture, caption, picture_gain.reshape(1, width), caption_gain.reshape(1, width))


def embed_rows(pooled, gain):
    values = pooled.astype(jnp.float32)
    centred = values - jnp.mean(values, axis=-1, keepdims=True)
    inverse = lax.rsqrt(jnp.mean(centred * centred, axis=-1, keepdims=True) + epsilon)
    normed = centred * inverse
    scaled = normed * gain
    inv_length = lax.rsqrt(jnp.sum(scaled * scaled, axis=-1, keepdims=True) + epsilon)
    return (scaled * inv_length, normed, inverse, inv_length)


def embed_back(direction, unit_rows, normed, inverse, inv_length, gain):
    tangent = (
        direction - unit_rows * jnp.sum(unit_rows * direction, axis=-1, keepdims=True)
    ) * inv_length
    gain_part = jnp.sum(tangent * normed, axis=0)
    scaled = tangent * gain
    gradient = (
        scaled
        - jnp.mean(scaled, axis=-1, keepdims=True)
        - normed * jnp.mean(scaled * normed, axis=-1, keepdims=True)
    ) * inverse
    return (gradient, gain_part)


def pair_weights(scores, labels_pos, kept, score_sharpness_factor, score_shift_amount, grad_factor):
    score_similarity_table = score_sharpness_factor * scores + score_shift_amount
    labels = jnp.where(labels_pos, 1.0, -1.0).astype(jnp.float32)
    margin = -labels * score_similarity_table
    loss_sum = jnp.sum(jnp.where(kept, jax.nn.softplus(margin), 0.0))
    weights = jnp.where(kept, -labels * jax.nn.sigmoid(margin), 0.0) * grad_factor
    return loss_sum, weights.astype(jnp.bfloat16)


def shards(
    picture_averaged_features,
    caption_averaged_features,
    picture_rescale_factor,
    caption_rescale_factor,
    exponent_of_sharpness,
    score_shift_term,
    objective_multiplier,
    matching_caption_index,
    genuine_entry_counts,
):
    block_rows = picture_averaged_features.shape[1]
    own_block = lax.axis_index("blk")
    image_unit_rows, image_normalized, image_inverse_length, image_length = embed_rows(
        picture_averaged_features[0], picture_rescale_factor
    )
    text_unit_rows, text_normalized, text_inverse_length, text_length = embed_rows(
        caption_averaged_features[0], caption_rescale_factor
    )
    both = embed_both(
        picture_averaged_features[0],
        caption_averaged_features[0],
        picture_rescale_factor,
        caption_rescale_factor,
    )
    picture_feature_entries = both[0]
    caption_feature_entries = both[1]
    block_counts = genuine_entry_counts[0]
    partner = matching_caption_index[0]
    real_count = jnp.sum(block_counts).astype(jnp.float32)
    score_sharpness_factor = jnp.exp(exponent_of_sharpness[0])
    score_shift_amount = score_shift_term[0]
    grad_factor = objective_multiplier[0] / real_count

    gathered, masks, offsets, natural = gather_blocks(both, "blk")
    positions = gathered.shape[1]
    piece = gathered.shape[2]
    image_all = gathered[0].reshape(positions * piece, -1)
    text_all = gathered[1].reshape(positions * piece, -1)
    if natural:
        held_block = jnp.arange(positions, dtype=jnp.int32)
    else:
        held_block = own_block ^ jnp.asarray(masks, jnp.int32)
    first_row = jnp.asarray(offsets, jnp.int32)[:, None] + jnp.arange(piece, dtype=jnp.int32)[None, :]
    rows = (held_block[:, None] * block_rows + first_row).reshape(-1)
    real_all = (first_row < block_counts[held_block][:, None]).reshape(-1)
    own_rows = jnp.arange(block_rows, dtype=jnp.int32)
    real_own = own_rows < lax.dynamic_index_in_dim(block_counts, own_block, keepdims=False)
    own_start = own_block * block_rows
    own_partner = lax.dynamic_slice_in_dim(partner, own_start, block_rows)
    own_texts = own_start + own_rows
    matched_image = jnp.sum(
        jnp.where(partner[:, None] == own_texts[None, :], jnp.arange(partner.shape[0], dtype=jnp.int32)[:, None], 0),
        axis=0,
    )

    row_scores = lax.dot_general(
        picture_feature_entries, text_all, (((1,), (1,)), ((), ())),
        preferred_element_type=jnp.float32,
    )
    row_pos = own_partner[:, None] == rows[None, :]
    row_kept = real_own[:, None] & real_all[None, :]
    loss_sum, row_weights = pair_weights(
        row_scores, row_pos, row_kept, score_sharpness_factor, score_shift_amount, grad_factor
    )
    image_direction = jnp.dot(row_weights, text_all, preferred_element_type=jnp.float32)

    col_scores = lax.dot_general(
        image_all, caption_feature_entries, (((1,), (1,)), ((), ())),
        preferred_element_type=jnp.float32,
    )
    col_pos = rows[:, None] == matched_image[None, :]
    col_kept = real_all[:, None] & real_own[None, :]
    unused, col_weights = pair_weights(
        col_scores, col_pos, col_kept, score_sharpness_factor, score_shift_amount, grad_factor
    )
    text_direction = lax.dot_general(
        col_weights, image_all, (((0,), (0,)), ((), ())),
        preferred_element_type=jnp.float32,
    )

    image_gradient, image_part = embed_back(
        score_sharpness_factor * image_direction,
        image_unit_rows,
        image_normalized,
        image_inverse_length,
        image_length,
        picture_rescale_factor,
    )
    text_gradient, text_part = embed_back(
        score_sharpness_factor * text_direction,
        text_unit_rows,
        text_normalized,
        text_inverse_length,
        text_length,
        caption_rescale_factor,
    )
    replicas = lax.axis_size("rep")
    group_index = lax.axis_index("rep")
    loss_vector = jnp.where(
        jnp.arange(replicas, dtype=jnp.int32) == group_index, loss_sum / real_count, 0.0
    )
    width = image_part.shape[0]
    flat = jnp.concatenate([image_part, text_part, loss_vector])
    total = all_sum(flat, ("blk", "rep"))
    gain_grads = total[: 2 * width].reshape(2, width)
    group_loss = lax.dynamic_slice_in_dim(total[2 * width:], group_index, 1)
    return (
        image_gradient.astype(jnp.bfloat16)[None],
        text_gradient.astype(jnp.bfloat16)[None],
        gain_grads,
        group_loss,
    )


def solution(mesh):
    placed = (
        P("rep", "blk", None),
        P("rep", "blk", None),
        P(),
        P(),
        P(),
        P(),
        P(),
        P("rep", None),
        P("rep", None),
    )
    return jax.shard_map(
        shards,
        mesh=mesh,
        in_specs=placed,
        out_specs=(P("rep", "blk", None), P("rep", "blk", None), P(), P("rep")),
        check_vma=False,
    )
```

```python
import jax
import jax.numpy as jnp
from jax import lax
from jax.sharding import PartitionSpec as P
from jax.experimental import pallas as pl
from jax.experimental.pallas import tpu as pltpu

epsilon = 1e-06


def xor_swap(value, axis, bit):
    count = lax.axis_size(axis)
    return lax.ppermute(value, axis, [(source, source ^ bit) for source in range(count)])


def power_of_two(count):
    return count > 1 and count & (count - 1) == 0


def gather_blocks(both, axis):
    count = lax.axis_size(axis)
    rows = both.shape[1]
    if not power_of_two(count) or count < 4 or rows % 2:
        gathered = lax.all_gather(both, axis, axis=1, tiled=False)
        return gathered, list(range(count)), [0] * count, True
    chip_bits = [1 << b for b in range(1, count.bit_length() - 1)]
    half = rows // 2
    orders = (chip_bits, chip_bits[::-1])
    routed = ([both[:, :half]], [both[:, half:]])
    routed_masks = ([0], [0])
    fresh = ([0], [0])
    shared = ([], [])
    shared_masks = ([], [])
    for step in range(len(chip_bits) + 1):
        last = step == len(chip_bits)
        sent = [None, None]
        if not last:
            sent = [xor_swap(tuple(routed[h]), axis, orders[h][step]) for h in range(2)]
        across = [xor_swap(tuple(routed[h][i] for i in fresh[h]), axis, 1) for h in range(2)]
        for h in range(2):
            shared[h].extend(across[h])
            shared_masks[h].extend([routed_masks[h][i] ^ 1 for i in fresh[h]])
            if not last:
                bit = orders[h][step]
                fresh[h][:] = list(range(len(routed[h]), 2 * len(routed[h])))
                routed[h].extend(sent[h])
                routed_masks[h].extend([mask ^ bit for mask in routed_masks[h]])
    gathered = routed[0] + shared[0] + routed[1] + shared[1]
    masks = routed_masks[0] + shared_masks[0] + routed_masks[1] + shared_masks[1]
    offsets = [0] * count + [half] * count
    return gathered, masks, offsets, False


def all_sum(value, axes):
    for axis in axes:
        count = lax.axis_size(axis)
        if not power_of_two(count):
            value = lax.psum(value, axis)
            continue
        bit = 1
        while bit < count:
            value = value + xor_swap(value, axis, bit)
            bit *= 2
    return value


def embed_kernel(pooled_ref, gain_ref, out_ref):
    for tower in range(2):
        values = pooled_ref[tower].astype(jnp.float32)
        centred = values - jnp.mean(values, axis=-1, keepdims=True)
        inverse = lax.rsqrt(jnp.mean(centred * centred, axis=-1, keepdims=True) + epsilon)
        scaled = centred * inverse * gain_ref[tower : tower + 1, :]
        inv_length = lax.rsqrt(jnp.sum(scaled * scaled, axis=-1, keepdims=True) + epsilon)
        out_ref[tower] = (scaled * inv_length).astype(out_ref.dtype)


def embed_both(pooled, gains):
    vmem = pltpu.MemorySpace.VMEM
    return pl.pallas_call(
        embed_kernel,
        out_shape=jax.ShapeDtypeStruct(pooled.shape, jnp.bfloat16),
        in_specs=[pl.BlockSpec(memory_space=vmem)] * 2,
        out_specs=pl.BlockSpec(memory_space=vmem),
    )(pooled, gains)


def embed_rows(pooled, gain):
    values = pooled.astype(jnp.float32)
    centred = values - jnp.mean(values, axis=-1, keepdims=True)
    inverse = lax.rsqrt(jnp.mean(centred * centred, axis=-1, keepdims=True) + epsilon)
    normed = centred * inverse
    scaled = normed * gain
    inv_length = lax.rsqrt(jnp.sum(scaled * scaled, axis=-1, keepdims=True) + epsilon)
    return (scaled * inv_length, normed, inverse, inv_length)


def embed_back(direction, unit_rows, normed, inverse, inv_length, gain):
    tangent = (
        direction - unit_rows * jnp.sum(unit_rows * direction, axis=-1, keepdims=True)
    ) * inv_length
    gain_part = jnp.sum(tangent * normed, axis=0)
    scaled = tangent * gain
    gradient = (
        scaled
        - jnp.mean(scaled, axis=-1, keepdims=True)
        - normed * jnp.mean(scaled * normed, axis=-1, keepdims=True)
    ) * inverse
    return (gradient, gain_part)


def pair_weights(scores, labels_pos, kept, score_sharpness_factor, score_shift_amount, grad_factor):
    score_similarity_table = score_sharpness_factor * scores + score_shift_amount
    labels = jnp.where(labels_pos, 1.0, -1.0).astype(jnp.float32)
    margin = -labels * score_similarity_table
    loss_sum = jnp.sum(jnp.where(kept, jax.nn.softplus(margin), 0.0))
    weights = jnp.where(kept, -labels * jax.nn.sigmoid(margin), 0.0) * grad_factor
    return loss_sum, weights.astype(jnp.bfloat16)


def grad_kernel(
    scalars_ref, counts_ref, pooled_ref, gain_ref, own_ref, gathered_ref, partner_ref, grads_ref, sums_ref
):
    blocks = counts_ref.shape[0] - 2
    own_block = counts_ref[blocks]
    group_index = counts_ref[blocks + 1]
    block_rows = own_ref.shape[1]
    group_rows = gathered_ref.shape[1]
    width = own_ref.shape[2]
    own_start = own_block * block_rows
    total = counts_ref[0]
    for block in range(1, blocks):
        total = total + counts_ref[block]
    real_count = jnp.full((1, 1), total, jnp.int32).astype(jnp.float32)
    score_sharpness_factor = jnp.exp(jnp.full((1, 1), scalars_ref[0], jnp.float32))
    score_shift_amount = jnp.full((1, 1), scalars_ref[1], jnp.float32)
    grad_factor = jnp.full((1, 1), scalars_ref[2], jnp.float32) / real_count

    lane = lax.broadcasted_iota(jnp.int32, (1, group_rows), 1)
    lane_limit = jnp.zeros((1, group_rows), jnp.int32)
    for block in range(blocks):
        lane_limit = jnp.where(lane // block_rows == block, counts_ref[block], lane_limit)
    real_group = (lane % block_rows) < lane_limit
    sub = lax.broadcasted_iota(jnp.int32, (block_rows, 1), 0)
    real_own = sub < counts_ref[own_block]
    kept = real_own & real_group

    partner_row = partner_ref[...]
    columns = lax.broadcasted_iota(jnp.int32, (block_rows, group_rows), 1)
    own_index = own_start + lax.broadcasted_iota(jnp.int32, (block_rows, group_rows), 0)
    own_partner = jnp.sum(
        jnp.where(columns == own_index, partner_row.astype(jnp.float32), 0.0), axis=1, keepdims=True
    ).astype(jnp.int32)
    positives = (
        own_partner == columns,
        partner_row == own_index,
    )

    loss_rows = []
    for tower in range(2):
        values = pooled_ref[tower].astype(jnp.float32)
        gain = gain_ref[tower : tower + 1, :]
        centred = values - jnp.mean(values, axis=-1, keepdims=True)
        inverse = lax.rsqrt(jnp.mean(centred * centred, axis=-1, keepdims=True) + epsilon)
        normed = centred * inverse
        scaled = normed * gain
        inv_length = lax.rsqrt(jnp.sum(scaled * scaled, axis=-1, keepdims=True) + epsilon)
        unit_rows = scaled * inv_length

        other = gathered_ref[1 - tower]
        scores = lax.dot_general(
            own_ref[tower], other, (((1,), (1,)), ((), ())), preferred_element_type=jnp.float32
        )
        score_similarity_table = score_sharpness_factor * scores + score_shift_amount
        labels = jnp.where(positives[tower], 1.0, -1.0)
        margin = -labels * score_similarity_table
        if tower == 0:
            softplus = jnp.maximum(margin, 0.0) + jnp.log1p(jnp.exp(-jnp.abs(margin)))
            loss_rows.append(jnp.sum(jnp.where(kept, softplus, 0.0), axis=(0, 1), keepdims=True))
        weights = jnp.where(kept, -labels * jax.nn.sigmoid(margin), 0.0) * grad_factor
        direction = score_sharpness_factor * jnp.dot(
            weights.astype(jnp.bfloat16), other, preferred_element_type=jnp.float32
        )
        tangent = (
            direction - unit_rows * jnp.sum(unit_rows * direction, axis=-1, keepdims=True)
        ) * inv_length
        sums_ref[tower : tower + 1, :] = jnp.sum(tangent * normed, axis=0, keepdims=True)
        scaled_back = tangent * gain
        gradient = (
            scaled_back
            - jnp.mean(scaled_back, axis=-1, keepdims=True)
            - normed * jnp.mean(scaled_back * normed, axis=-1, keepdims=True)
        ) * inverse
        grads_ref[tower] = gradient.astype(grads_ref.dtype)
    group_lane = lax.broadcasted_iota(jnp.int32, (1, width), 1)
    sums_ref[2:3, :] = jnp.where(group_lane == group_index, loss_rows[0] / real_count, 0.0)


def shards(
    picture_averaged_features,
    caption_averaged_features,
    picture_rescale_factor,
    caption_rescale_factor,
    exponent_of_sharpness,
    score_shift_term,
    objective_multiplier,
    matching_caption_index,
    genuine_entry_counts,
):
    block_rows = picture_averaged_features.shape[1]
    width = picture_averaged_features.shape[2]
    members = lax.axis_size("blk")
    own_block = lax.axis_index("blk")
    group_index = lax.axis_index("rep")
    pooled = jnp.concatenate([picture_averaged_features, caption_averaged_features])
    gains = jnp.stack([picture_rescale_factor, caption_rescale_factor])
    both = embed_both(pooled, gains)

    pieces, masks, offsets, natural = gather_blocks(both, "blk")
    if natural:
        gathered = pieces.reshape(2, members * block_rows, width)
    else:
        gathered = jnp.zeros((2, members, block_rows, width), both.dtype)
        for piece, mask, offset in zip(pieces, masks, offsets):
            gathered = lax.dynamic_update_slice(
                gathered, piece[:, None], (0, own_block ^ mask, offset, 0)
            )
        gathered = gathered.reshape(2, members * block_rows, width)

    scalars = jnp.concatenate([exponent_of_sharpness, score_shift_term, objective_multiplier])
    counts = jnp.concatenate(
        [genuine_entry_counts[0], jnp.stack([own_block, group_index]).astype(jnp.int32)]
    )
    smem = pltpu.MemorySpace.SMEM
    vmem = pltpu.MemorySpace.VMEM
    grads, sums = pl.pallas_call(
        grad_kernel,
        out_shape=(
            jax.ShapeDtypeStruct((2, block_rows, width), jnp.bfloat16),
            jax.ShapeDtypeStruct((3, width), jnp.float32),
        ),
        in_specs=[pl.BlockSpec(memory_space=smem)] * 2 + [pl.BlockSpec(memory_space=vmem)] * 5,
        out_specs=(pl.BlockSpec(memory_space=vmem), pl.BlockSpec(memory_space=vmem)),
    )(scalars, counts, pooled, gains, both, gathered, matching_caption_index)

    total = all_sum(sums, ("blk", "rep"))
    gain_grads = total[:2]
    group_loss = lax.dynamic_slice_in_dim(total[2], group_index, 1)
    return (grads[0:1], grads[1:2], gain_grads, group_loss)


def solution(mesh):
    placed = (
        P("rep", "blk", None),
        P("rep", "blk", None),
        P(),
        P(),
        P(),
        P(),
        P(),
        P("rep", None),
        P("rep", None),
    )
    return jax.shard_map(
        shards,
        mesh=mesh,
        in_specs=placed,
        out_specs=(P("rep", "blk", None), P("rep", "blk", None), P(), P("rep")),
        check_vma=False,
    )
```

```python
import functools

import jax
import jax.numpy as jnp
from jax import lax
from jax.sharding import PartitionSpec as P
from jax.experimental import pallas as pl
from jax.experimental.pallas import tpu as pltpu

epsilon = 1e-06


def xor_swap(value, axis, bit):
    count = lax.axis_size(axis)
    return lax.ppermute(value, axis, [(source, source ^ bit) for source in range(count)])


def power_of_two(count):
    return count > 1 and count & (count - 1) == 0


def gather_blocks(first, second, axis):
    count = lax.axis_size(axis)
    half = first.shape[1]
    if not power_of_two(count) or count < 4:
        own = lax.axis_index(axis)
        pieces = [lax.all_gather(part, axis, axis=1, tiled=False) for part in (first, second)]
        pieces = [
            lax.dynamic_index_in_dim(part, own ^ mask, axis=1, keepdims=False)
            for part in pieces
            for mask in range(count)
        ]
        return pieces, list(range(count)) * 2, [0] * count + [half] * count
    chip_bits = [1 << b for b in range(1, count.bit_length() - 1)]
    orders = (chip_bits, chip_bits[::-1])
    routed = ([first], [second])
    routed_masks = ([0], [0])
    fresh = ([0], [0])
    shared = ([], [])
    shared_masks = ([], [])
    for step in range(len(chip_bits) + 1):
        last = step == len(chip_bits)
        sent = [None, None]
        if not last:
            sent = [xor_swap(tuple(routed[h]), axis, orders[h][step]) for h in range(2)]
        across = [xor_swap(tuple(routed[h][i] for i in fresh[h]), axis, 1) for h in range(2)]
        for h in range(2):
            shared[h].extend(across[h])
            shared_masks[h].extend([routed_masks[h][i] ^ 1 for i in fresh[h]])
            if not last:
                bit = orders[h][step]
                fresh[h][:] = list(range(len(routed[h]), 2 * len(routed[h])))
                routed[h].extend(sent[h])
                routed_masks[h].extend([mask ^ bit for mask in routed_masks[h]])
    gathered = routed[0] + shared[0] + routed[1] + shared[1]
    masks = routed_masks[0] + shared_masks[0] + routed_masks[1] + shared_masks[1]
    offsets = [0] * count + [half] * count
    return gathered, masks, offsets


def all_sum(value, axes):
    for axis in axes:
        count = lax.axis_size(axis)
        if not power_of_two(count):
            value = lax.psum(value, axis)
            continue
        bit = 1
        while bit < count:
            value = value + xor_swap(value, axis, bit)
            bit *= 2
    return value


def embed_kernel(picture_ref, caption_ref, picture_gain_ref, caption_gain_ref, first_ref, second_ref):
    half = first_ref.shape[1]
    towers = ((picture_ref, picture_gain_ref), (caption_ref, caption_gain_ref))
    for tower, (pooled_ref, gain_ref) in enumerate(towers):
        values = pooled_ref[0].astype(jnp.float32)
        centred = values - jnp.mean(values, axis=-1, keepdims=True)
        inverse = lax.rsqrt(jnp.mean(centred * centred, axis=-1, keepdims=True) + epsilon)
        scaled = centred * inverse * gain_ref[...][None, :]
        inv_length = lax.rsqrt(jnp.sum(scaled * scaled, axis=-1, keepdims=True) + epsilon)
        unit_rows = (scaled * inv_length).astype(first_ref.dtype)
        first_ref[tower] = unit_rows[:half]
        second_ref[tower] = unit_rows[half:]


def embed_both(picture, caption, picture_gain, caption_gain):
    rows, width = picture.shape[1:]
    vmem = pltpu.MemorySpace.VMEM
    half = jax.ShapeDtypeStruct((2, rows // 2, width), jnp.bfloat16)
    return pl.pallas_call(
        embed_kernel,
        out_shape=(half, half),
        in_specs=[pl.BlockSpec(memory_space=vmem)] * 4,
        out_specs=(pl.BlockSpec(memory_space=vmem), pl.BlockSpec(memory_space=vmem)),
    )(picture, caption, picture_gain, caption_gain)


def grad_kernel(masks, offsets, *refs):
    (sharpness_ref, shift_ref, multiplier_ref, counts_ref, picture_ref, caption_ref, picture_gain_ref,
     caption_gain_ref, gathered_ref, partner_ref, image_grad_ref, text_grad_ref, sums_ref) = refs
    blocks = counts_ref.shape[1]
    own_block = lax.axis_index("blk")
    group_index = lax.axis_index("rep")
    block_rows = picture_ref.shape[1]
    width = picture_ref.shape[2]
    piece = gathered_ref.shape[1] // len(masks)
    group_rows = gathered_ref.shape[1]
    own_start = own_block * block_rows
    total = counts_ref[0, 0]
    for block in range(1, blocks):
        total = total + counts_ref[0, block]
    real_count = jnp.full((1, 1), total, jnp.int32).astype(jnp.float32)
    score_sharpness_factor = jnp.exp(jnp.full((1, 1), sharpness_ref[0], jnp.float32))
    score_shift_amount = jnp.full((1, 1), shift_ref[0], jnp.float32)
    grad_factor = jnp.full((1, 1), multiplier_ref[0], jnp.float32) / real_count

    lane = lax.broadcasted_iota(jnp.int32, (1, group_rows), 1)
    held_row = jnp.zeros((1, group_rows), jnp.int32)
    limit = jnp.zeros((1, group_rows), jnp.int32)
    for position, (mask, offset) in enumerate(zip(masks, offsets)):
        block = own_block ^ mask
        here = lane // piece == position
        held_row = jnp.where(here, block * block_rows + offset + lane % piece, held_row)
        limit = jnp.where(here, counts_ref[0, block], limit)
    real_group = (held_row % block_rows) < limit
    sub = lax.broadcasted_iota(jnp.int32, (block_rows, 1), 0)
    real_own = sub < counts_ref[0, own_block]
    kept = real_own & real_group

    natural = lax.broadcasted_iota(jnp.int32, (block_rows, group_rows), 1)
    own_index = own_start + lax.broadcasted_iota(jnp.int32, (block_rows, group_rows), 0)
    partner_row = partner_ref[...]
    own_partner = jnp.sum(
        jnp.where(natural == own_index, partner_row.astype(jnp.float32), 0.0), axis=1, keepdims=True
    ).astype(jnp.int32)
    matched_image = jnp.sum(
        jnp.where(partner_row == own_index, natural.astype(jnp.float32), 0.0), axis=1, keepdims=True
    ).astype(jnp.int32)
    positives = (own_partner == held_row, matched_image == held_row)

    start_b = len(masks) // 2 * piece
    loss_rows = []
    towers = ((picture_ref, picture_gain_ref, image_grad_ref), (caption_ref, caption_gain_ref, text_grad_ref))
    for tower, (pooled_ref, gain_ref, grad_ref) in enumerate(towers):
        values = pooled_ref[0].astype(jnp.float32)
        gain = gain_ref[...][None, :]
        centred = values - jnp.mean(values, axis=-1, keepdims=True)
        inverse = lax.rsqrt(jnp.mean(centred * centred, axis=-1, keepdims=True) + epsilon)
        normed = centred * inverse
        scaled = normed * gain
        inv_length = lax.rsqrt(jnp.sum(scaled * scaled, axis=-1, keepdims=True) + epsilon)
        unit_rows = scaled * inv_length

        own = jnp.concatenate(
            [gathered_ref[tower, 0:piece, :], gathered_ref[tower, start_b : start_b + piece, :]], axis=0
        )
        other = gathered_ref[1 - tower]
        scores = lax.dot_general(own, other, (((1,), (1,)), ((), ())), preferred_element_type=jnp.float32)
        score_similarity_table = score_sharpness_factor * scores + score_shift_amount
        labels = jnp.where(positives[tower], 1.0, -1.0)
        margin = -labels * score_similarity_table
        if tower == 0:
            softplus = jnp.maximum(margin, 0.0) + jnp.log1p(jnp.exp(-jnp.abs(margin)))
            loss_rows.append(jnp.sum(jnp.where(kept, softplus, 0.0), axis=(0, 1), keepdims=True))
        weights = jnp.where(kept, -labels * jax.nn.sigmoid(margin), 0.0) * grad_factor
        direction = score_sharpness_factor * jnp.dot(
            weights.astype(jnp.bfloat16), other, preferred_element_type=jnp.float32
        )
        tangent = (
            direction - unit_rows * jnp.sum(unit_rows * direction, axis=-1, keepdims=True)
        ) * inv_length
        sums_ref[tower : tower + 1, :] = jnp.sum(tangent * normed, axis=0, keepdims=True)
        scaled_back = tangent * gain
        gradient = (
            scaled_back
            - jnp.mean(scaled_back, axis=-1, keepdims=True)
            - normed * jnp.mean(scaled_back * normed, axis=-1, keepdims=True)
        ) * inverse
        grad_ref[0] = gradient.astype(grad_ref.dtype)
    group_lane = lax.broadcasted_iota(jnp.int32, (1, width), 1)
    sums_ref[2:3, :] = jnp.where(group_lane == group_index, loss_rows[0] / real_count, 0.0)


def shards(
    picture_averaged_features,
    caption_averaged_features,
    picture_rescale_factor,
    caption_rescale_factor,
    exponent_of_sharpness,
    score_shift_term,
    objective_multiplier,
    matching_caption_index,
    genuine_entry_counts,
):
    width = picture_averaged_features.shape[2]
    first, second = embed_both(
        picture_averaged_features, caption_averaged_features, picture_rescale_factor, caption_rescale_factor
    )
    pieces, masks, offsets = gather_blocks(first, second, "blk")
    gathered = jnp.concatenate(pieces, axis=1)

    smem = pltpu.MemorySpace.SMEM
    vmem = pltpu.MemorySpace.VMEM
    grad_shape = jax.ShapeDtypeStruct(picture_averaged_features.shape, jnp.bfloat16)
    image_grad, text_grad, sums = pl.pallas_call(
        functools.partial(grad_kernel, tuple(masks), tuple(offsets)),
        out_shape=(grad_shape, grad_shape, jax.ShapeDtypeStruct((3, width), jnp.float32)),
        in_specs=[pl.BlockSpec(memory_space=smem)] * 4 + [pl.BlockSpec(memory_space=vmem)] * 6,
        out_specs=(pl.BlockSpec(memory_space=vmem),) * 3,
    )(
        exponent_of_sharpness,
        score_shift_term,
        objective_multiplier,
        genuine_entry_counts,
        picture_averaged_features,
        caption_averaged_features,
        picture_rescale_factor,
        caption_rescale_factor,
        gathered,
        matching_caption_index,
    )

    total = all_sum(sums, ("blk", "rep"))
    gain_grads = total[:2]
    group_loss = lax.dynamic_slice_in_dim(total[2], lax.axis_index("rep"), 1)
    return (image_grad, text_grad, gain_grads, group_loss)


def solution(mesh):
    placed = (
        P("rep", "blk", None),
        P("rep", "blk", None),
        P(),
        P(),
        P(),
        P(),
        P(),
        P("rep", None),
        P("rep", None),
    )
    return jax.shard_map(
        shards,
        mesh=mesh,
        in_specs=placed,
        out_specs=(P("rep", "blk", None), P("rep", "blk", None), P(), P("rep")),
        check_vma=False,
    )
```

```python
import functools

import jax
import jax.numpy as jnp
from jax import lax
from jax.sharding import PartitionSpec as P
from jax.experimental import pallas as pl
from jax.experimental.pallas import tpu as pltpu

epsilon = 1e-06


def xor_swap(value, axis, bit):
    count = lax.axis_size(axis)
    return lax.ppermute(value, axis, [(source, source ^ bit) for source in range(count)])


def power_of_two(count):
    return count > 1 and count & (count - 1) == 0


def gather_blocks(first, second, axis):
    count = lax.axis_size(axis)
    half = first.shape[1]
    if not power_of_two(count) or count < 4:
        own = lax.axis_index(axis)
        pieces = [lax.all_gather(part, axis, axis=1, tiled=False) for part in (first, second)]
        pieces = [
            lax.dynamic_index_in_dim(part, own ^ mask, axis=1, keepdims=False)
            for part in pieces
            for mask in range(count)
        ]
        return pieces, list(range(count)) * 2, [0] * count + [half] * count
    chip_bits = [1 << b for b in range(1, count.bit_length() - 1)]
    orders = (chip_bits, chip_bits[::-1])
    routed = ([first], [second])
    routed_masks = ([0], [0])
    fresh = ([0], [0])
    shared = ([], [])
    shared_masks = ([], [])
    for step in range(len(chip_bits) + 1):
        last = step == len(chip_bits)
        sent = [None, None]
        if not last:
            sent = [xor_swap(tuple(routed[h]), axis, orders[h][step]) for h in range(2)]
        across = [xor_swap(tuple(routed[h][i] for i in fresh[h]), axis, 1) for h in range(2)]
        for h in range(2):
            shared[h].extend(across[h])
            shared_masks[h].extend([routed_masks[h][i] ^ 1 for i in fresh[h]])
            if not last:
                bit = orders[h][step]
                fresh[h][:] = list(range(len(routed[h]), 2 * len(routed[h])))
                routed[h].extend(sent[h])
                routed_masks[h].extend([mask ^ bit for mask in routed_masks[h]])
    gathered = routed[0] + shared[0] + routed[1] + shared[1]
    masks = routed_masks[0] + shared_masks[0] + routed_masks[1] + shared_masks[1]
    offsets = [0] * count + [half] * count
    return gathered, masks, offsets


def all_sum(value, axis, keep=None):
    keep = value.shape[0] if keep is None else keep
    count = lax.axis_size(axis)
    if not power_of_two(count):
        return lax.psum(value, axis)[:keep]
    bit = 1
    while bit < count:
        if bit * 2 < count:
            value = value + xor_swap(value, axis, bit)
        else:
            value = value[:keep] + xor_swap(value, axis, bit)[:keep]
        bit *= 2
    return value


def embed_kernel(picture_ref, caption_ref, picture_gain_ref, caption_gain_ref, first_ref, second_ref):
    half = first_ref.shape[1]
    towers = ((picture_ref, picture_gain_ref), (caption_ref, caption_gain_ref))
    for tower, (pooled_ref, gain_ref) in enumerate(towers):
        values = pooled_ref[0].astype(jnp.float32)
        centred = values - jnp.mean(values, axis=-1, keepdims=True)
        inverse = lax.rsqrt(jnp.mean(centred * centred, axis=-1, keepdims=True) + epsilon)
        scaled = centred * inverse * gain_ref[...][None, :]
        inv_length = lax.rsqrt(jnp.sum(scaled * scaled, axis=-1, keepdims=True) + epsilon)
        unit_rows = (scaled * inv_length).astype(first_ref.dtype)
        first_ref[tower] = unit_rows[:half]
        second_ref[tower] = unit_rows[half:]


def embed_both(picture, caption, picture_gain, caption_gain):
    rows, width = picture.shape[1:]
    vmem = pltpu.MemorySpace.VMEM
    half = jax.ShapeDtypeStruct((2, rows // 2, width), jnp.bfloat16)
    return pl.pallas_call(
        embed_kernel,
        out_shape=(half, half),
        in_specs=[pl.BlockSpec(memory_space=vmem)] * 4,
        out_specs=(pl.BlockSpec(memory_space=vmem), pl.BlockSpec(memory_space=vmem)),
    )(picture, caption, picture_gain, caption_gain)


def grad_kernel(masks, offsets, *refs):
    (sharpness_ref, shift_ref, multiplier_ref, counts_ref, picture_ref, caption_ref, picture_gain_ref,
     caption_gain_ref, partner_ref) = refs[:9]
    pieces = refs[9 : 9 + len(masks)]
    image_grad_ref, text_grad_ref, sums_ref, gathered_ref, copy_sems = refs[9 + len(masks) :]
    piece = pieces[0].shape[1]
    arrivals = [
        pltpu.make_async_copy(
            source, gathered_ref.at[:, position * piece : (position + 1) * piece, :], copy_sems.at[position]
        )
        for position, source in enumerate(pieces)
    ]
    for arrival in arrivals:
        arrival.start()
    blocks = counts_ref.shape[1]
    own_block = lax.axis_index("blk")
    block_rows = picture_ref.shape[1]
    width = picture_ref.shape[2]
    group_rows = gathered_ref.shape[1]
    own_start = own_block * block_rows
    total = counts_ref[0, 0]
    for block in range(1, blocks):
        total = total + counts_ref[0, block]
    real_count = jnp.full((1, 1), total, jnp.int32).astype(jnp.float32)
    score_sharpness_factor = jnp.exp(jnp.full((1, 1), sharpness_ref[0], jnp.float32))
    score_shift_amount = jnp.full((1, 1), shift_ref[0], jnp.float32)
    grad_factor = jnp.full((1, 1), multiplier_ref[0], jnp.float32) / real_count

    lane = lax.broadcasted_iota(jnp.int32, (1, group_rows), 1)
    held_row = jnp.zeros((1, group_rows), jnp.int32)
    limit = jnp.zeros((1, group_rows), jnp.int32)
    for position, (mask, offset) in enumerate(zip(masks, offsets)):
        block = own_block ^ mask
        here = lane // piece == position
        held_row = jnp.where(here, block * block_rows + offset + lane % piece, held_row)
        limit = jnp.where(here, counts_ref[0, block], limit)
    real_group = (held_row % block_rows) < limit
    sub = lax.broadcasted_iota(jnp.int32, (block_rows, 1), 0)
    real_own = sub < counts_ref[0, own_block]
    kept = real_own & real_group

    natural = lax.broadcasted_iota(jnp.int32, (block_rows, group_rows), 1)
    own_index = own_start + lax.broadcasted_iota(jnp.int32, (block_rows, group_rows), 0)
    partner_row = partner_ref[...]
    own_partner = jnp.sum(
        jnp.where(natural == own_index, partner_row.astype(jnp.float32), 0.0), axis=1, keepdims=True
    ).astype(jnp.int32)
    matched_image = jnp.sum(
        jnp.where(partner_row == own_index, natural.astype(jnp.float32), 0.0), axis=1, keepdims=True
    ).astype(jnp.int32)
    positives = (own_partner == held_row, matched_image == held_row)

    start_b = len(masks) // 2 * piece
    for arrival in arrivals:
        arrival.wait()
    loss_rows = []
    towers = ((picture_ref, picture_gain_ref, image_grad_ref), (caption_ref, caption_gain_ref, text_grad_ref))
    for tower, (pooled_ref, gain_ref, grad_ref) in enumerate(towers):
        values = pooled_ref[0].astype(jnp.float32)
        gain = gain_ref[...][None, :]
        centred = values - jnp.mean(values, axis=-1, keepdims=True)
        inverse = lax.rsqrt(jnp.mean(centred * centred, axis=-1, keepdims=True) + epsilon)
        normed = centred * inverse
        scaled = normed * gain
        inv_length = lax.rsqrt(jnp.sum(scaled * scaled, axis=-1, keepdims=True) + epsilon)
        unit_rows = scaled * inv_length

        own = jnp.concatenate(
            [gathered_ref[tower, 0:piece, :], gathered_ref[tower, start_b : start_b + piece, :]], axis=0
        )
        other = gathered_ref[1 - tower]
        scores = lax.dot_general(own, other, (((1,), (1,)), ((), ())), preferred_element_type=jnp.float32)
        score_similarity_table = score_sharpness_factor * scores + score_shift_amount
        labels = jnp.where(positives[tower], 1.0, -1.0)
        margin = -labels * score_similarity_table
        if tower == 0:
            softplus = jnp.maximum(margin, 0.0) + jnp.log1p(jnp.exp(-jnp.abs(margin)))
            loss_rows.append(jnp.sum(jnp.where(kept, softplus, 0.0), axis=(0, 1), keepdims=True))
        weights = jnp.where(kept, -labels * jax.nn.sigmoid(margin), 0.0) * grad_factor
        direction = score_sharpness_factor * jnp.dot(
            weights.astype(jnp.bfloat16), other, preferred_element_type=jnp.float32
        )
        tangent = (
            direction - unit_rows * jnp.sum(unit_rows * direction, axis=-1, keepdims=True)
        ) * inv_length
        sums_ref[tower : tower + 1, :] = jnp.sum(tangent * normed, axis=0, keepdims=True)
        scaled_back = tangent * gain
        gradient = (
            scaled_back
            - jnp.mean(scaled_back, axis=-1, keepdims=True)
            - normed * jnp.mean(scaled_back * normed, axis=-1, keepdims=True)
        ) * inverse
        grad_ref[0] = gradient.astype(grad_ref.dtype)
    first_lane = lax.broadcasted_iota(jnp.int32, (1, width), 1) == 0
    sums_ref[2:3, :] = jnp.where(first_lane, loss_rows[0] / real_count, 0.0)


def shards(
    picture_averaged_features,
    caption_averaged_features,
    picture_rescale_factor,
    caption_rescale_factor,
    exponent_of_sharpness,
    score_shift_term,
    objective_multiplier,
    matching_caption_index,
    genuine_entry_counts,
):
    width = picture_averaged_features.shape[2]
    first, second = embed_both(
        picture_averaged_features, caption_averaged_features, picture_rescale_factor, caption_rescale_factor
    )
    pieces, masks, offsets = gather_blocks(first, second, "blk")

    smem = pltpu.MemorySpace.SMEM
    vmem = pltpu.MemorySpace.VMEM
    grad_shape = jax.ShapeDtypeStruct(picture_averaged_features.shape, jnp.bfloat16)
    image_grad, text_grad, sums = pl.pallas_call(
        functools.partial(grad_kernel, tuple(masks), tuple(offsets)),
        out_shape=(grad_shape, grad_shape, jax.ShapeDtypeStruct((3, width), jnp.float32)),
        in_specs=[pl.BlockSpec(memory_space=smem)] * 4
        + [pl.BlockSpec(memory_space=vmem)] * 5
        + [pl.BlockSpec(memory_space=pl.ANY)] * len(pieces),
        out_specs=(pl.BlockSpec(memory_space=vmem),) * 3,
        scratch_shapes=[
            pltpu.VMEM((2, len(pieces) * pieces[0].shape[1], width), pieces[0].dtype),
            pltpu.SemaphoreType.DMA((len(pieces),)),
        ],
    )(
        exponent_of_sharpness,
        score_shift_term,
        objective_multiplier,
        genuine_entry_counts,
        picture_averaged_features,
        caption_averaged_features,
        picture_rescale_factor,
        caption_rescale_factor,
        matching_caption_index,
        *pieces,
    )

    group_sums = all_sum(sums, "blk")
    group_loss = group_sums[2, 0:1]
    gain_grads = all_sum(group_sums, "rep", keep=2)
    return (image_grad, text_grad, gain_grads, group_loss)


def solution(mesh):
    placed = (
        P("rep", "blk", None),
        P("rep", "blk", None),
        P(),
        P(),
        P(),
        P(),
        P(),
        P("rep", None),
        P("rep", None),
    )
    return jax.shard_map(
        shards,
        mesh=mesh,
        in_specs=placed,
        out_specs=(P("rep", "blk", None), P("rep", "blk", None), P(), P("rep")),
        check_vma=False,
    )
```

```python
import functools

import jax
import jax.numpy as jnp
from jax import lax
from jax.sharding import PartitionSpec as P
from jax.experimental import pallas as pl
from jax.experimental.pallas import tpu as pltpu

epsilon = 1e-06


def xor_swap(value, axis, bit):
    count = lax.axis_size(axis)
    return lax.ppermute(value, axis, [(source, source ^ bit) for source in range(count)])


def power_of_two(count):
    return count > 1 and count & (count - 1) == 0


def gather_blocks(first, second, axis):
    count = lax.axis_size(axis)
    half = first.shape[1]
    if not power_of_two(count) or count < 4:
        own = lax.axis_index(axis)
        pieces = [lax.all_gather(part, axis, axis=1, tiled=False) for part in (first, second)]
        pieces = [
            lax.dynamic_index_in_dim(part, own ^ mask, axis=1, keepdims=False)
            for part in pieces
            for mask in range(count)
        ]
        return pieces, list(range(count)) * 2, [0] * count + [half] * count
    chip_bits = [1 << b for b in range(1, count.bit_length() - 1)]
    orders = (chip_bits, chip_bits[::-1])
    routed = ([first], [second])
    routed_masks = ([0], [0])
    fresh = ([0], [0])
    shared = ([], [])
    shared_masks = ([], [])
    for step in range(len(chip_bits) + 1):
        last = step == len(chip_bits)
        sent = [None, None]
        if not last:
            sent = [xor_swap(tuple(routed[h]), axis, orders[h][step]) for h in range(2)]
        across = [xor_swap(tuple(routed[h][i] for i in fresh[h]), axis, 1) for h in range(2)]
        for h in range(2):
            shared[h].extend(across[h])
            shared_masks[h].extend([routed_masks[h][i] ^ 1 for i in fresh[h]])
            if not last:
                bit = orders[h][step]
                fresh[h][:] = list(range(len(routed[h]), 2 * len(routed[h])))
                routed[h].extend(sent[h])
                routed_masks[h].extend([mask ^ bit for mask in routed_masks[h]])
    gathered = routed[0] + shared[0] + routed[1] + shared[1]
    masks = routed_masks[0] + shared_masks[0] + routed_masks[1] + shared_masks[1]
    offsets = [0] * count + [half] * count
    return gathered, masks, offsets


def all_sum(value, axis, keep=None):
    keep = value.shape[0] if keep is None else keep
    count = lax.axis_size(axis)
    if not power_of_two(count):
        return lax.psum(value, axis)[:keep]
    bit = 1
    while bit < count:
        if bit * 2 < count:
            value = value + xor_swap(value, axis, bit)
        else:
            value = value[:keep] + xor_swap(value, axis, bit)[:keep]
        bit *= 2
    return value


def embed_kernel(picture_ref, caption_ref, picture_gain_ref, caption_gain_ref, first_ref, second_ref):
    half = first_ref.shape[1]
    towers = ((picture_ref, picture_gain_ref), (caption_ref, caption_gain_ref))
    for tower, (pooled_ref, gain_ref) in enumerate(towers):
        values = pooled_ref[0].astype(jnp.float32)
        centred = values - jnp.mean(values, axis=-1, keepdims=True)
        inverse = lax.rsqrt(jnp.mean(centred * centred, axis=-1, keepdims=True) + epsilon)
        scaled = centred * inverse * gain_ref[...][None, :]
        inv_length = lax.rsqrt(jnp.sum(scaled * scaled, axis=-1, keepdims=True) + epsilon)
        unit_rows = (scaled * inv_length).astype(first_ref.dtype)
        first_ref[tower] = unit_rows[:half]
        second_ref[tower] = unit_rows[half:]


def embed_both(picture, caption, picture_gain, caption_gain):
    rows, width = picture.shape[1:]
    vmem = pltpu.MemorySpace.VMEM
    half = jax.ShapeDtypeStruct((2, rows // 2, width), jnp.bfloat16)
    return pl.pallas_call(
        embed_kernel,
        out_shape=(half, half),
        in_specs=[pl.BlockSpec(memory_space=vmem)] * 4,
        out_specs=(pl.BlockSpec(memory_space=vmem), pl.BlockSpec(memory_space=vmem)),
    )(picture, caption, picture_gain, caption_gain)


def grad_kernel(masks, offsets, *refs):
    (sharpness_ref, shift_ref, multiplier_ref, counts_ref, picture_ref, caption_ref, picture_gain_ref,
     caption_gain_ref, partner_ref) = refs[:9]
    pieces = refs[9 : 9 + len(masks)]
    image_grad_ref, text_grad_ref, sums_ref, gathered_ref, copy_sems = refs[9 + len(masks) :]
    piece = pieces[0].shape[1]
    arrivals = [
        pltpu.make_async_copy(
            source, gathered_ref.at[:, position * piece : (position + 1) * piece, :], copy_sems.at[position]
        )
        for position, source in enumerate(pieces)
    ]
    for arrival in arrivals:
        arrival.start()
    blocks = counts_ref.shape[1]
    own_block = lax.axis_index("blk")
    block_rows = picture_ref.shape[1]
    width = picture_ref.shape[2]
    group_rows = gathered_ref.shape[1]
    own_start = own_block * block_rows
    total = counts_ref[0, 0]
    for block in range(1, blocks):
        total = total + counts_ref[0, block]
    real_count = jnp.full((1, 1), total, jnp.int32).astype(jnp.float32)
    score_sharpness_factor = jnp.exp(jnp.full((1, 1), sharpness_ref[0], jnp.float32))
    score_shift_amount = jnp.full((1, 1), shift_ref[0], jnp.float32)
    grad_factor = jnp.full((1, 1), multiplier_ref[0], jnp.float32) / real_count

    lane = lax.broadcasted_iota(jnp.int32, (1, group_rows), 1)
    held_row = jnp.zeros((1, group_rows), jnp.int32)
    limit = jnp.zeros((1, group_rows), jnp.int32)
    for position, (mask, offset) in enumerate(zip(masks, offsets)):
        block = own_block ^ mask
        here = lane // piece == position
        held_row = jnp.where(here, block * block_rows + offset + lane % piece, held_row)
        limit = jnp.where(here, counts_ref[0, block], limit)
    real_group = (held_row % block_rows) < limit
    sub = lax.broadcasted_iota(jnp.int32, (block_rows, 1), 0)
    real_own = sub < counts_ref[0, own_block]
    kept = real_own & real_group

    natural = lax.broadcasted_iota(jnp.int32, (block_rows, group_rows), 1)
    own_index = own_start + lax.broadcasted_iota(jnp.int32, (block_rows, group_rows), 0)
    partner_row = partner_ref[...]
    own_partner = jnp.sum(
        jnp.where(natural == own_index, partner_row.astype(jnp.float32), 0.0), axis=1, keepdims=True
    ).astype(jnp.int32)
    matched_image = jnp.sum(
        jnp.where(partner_row == own_index, natural.astype(jnp.float32), 0.0), axis=1, keepdims=True
    ).astype(jnp.int32)
    positives = (own_partner == held_row, matched_image == held_row)

    start_b = len(masks) // 2 * piece
    for arrival in arrivals:
        arrival.wait()
    loss_rows = []
    towers = ((picture_ref, picture_gain_ref, image_grad_ref), (caption_ref, caption_gain_ref, text_grad_ref))
    for tower, (pooled_ref, gain_ref, grad_ref) in enumerate(towers):
        values = pooled_ref[0].astype(jnp.float32)
        gain = gain_ref[...][None, :]
        centred = values - jnp.mean(values, axis=-1, keepdims=True)
        inverse = lax.rsqrt(jnp.mean(centred * centred, axis=-1, keepdims=True) + epsilon)
        normed = centred * inverse
        scaled = normed * gain
        inv_length = lax.rsqrt(jnp.sum(scaled * scaled, axis=-1, keepdims=True) + epsilon)
        unit_rows = scaled * inv_length

        own = jnp.concatenate(
            [gathered_ref[tower, 0:piece, :], gathered_ref[tower, start_b : start_b + piece, :]], axis=0
        )
        other = gathered_ref[1 - tower]
        scores = lax.dot_general(own, other, (((1,), (1,)), ((), ())), preferred_element_type=jnp.float32)
        score_similarity_table = score_sharpness_factor * scores + score_shift_amount
        labels = jnp.where(positives[tower], 1.0, -1.0)
        margin = -labels * score_similarity_table
        if tower == 0:
            softplus = jnp.maximum(margin, 0.0) + jnp.log1p(jnp.exp(-jnp.abs(margin)))
            loss_rows.append(jnp.sum(jnp.where(kept, softplus, 0.0), axis=(0, 1), keepdims=True))
        weights = jnp.where(kept, -labels * jax.nn.sigmoid(margin), 0.0) * grad_factor
        direction = score_sharpness_factor * jnp.dot(
            weights.astype(jnp.bfloat16), other, preferred_element_type=jnp.float32
        )
        tangent = (
            direction - unit_rows * jnp.sum(unit_rows * direction, axis=-1, keepdims=True)
        ) * inv_length
        sums_ref[tower : tower + 1, :] = jnp.sum(tangent * normed, axis=0, keepdims=True)
        scaled_back = tangent * gain
        gradient = (
            scaled_back
            - jnp.mean(scaled_back, axis=-1, keepdims=True)
            - normed * jnp.mean(scaled_back * normed, axis=-1, keepdims=True)
        ) * inverse
        grad_ref[0] = gradient.astype(grad_ref.dtype)
    first_lane = lax.broadcasted_iota(jnp.int32, (1, width), 1) == 0
    sums_ref[2:3, :] = jnp.where(first_lane, loss_rows[0] / real_count, 0.0)


def group_kernel(image_masks, text_masks, *refs):
    (sharpness_ref, shift_ref, multiplier_ref, counts_ref, picture_gain_ref, caption_gain_ref,
     partner_ref) = refs[:7]
    count = len(image_masks)
    pieces = refs[7 : 7 + 2 * count]
    (image_grad_ref, text_grad_ref, sums_ref, raw_ref, unit_ref, short_ref, normed_ref, inverse_ref,
     length_ref, weights_ref, flipped_ref, copy_sems) = refs[7 + 2 * count :]
    block_rows = pieces[0].shape[1]
    group_rows = raw_ref.shape[1]
    width = raw_ref.shape[2]
    arrivals = []
    for position, source in enumerate(pieces):
        tower, slot = divmod(position, count)
        rows = pl.ds(slot * block_rows, block_rows)
        arrival = pltpu.make_async_copy(source.at[0], raw_ref.at[tower, rows, :], copy_sems.at[position])
        arrival.start()
        arrivals.append(arrival)

    own_block = lax.axis_index("blk")
    blocks = counts_ref.shape[1]
    total = counts_ref[0, 0]
    for block in range(1, blocks):
        total = total + counts_ref[0, block]
    real_count = jnp.full((1, 1), total, jnp.int32).astype(jnp.float32)
    score_sharpness_factor = jnp.exp(jnp.full((1, 1), sharpness_ref[0], jnp.float32))
    score_shift_amount = jnp.full((1, 1), shift_ref[0], jnp.float32)
    grad_factor = jnp.full((1, 1), multiplier_ref[0], jnp.float32) / real_count

    def held(masks, shape, dim):
        place = lax.broadcasted_iota(jnp.int32, shape, dim)
        row = jnp.zeros(shape, jnp.int32)
        limit = jnp.zeros(shape, jnp.int32)
        for slot, mask in enumerate(masks):
            block = own_block ^ mask
            here = place // block_rows == slot
            row = jnp.where(here, block * block_rows + place % block_rows, row)
            limit = jnp.where(here, counts_ref[0, block], limit)
        return row, (row % block_rows) < limit

    image_row, image_real = held(image_masks, (group_rows, 1), 0)
    text_row, text_real = held(text_masks, (1, group_rows), 1)
    natural = lax.broadcasted_iota(jnp.int32, (group_rows, group_rows), 1)
    partner_of_image = jnp.sum(
        jnp.where(natural == image_row, partner_ref[...].astype(jnp.float32), 0.0), axis=1, keepdims=True
    ).astype(jnp.int32)

    for arrival in arrivals:
        arrival.wait()
    gains = (picture_gain_ref[...][None, :], caption_gain_ref[...][None, :])
    chunk = min(128, group_rows)
    for tower in range(2):
        for first in range(0, group_rows, chunk):
            rows = pl.ds(first, chunk)
            values = raw_ref[tower, rows, :].astype(jnp.float32)
            centred = values - jnp.mean(values, axis=-1, keepdims=True)
            inverse = lax.rsqrt(jnp.mean(centred * centred, axis=-1, keepdims=True) + epsilon)
            normed = centred * inverse
            scaled = normed * gains[tower]
            inv_length = lax.rsqrt(jnp.sum(scaled * scaled, axis=-1, keepdims=True) + epsilon)
            unit_rows = scaled * inv_length
            unit_ref[tower, rows, :] = unit_rows
            short_ref[tower, rows, :] = unit_rows.astype(short_ref.dtype)
            normed_ref[tower, rows, :] = normed
            inverse_ref[tower, rows, :] = inverse
            length_ref[tower, rows, :] = inv_length

    loss = jnp.zeros((1, 1), jnp.float32)
    for first in range(0, group_rows, chunk):
        rows = pl.ds(first, chunk)
        scores = lax.dot_general(
            short_ref[0, rows, :], short_ref[1], (((1,), (1,)), ((), ())), preferred_element_type=jnp.float32
        )
        score_similarity_table = score_sharpness_factor * scores + score_shift_amount
        labels = jnp.where(partner_of_image[first : first + chunk] == text_row, 1.0, -1.0)
        kept = image_real[first : first + chunk] & text_real
        margin = -labels * score_similarity_table
        softplus = jnp.maximum(margin, 0.0) + jnp.log1p(jnp.exp(-jnp.abs(margin)))
        loss = loss + jnp.sum(jnp.where(kept, softplus, 0.0), axis=(0, 1), keepdims=True)
        weights = jnp.where(kept, -labels * jax.nn.sigmoid(margin), 0.0) * grad_factor
        weights_ref[rows, :] = weights.astype(weights_ref.dtype)
        flipped_ref[:, rows] = weights.T.astype(flipped_ref.dtype)

    for tower, (pair_ref, grad_ref) in enumerate(((weights_ref, image_grad_ref), (flipped_ref, text_grad_ref))):
        gain_sum = jnp.zeros((1, width), jnp.float32)
        for first in range(0, group_rows, chunk):
            rows = pl.ds(first, chunk)
            direction = score_sharpness_factor * jnp.dot(
                pair_ref[rows, :], short_ref[1 - tower], preferred_element_type=jnp.float32
            )
            unit_rows = unit_ref[tower, rows, :]
            normed = normed_ref[tower, rows, :]
            tangent = (
                direction - unit_rows * jnp.sum(unit_rows * direction, axis=-1, keepdims=True)
            ) * length_ref[tower, rows, :]
            gain_sum = gain_sum + jnp.sum(tangent * normed, axis=0, keepdims=True)
            if first == 0:
                own = slice(0, block_rows)
                scaled_back = tangent[own] * gains[tower]
                gradient = (
                    scaled_back
                    - jnp.mean(scaled_back, axis=-1, keepdims=True)
                    - normed[own] * jnp.mean(scaled_back * normed[own], axis=-1, keepdims=True)
                ) * inverse_ref[tower, 0:block_rows, :]
                grad_ref[0] = gradient.astype(grad_ref.dtype)
        sums_ref[tower : tower + 1, :] = gain_sum
    first_lane = lax.broadcasted_iota(jnp.int32, (1, width), 1) == 0
    sums_ref[2:3, :] = jnp.where(first_lane, loss / real_count, 0.0)


def whole_group(
    picture_averaged_features,
    caption_averaged_features,
    picture_rescale_factor,
    caption_rescale_factor,
    exponent_of_sharpness,
    score_shift_term,
    objective_multiplier,
    matching_caption_index,
    genuine_entry_counts,
):
    count = lax.axis_size("blk")
    block_rows, width = picture_averaged_features.shape[1:]
    group_rows = count * block_rows
    pieces, masks, unused = gather_blocks(picture_averaged_features, caption_averaged_features, "blk")
    smem = pltpu.MemorySpace.SMEM
    vmem = pltpu.MemorySpace.VMEM
    grad_shape = jax.ShapeDtypeStruct(picture_averaged_features.shape, jnp.bfloat16)
    full = (2, group_rows, width)
    column = (2, group_rows, 1)
    image_grad, text_grad, sums = pl.pallas_call(
        functools.partial(group_kernel, tuple(masks[:count]), tuple(masks[count:])),
        out_shape=(grad_shape, grad_shape, jax.ShapeDtypeStruct((3, width), jnp.float32)),
        in_specs=[pl.BlockSpec(memory_space=smem)] * 4
        + [pl.BlockSpec(memory_space=vmem)] * 3
        + [pl.BlockSpec(memory_space=pl.ANY)] * len(pieces),
        out_specs=(pl.BlockSpec(memory_space=vmem),) * 3,
        scratch_shapes=[
            pltpu.VMEM(full, jnp.bfloat16),
            pltpu.VMEM(full, jnp.float32),
            pltpu.VMEM(full, jnp.bfloat16),
            pltpu.VMEM(full, jnp.float32),
            pltpu.VMEM(column, jnp.float32),
            pltpu.VMEM(column, jnp.float32),
            pltpu.VMEM((group_rows, group_rows), jnp.bfloat16),
            pltpu.VMEM((group_rows, group_rows), jnp.bfloat16),
            pltpu.SemaphoreType.DMA((len(pieces),)),
        ],
    )(
        exponent_of_sharpness,
        score_shift_term,
        objective_multiplier,
        genuine_entry_counts,
        picture_rescale_factor,
        caption_rescale_factor,
        matching_caption_index,
        *pieces,
    )
    group_loss = sums[2, 0:1]
    gain_grads = all_sum(sums, "rep", keep=2)
    return (image_grad, text_grad, gain_grads, group_loss)


def shards(
    picture_averaged_features,
    caption_averaged_features,
    picture_rescale_factor,
    caption_rescale_factor,
    exponent_of_sharpness,
    score_shift_term,
    objective_multiplier,
    matching_caption_index,
    genuine_entry_counts,
):
    width = picture_averaged_features.shape[2]
    first, second = embed_both(
        picture_averaged_features, caption_averaged_features, picture_rescale_factor, caption_rescale_factor
    )
    pieces, masks, offsets = gather_blocks(first, second, "blk")

    smem = pltpu.MemorySpace.SMEM
    vmem = pltpu.MemorySpace.VMEM
    grad_shape = jax.ShapeDtypeStruct(picture_averaged_features.shape, jnp.bfloat16)
    image_grad, text_grad, sums = pl.pallas_call(
        functools.partial(grad_kernel, tuple(masks), tuple(offsets)),
        out_shape=(grad_shape, grad_shape, jax.ShapeDtypeStruct((3, width), jnp.float32)),
        in_specs=[pl.BlockSpec(memory_space=smem)] * 4
        + [pl.BlockSpec(memory_space=vmem)] * 5
        + [pl.BlockSpec(memory_space=pl.ANY)] * len(pieces),
        out_specs=(pl.BlockSpec(memory_space=vmem),) * 3,
        scratch_shapes=[
            pltpu.VMEM((2, len(pieces) * pieces[0].shape[1], width), pieces[0].dtype),
            pltpu.SemaphoreType.DMA((len(pieces),)),
        ],
    )(
        exponent_of_sharpness,
        score_shift_term,
        objective_multiplier,
        genuine_entry_counts,
        picture_averaged_features,
        caption_averaged_features,
        picture_rescale_factor,
        caption_rescale_factor,
        matching_caption_index,
        *pieces,
    )

    group_sums = all_sum(sums, "blk")
    group_loss = group_sums[2, 0:1]
    gain_grads = all_sum(group_sums, "rep", keep=2)
    return (image_grad, text_grad, gain_grads, group_loss)


def body(*args):
    group_rows = args[0].shape[1] * lax.axis_size("blk")
    return (whole_group if group_rows <= 512 else shards)(*args)


def solution(mesh):
    placed = (
        P("rep", "blk", None),
        P("rep", "blk", None),
        P(),
        P(),
        P(),
        P(),
        P(),
        P("rep", None),
        P("rep", None),
    )
    return jax.shard_map(
        body,
        mesh=mesh,
        in_specs=placed,
        out_specs=(P("rep", "blk", None), P("rep", "blk", None), P(), P("rep")),
        check_vma=False,
    )
```

```python
import functools

import jax
import jax.numpy as jnp
from jax import lax
from jax.sharding import PartitionSpec as P
from jax.experimental import pallas as pl
from jax.experimental.pallas import tpu as pltpu

epsilon = 1e-06


def xor_swap(value, axis, bit):
    count = lax.axis_size(axis)
    return lax.ppermute(value, axis, [(source, source ^ bit) for source in range(count)])


def power_of_two(count):
    return count > 1 and count & (count - 1) == 0


def gather_blocks(first, second, axis):
    count = lax.axis_size(axis)
    half = first.shape[1]
    if not power_of_two(count) or count < 4:
        own = lax.axis_index(axis)
        pieces = [lax.all_gather(part, axis, axis=1, tiled=False) for part in (first, second)]
        pieces = [
            lax.dynamic_index_in_dim(part, own ^ mask, axis=1, keepdims=False)
            for part in pieces
            for mask in range(count)
        ]
        return pieces, list(range(count)) * 2, [0] * count + [half] * count
    chip_bits = [1 << b for b in range(1, count.bit_length() - 1)]
    orders = (chip_bits, chip_bits[::-1])
    routed = ([first], [second])
    routed_masks = ([0], [0])
    fresh = ([0], [0])
    shared = ([], [])
    shared_masks = ([], [])
    for step in range(len(chip_bits) + 1):
        last = step == len(chip_bits)
        sent = [None, None]
        if not last:
            sent = [xor_swap(tuple(routed[h]), axis, orders[h][step]) for h in range(2)]
        across = [xor_swap(tuple(routed[h][i] for i in fresh[h]), axis, 1) for h in range(2)]
        for h in range(2):
            shared[h].extend(across[h])
            shared_masks[h].extend([routed_masks[h][i] ^ 1 for i in fresh[h]])
            if not last:
                bit = orders[h][step]
                fresh[h][:] = list(range(len(routed[h]), 2 * len(routed[h])))
                routed[h].extend(sent[h])
                routed_masks[h].extend([mask ^ bit for mask in routed_masks[h]])
    gathered = routed[0] + shared[0] + routed[1] + shared[1]
    masks = routed_masks[0] + shared_masks[0] + routed_masks[1] + shared_masks[1]
    offsets = [0] * count + [half] * count
    return gathered, masks, offsets


def all_sum(value, axis, keep=None):
    keep = value.shape[0] if keep is None else keep
    count = lax.axis_size(axis)
    if not power_of_two(count):
        return lax.psum(value, axis)[:keep]
    bit = 1
    while bit < count:
        if bit * 2 < count:
            value = value + xor_swap(value, axis, bit)
        else:
            value = value[:keep] + xor_swap(value, axis, bit)[:keep]
        bit *= 2
    return value


def embed_kernel(picture_ref, caption_ref, picture_gain_ref, caption_gain_ref, first_ref, second_ref):
    half = first_ref.shape[1]
    towers = ((picture_ref, picture_gain_ref), (caption_ref, caption_gain_ref))
    for tower, (pooled_ref, gain_ref) in enumerate(towers):
        values = pooled_ref[0].astype(jnp.float32)
        centred = values - jnp.mean(values, axis=-1, keepdims=True)
        inverse = lax.rsqrt(jnp.mean(centred * centred, axis=-1, keepdims=True) + epsilon)
        scaled = centred * inverse * gain_ref[...][None, :]
        inv_length = lax.rsqrt(jnp.sum(scaled * scaled, axis=-1, keepdims=True) + epsilon)
        unit_rows = (scaled * inv_length).astype(first_ref.dtype)
        first_ref[tower] = unit_rows[:half]
        second_ref[tower] = unit_rows[half:]


def embed_both(picture, caption, picture_gain, caption_gain):
    rows, width = picture.shape[1:]
    vmem = pltpu.MemorySpace.VMEM
    half = jax.ShapeDtypeStruct((2, rows // 2, width), jnp.bfloat16)
    return pl.pallas_call(
        embed_kernel,
        out_shape=(half, half),
        in_specs=[pl.BlockSpec(memory_space=vmem)] * 4,
        out_specs=(pl.BlockSpec(memory_space=vmem), pl.BlockSpec(memory_space=vmem)),
    )(picture, caption, picture_gain, caption_gain)


def grad_kernel(masks, offsets, *refs):
    (sharpness_ref, shift_ref, multiplier_ref, counts_ref, picture_ref, caption_ref, picture_gain_ref,
     caption_gain_ref, partner_ref) = refs[:9]
    pieces = refs[9 : 9 + len(masks)]
    image_grad_ref, text_grad_ref, sums_ref, gathered_ref, copy_sems = refs[9 + len(masks) :]
    piece = pieces[0].shape[1]
    arrivals = [
        pltpu.make_async_copy(
            source, gathered_ref.at[:, position * piece : (position + 1) * piece, :], copy_sems.at[position]
        )
        for position, source in enumerate(pieces)
    ]
    for arrival in arrivals:
        arrival.start()
    blocks = counts_ref.shape[1]
    own_block = lax.axis_index("blk")
    block_rows = picture_ref.shape[1]
    width = picture_ref.shape[2]
    group_rows = gathered_ref.shape[1]
    own_start = own_block * block_rows
    total = counts_ref[0, 0]
    for block in range(1, blocks):
        total = total + counts_ref[0, block]
    real_count = jnp.full((1, 1), total, jnp.int32).astype(jnp.float32)
    score_sharpness_factor = jnp.exp(jnp.full((1, 1), sharpness_ref[0], jnp.float32))
    score_shift_amount = jnp.full((1, 1), shift_ref[0], jnp.float32)
    grad_factor = jnp.full((1, 1), multiplier_ref[0], jnp.float32) / real_count

    lane = lax.broadcasted_iota(jnp.int32, (1, group_rows), 1)
    held_row = jnp.zeros((1, group_rows), jnp.int32)
    limit = jnp.zeros((1, group_rows), jnp.int32)
    for position, (mask, offset) in enumerate(zip(masks, offsets)):
        block = own_block ^ mask
        here = lane // piece == position
        held_row = jnp.where(here, block * block_rows + offset + lane % piece, held_row)
        limit = jnp.where(here, counts_ref[0, block], limit)
    real_group = (held_row % block_rows) < limit
    sub = lax.broadcasted_iota(jnp.int32, (block_rows, 1), 0)
    real_own = sub < counts_ref[0, own_block]
    kept = real_own & real_group

    natural = lax.broadcasted_iota(jnp.int32, (block_rows, group_rows), 1)
    own_index = own_start + lax.broadcasted_iota(jnp.int32, (block_rows, group_rows), 0)
    partner_row = partner_ref[...]
    own_partner = jnp.sum(
        jnp.where(natural == own_index, partner_row.astype(jnp.float32), 0.0), axis=1, keepdims=True
    ).astype(jnp.int32)
    matched_image = jnp.sum(
        jnp.where(partner_row == own_index, natural.astype(jnp.float32), 0.0), axis=1, keepdims=True
    ).astype(jnp.int32)
    positives = (own_partner == held_row, matched_image == held_row)

    start_b = len(masks) // 2 * piece
    for arrival in arrivals:
        arrival.wait()
    loss_rows = []
    towers = ((picture_ref, picture_gain_ref, image_grad_ref), (caption_ref, caption_gain_ref, text_grad_ref))
    for tower, (pooled_ref, gain_ref, grad_ref) in enumerate(towers):
        values = pooled_ref[0].astype(jnp.float32)
        gain = gain_ref[...][None, :]
        centred = values - jnp.mean(values, axis=-1, keepdims=True)
        inverse = lax.rsqrt(jnp.mean(centred * centred, axis=-1, keepdims=True) + epsilon)
        normed = centred * inverse
        scaled = normed * gain
        inv_length = lax.rsqrt(jnp.sum(scaled * scaled, axis=-1, keepdims=True) + epsilon)
        unit_rows = scaled * inv_length

        own = jnp.concatenate(
            [gathered_ref[tower, 0:piece, :], gathered_ref[tower, start_b : start_b + piece, :]], axis=0
        )
        other = gathered_ref[1 - tower]
        scores = lax.dot_general(own, other, (((1,), (1,)), ((), ())), preferred_element_type=jnp.float32)
        score_similarity_table = score_sharpness_factor * scores + score_shift_amount
        labels = jnp.where(positives[tower], 1.0, -1.0)
        margin = -labels * score_similarity_table
        if tower == 0:
            softplus = jnp.maximum(margin, 0.0) + jnp.log1p(jnp.exp(-jnp.abs(margin)))
            loss_rows.append(jnp.sum(jnp.where(kept, softplus, 0.0), axis=(0, 1), keepdims=True))
        weights = jnp.where(kept, -labels * jax.nn.sigmoid(margin), 0.0) * grad_factor
        direction = score_sharpness_factor * jnp.dot(
            weights.astype(jnp.bfloat16), other, preferred_element_type=jnp.float32
        )
        tangent = (
            direction - unit_rows * jnp.sum(unit_rows * direction, axis=-1, keepdims=True)
        ) * inv_length
        sums_ref[tower : tower + 1, :] = jnp.sum(tangent * normed, axis=0, keepdims=True)
        scaled_back = tangent * gain
        gradient = (
            scaled_back
            - jnp.mean(scaled_back, axis=-1, keepdims=True)
            - normed * jnp.mean(scaled_back * normed, axis=-1, keepdims=True)
        ) * inverse
        grad_ref[0] = gradient.astype(grad_ref.dtype)
    first_lane = lax.broadcasted_iota(jnp.int32, (1, width), 1) == 0
    sums_ref[2:3, :] = jnp.where(first_lane, loss_rows[0] / real_count, 0.0)


def group_kernel(image_masks, text_masks, *refs):
    (sharpness_ref, shift_ref, multiplier_ref, counts_ref, picture_gain_ref, caption_gain_ref,
     partner_ref) = refs[:7]
    count = len(image_masks)
    pieces = refs[7 : 7 + 2 * count]
    (image_grad_ref, text_grad_ref, sums_ref, raw_ref, unit_ref, short_ref, normed_ref, inverse_ref,
     length_ref, weights_ref, copy_sems) = refs[7 + 2 * count :]
    block_rows = pieces[0].shape[1]
    group_rows = raw_ref.shape[1]
    width = raw_ref.shape[2]
    arrivals = []
    for position, source in enumerate(pieces):
        tower, slot = divmod(position, count)
        rows = pl.ds(slot * block_rows, block_rows)
        arrival = pltpu.make_async_copy(source.at[0], raw_ref.at[tower, rows, :], copy_sems.at[position])
        arrival.start()
        arrivals.append(arrival)

    own_block = lax.axis_index("blk")
    blocks = counts_ref.shape[1]
    total = counts_ref[0, 0]
    for block in range(1, blocks):
        total = total + counts_ref[0, block]
    real_count = jnp.full((1, 1), total, jnp.int32).astype(jnp.float32)
    score_sharpness_factor = jnp.exp(jnp.full((1, 1), sharpness_ref[0], jnp.float32))
    score_shift_amount = jnp.full((1, 1), shift_ref[0], jnp.float32)
    grad_factor = jnp.full((1, 1), multiplier_ref[0], jnp.float32) / real_count

    def held(masks, shape, dim):
        place = lax.broadcasted_iota(jnp.int32, shape, dim)
        row = jnp.zeros(shape, jnp.int32)
        limit = jnp.zeros(shape, jnp.int32)
        for slot, mask in enumerate(masks):
            block = own_block ^ mask
            here = place // block_rows == slot
            row = jnp.where(here, block * block_rows + place % block_rows, row)
            limit = jnp.where(here, counts_ref[0, block], limit)
        return row, (row % block_rows) < limit

    image_row, image_real = held(image_masks, (group_rows, 1), 0)
    text_row, text_real = held(text_masks, (1, group_rows), 1)
    natural = lax.broadcasted_iota(jnp.int32, (group_rows, group_rows), 1)
    partner_of_image = jnp.sum(
        jnp.where(natural == image_row, partner_ref[...].astype(jnp.float32), 0.0), axis=1, keepdims=True
    ).astype(jnp.int32)

    for arrival in arrivals:
        arrival.wait()
    gains = (picture_gain_ref[...][None, :], caption_gain_ref[...][None, :])
    chunk = min(128, group_rows)
    for tower in range(2):
        for first in range(0, group_rows, chunk):
            rows = pl.ds(first, chunk)
            values = raw_ref[tower, rows, :].astype(jnp.float32)
            centred = values - jnp.mean(values, axis=-1, keepdims=True)
            inverse = lax.rsqrt(jnp.mean(centred * centred, axis=-1, keepdims=True) + epsilon)
            normed = centred * inverse
            scaled = normed * gains[tower]
            inv_length = lax.rsqrt(jnp.sum(scaled * scaled, axis=-1, keepdims=True) + epsilon)
            unit_rows = scaled * inv_length
            unit_ref[tower, rows, :] = unit_rows
            short_ref[tower, rows, :] = unit_rows.astype(short_ref.dtype)
            normed_ref[tower, rows, :] = normed
            inverse_ref[tower, rows, :] = inverse
            length_ref[tower, rows, :] = inv_length

    loss = jnp.zeros((1, 1), jnp.float32)
    for first in range(0, group_rows, chunk):
        rows = pl.ds(first, chunk)
        scores = lax.dot_general(
            short_ref[0, rows, :], short_ref[1], (((1,), (1,)), ((), ())), preferred_element_type=jnp.float32
        )
        score_similarity_table = score_sharpness_factor * scores + score_shift_amount
        labels = jnp.where(partner_of_image[first : first + chunk] == text_row, 1.0, -1.0)
        kept = image_real[first : first + chunk] & text_real
        margin = -labels * score_similarity_table
        decay = jnp.exp(-jnp.abs(margin))
        softplus = jnp.maximum(margin, 0.0) + jnp.log1p(decay)
        loss = loss + jnp.sum(jnp.where(kept, softplus, 0.0), axis=(0, 1), keepdims=True)
        sigmoid = jnp.where(margin >= 0.0, 1.0, decay) / (1.0 + decay)
        weights = jnp.where(kept, -labels * sigmoid, 0.0) * grad_factor
        weights_ref[rows, :] = weights.astype(weights_ref.dtype)

    for tower, grad_ref in enumerate((image_grad_ref, text_grad_ref)):
        gain_sum = jnp.zeros((1, width), jnp.float32)
        for first in range(0, group_rows, chunk):
            rows = pl.ds(first, chunk)
            if tower == 0:
                pairs = weights_ref[rows, :]
                contract = (((1,), (0,)), ((), ()))
            else:
                pairs = weights_ref[:, rows]
                contract = (((0,), (0,)), ((), ()))
            direction = score_sharpness_factor * lax.dot_general(
                pairs, short_ref[1 - tower], contract, preferred_element_type=jnp.float32
            )
            unit_rows = unit_ref[tower, rows, :]
            normed = normed_ref[tower, rows, :]
            tangent = (
                direction - unit_rows * jnp.sum(unit_rows * direction, axis=-1, keepdims=True)
            ) * length_ref[tower, rows, :]
            gain_sum = gain_sum + jnp.sum(tangent * normed, axis=0, keepdims=True)
            if first == 0:
                own = slice(0, block_rows)
                scaled_back = tangent[own] * gains[tower]
                gradient = (
                    scaled_back
                    - jnp.mean(scaled_back, axis=-1, keepdims=True)
                    - normed[own] * jnp.mean(scaled_back * normed[own], axis=-1, keepdims=True)
                ) * inverse_ref[tower, 0:block_rows, :]
                grad_ref[0] = gradient.astype(grad_ref.dtype)
        sums_ref[tower : tower + 1, :] = gain_sum
    first_lane = lax.broadcasted_iota(jnp.int32, (1, width), 1) == 0
    sums_ref[2:3, :] = jnp.where(first_lane, loss / real_count, 0.0)


def whole_group(
    picture_averaged_features,
    caption_averaged_features,
    picture_rescale_factor,
    caption_rescale_factor,
    exponent_of_sharpness,
    score_shift_term,
    objective_multiplier,
    matching_caption_index,
    genuine_entry_counts,
):
    count = lax.axis_size("blk")
    block_rows, width = picture_averaged_features.shape[1:]
    group_rows = count * block_rows
    pieces, masks, unused = gather_blocks(picture_averaged_features, caption_averaged_features, "blk")
    smem = pltpu.MemorySpace.SMEM
    vmem = pltpu.MemorySpace.VMEM
    grad_shape = jax.ShapeDtypeStruct(picture_averaged_features.shape, jnp.bfloat16)
    full = (2, group_rows, width)
    column = (2, group_rows, 1)
    image_grad, text_grad, sums = pl.pallas_call(
        functools.partial(group_kernel, tuple(masks[:count]), tuple(masks[count:])),
        out_shape=(grad_shape, grad_shape, jax.ShapeDtypeStruct((3, width), jnp.float32)),
        in_specs=[pl.BlockSpec(memory_space=smem)] * 4
        + [pl.BlockSpec(memory_space=vmem)] * 3
        + [pl.BlockSpec(memory_space=pl.ANY)] * len(pieces),
        out_specs=(pl.BlockSpec(memory_space=vmem),) * 3,
        scratch_shapes=[
            pltpu.VMEM(full, jnp.bfloat16),
            pltpu.VMEM(full, jnp.float32),
            pltpu.VMEM(full, jnp.bfloat16),
            pltpu.VMEM(full, jnp.float32),
            pltpu.VMEM(column, jnp.float32),
            pltpu.VMEM(column, jnp.float32),
            pltpu.VMEM((group_rows, group_rows), jnp.bfloat16),
            pltpu.SemaphoreType.DMA((len(pieces),)),
        ],
    )(
        exponent_of_sharpness,
        score_shift_term,
        objective_multiplier,
        genuine_entry_counts,
        picture_rescale_factor,
        caption_rescale_factor,
        matching_caption_index,
        *pieces,
    )
    group_loss = sums[2, 0:1]
    gain_grads = all_sum(sums, "rep", keep=2)
    return (image_grad, text_grad, gain_grads, group_loss)


def shards(
    picture_averaged_features,
    caption_averaged_features,
    picture_rescale_factor,
    caption_rescale_factor,
    exponent_of_sharpness,
    score_shift_term,
    objective_multiplier,
    matching_caption_index,
    genuine_entry_counts,
):
    width = picture_averaged_features.shape[2]
    first, second = embed_both(
        picture_averaged_features, caption_averaged_features, picture_rescale_factor, caption_rescale_factor
    )
    pieces, masks, offsets = gather_blocks(first, second, "blk")

    smem = pltpu.MemorySpace.SMEM
    vmem = pltpu.MemorySpace.VMEM
    grad_shape = jax.ShapeDtypeStruct(picture_averaged_features.shape, jnp.bfloat16)
    image_grad, text_grad, sums = pl.pallas_call(
        functools.partial(grad_kernel, tuple(masks), tuple(offsets)),
        out_shape=(grad_shape, grad_shape, jax.ShapeDtypeStruct((3, width), jnp.float32)),
        in_specs=[pl.BlockSpec(memory_space=smem)] * 4
        + [pl.BlockSpec(memory_space=vmem)] * 5
        + [pl.BlockSpec(memory_space=pl.ANY)] * len(pieces),
        out_specs=(pl.BlockSpec(memory_space=vmem),) * 3,
        scratch_shapes=[
            pltpu.VMEM((2, len(pieces) * pieces[0].shape[1], width), pieces[0].dtype),
            pltpu.SemaphoreType.DMA((len(pieces),)),
        ],
    )(
        exponent_of_sharpness,
        score_shift_term,
        objective_multiplier,
        genuine_entry_counts,
        picture_averaged_features,
        caption_averaged_features,
        picture_rescale_factor,
        caption_rescale_factor,
        matching_caption_index,
        *pieces,
    )

    group_sums = all_sum(sums, "blk")
    group_loss = group_sums[2, 0:1]
    gain_grads = all_sum(group_sums, "rep", keep=2)
    return (image_grad, text_grad, gain_grads, group_loss)


def body(*args):
    group_rows = args[0].shape[1] * lax.axis_size("blk")
    return (whole_group if group_rows <= 512 else shards)(*args)


def solution(mesh):
    placed = (
        P("rep", "blk", None),
        P("rep", "blk", None),
        P(),
        P(),
        P(),
        P(),
        P(),
        P("rep", None),
        P("rep", None),
    )
    return jax.shard_map(
        body,
        mesh=mesh,
        in_specs=placed,
        out_specs=(P("rep", "blk", None), P("rep", "blk", None), P(), P("rep")),
        check_vma=False,
    )
```

```python
import functools

import jax
import jax.numpy as jnp
from jax import lax
from jax.sharding import PartitionSpec as P
from jax.experimental import pallas as pl
from jax.experimental.pallas import tpu as pltpu

epsilon = 1e-06


def xor_swap(value, axis, bit):
    count = lax.axis_size(axis)
    return lax.ppermute(value, axis, [(source, source ^ bit) for source in range(count)])


def power_of_two(count):
    return count > 1 and count & (count - 1) == 0


def gather_blocks(first, second, axis):
    count = lax.axis_size(axis)
    half = first.shape[1]
    if not power_of_two(count) or count < 4:
        own = lax.axis_index(axis)
        pieces = [lax.all_gather(part, axis, axis=1, tiled=False) for part in (first, second)]
        pieces = [
            lax.dynamic_index_in_dim(part, own ^ mask, axis=1, keepdims=False)
            for part in pieces
            for mask in range(count)
        ]
        return pieces, list(range(count)) * 2, [0] * count + [half] * count
    chip_bits = [1 << b for b in range(1, count.bit_length() - 1)]
    orders = (chip_bits, chip_bits[::-1])
    routed = ([first], [second])
    routed_masks = ([0], [0])
    fresh = ([0], [0])
    shared = ([], [])
    shared_masks = ([], [])
    for step in range(len(chip_bits) + 1):
        last = step == len(chip_bits)
        sent = [None, None]
        if not last:
            sent = [xor_swap(tuple(routed[h]), axis, orders[h][step]) for h in range(2)]
        across = [xor_swap(tuple(routed[h][i] for i in fresh[h]), axis, 1) for h in range(2)]
        for h in range(2):
            shared[h].extend(across[h])
            shared_masks[h].extend([routed_masks[h][i] ^ 1 for i in fresh[h]])
            if not last:
                bit = orders[h][step]
                fresh[h][:] = list(range(len(routed[h]), 2 * len(routed[h])))
                routed[h].extend(sent[h])
                routed_masks[h].extend([mask ^ bit for mask in routed_masks[h]])
    gathered = routed[0] + shared[0] + routed[1] + shared[1]
    masks = routed_masks[0] + shared_masks[0] + routed_masks[1] + shared_masks[1]
    offsets = [0] * count + [half] * count
    return gathered, masks, offsets


def all_sum(value, axis, keep=None):
    keep = value.shape[0] if keep is None else keep
    count = lax.axis_size(axis)
    if not power_of_two(count):
        return lax.psum(value, axis)[:keep]
    bit = 1
    while bit < count:
        if bit * 2 < count:
            value = value + xor_swap(value, axis, bit)
        else:
            value = value[:keep] + xor_swap(value, axis, bit)[:keep]
        bit *= 2
    return value


def embed_kernel(picture_ref, caption_ref, picture_gain_ref, caption_gain_ref, first_ref, second_ref):
    half = first_ref.shape[1]
    towers = ((picture_ref, picture_gain_ref), (caption_ref, caption_gain_ref))
    for tower, (pooled_ref, gain_ref) in enumerate(towers):
        values = pooled_ref[0].astype(jnp.float32)
        centred = values - jnp.mean(values, axis=-1, keepdims=True)
        inverse = lax.rsqrt(jnp.mean(centred * centred, axis=-1, keepdims=True) + epsilon)
        scaled = centred * inverse * gain_ref[...][None, :]
        inv_length = lax.rsqrt(jnp.sum(scaled * scaled, axis=-1, keepdims=True) + epsilon)
        unit_rows = (scaled * inv_length).astype(first_ref.dtype)
        first_ref[tower] = unit_rows[:half]
        second_ref[tower] = unit_rows[half:]


def embed_both(picture, caption, picture_gain, caption_gain):
    rows, width = picture.shape[1:]
    vmem = pltpu.MemorySpace.VMEM
    half = jax.ShapeDtypeStruct((2, rows // 2, width), jnp.bfloat16)
    return pl.pallas_call(
        embed_kernel,
        out_shape=(half, half),
        in_specs=[pl.BlockSpec(memory_space=vmem)] * 4,
        out_specs=(pl.BlockSpec(memory_space=vmem), pl.BlockSpec(memory_space=vmem)),
    )(picture, caption, picture_gain, caption_gain)


def grad_kernel(masks, offsets, *refs):
    (sharpness_ref, shift_ref, multiplier_ref, counts_ref, picture_ref, caption_ref, picture_gain_ref,
     caption_gain_ref, partner_ref) = refs[:9]
    pieces = refs[9 : 9 + len(masks)]
    image_grad_ref, text_grad_ref, sums_ref, gathered_ref, copy_sems = refs[9 + len(masks) :]
    piece = pieces[0].shape[1]
    arrivals = [
        pltpu.make_async_copy(
            source, gathered_ref.at[:, position * piece : (position + 1) * piece, :], copy_sems.at[position]
        )
        for position, source in enumerate(pieces)
    ]
    for arrival in arrivals:
        arrival.start()
    blocks = counts_ref.shape[1]
    own_block = lax.axis_index("blk")
    block_rows = picture_ref.shape[1]
    width = picture_ref.shape[2]
    group_rows = gathered_ref.shape[1]
    own_start = own_block * block_rows
    total = counts_ref[0, 0]
    for block in range(1, blocks):
        total = total + counts_ref[0, block]
    real_count = jnp.full((1, 1), total, jnp.int32).astype(jnp.float32)
    score_sharpness_factor = jnp.exp(jnp.full((1, 1), sharpness_ref[0], jnp.float32))
    score_shift_amount = jnp.full((1, 1), shift_ref[0], jnp.float32)
    grad_factor = jnp.full((1, 1), multiplier_ref[0], jnp.float32) / real_count

    lane = lax.broadcasted_iota(jnp.int32, (1, group_rows), 1)
    held_row = jnp.zeros((1, group_rows), jnp.int32)
    limit = jnp.zeros((1, group_rows), jnp.int32)
    for position, (mask, offset) in enumerate(zip(masks, offsets)):
        block = own_block ^ mask
        here = lane // piece == position
        held_row = jnp.where(here, block * block_rows + offset + lane % piece, held_row)
        limit = jnp.where(here, counts_ref[0, block], limit)
    real_group = (held_row % block_rows) < limit
    sub = lax.broadcasted_iota(jnp.int32, (block_rows, 1), 0)
    real_own = sub < counts_ref[0, own_block]
    kept = real_own & real_group

    natural = lax.broadcasted_iota(jnp.int32, (block_rows, group_rows), 1)
    own_index = own_start + lax.broadcasted_iota(jnp.int32, (block_rows, group_rows), 0)
    partner_row = partner_ref[...]
    own_partner = jnp.sum(
        jnp.where(natural == own_index, partner_row.astype(jnp.float32), 0.0), axis=1, keepdims=True
    ).astype(jnp.int32)
    matched_image = jnp.sum(
        jnp.where(partner_row == own_index, natural.astype(jnp.float32), 0.0), axis=1, keepdims=True
    ).astype(jnp.int32)
    positives = (own_partner == held_row, matched_image == held_row)

    start_b = len(masks) // 2 * piece
    for arrival in arrivals:
        arrival.wait()
    loss_rows = []
    towers = ((picture_ref, picture_gain_ref, image_grad_ref), (caption_ref, caption_gain_ref, text_grad_ref))
    for tower, (pooled_ref, gain_ref, grad_ref) in enumerate(towers):
        values = pooled_ref[0].astype(jnp.float32)
        gain = gain_ref[...][None, :]
        centred = values - jnp.mean(values, axis=-1, keepdims=True)
        inverse = lax.rsqrt(jnp.mean(centred * centred, axis=-1, keepdims=True) + epsilon)
        normed = centred * inverse
        scaled = normed * gain
        inv_length = lax.rsqrt(jnp.sum(scaled * scaled, axis=-1, keepdims=True) + epsilon)
        unit_rows = scaled * inv_length

        own = jnp.concatenate(
            [gathered_ref[tower, 0:piece, :], gathered_ref[tower, start_b : start_b + piece, :]], axis=0
        )
        other = gathered_ref[1 - tower]
        scores = lax.dot_general(own, other, (((1,), (1,)), ((), ())), preferred_element_type=jnp.float32)
        score_similarity_table = score_sharpness_factor * scores + score_shift_amount
        labels = jnp.where(positives[tower], 1.0, -1.0)
        margin = -labels * score_similarity_table
        if tower == 0:
            softplus = jnp.maximum(margin, 0.0) + jnp.log1p(jnp.exp(-jnp.abs(margin)))
            loss_rows.append(jnp.sum(jnp.where(kept, softplus, 0.0), axis=(0, 1), keepdims=True))
        weights = jnp.where(kept, -labels * jax.nn.sigmoid(margin), 0.0) * grad_factor
        direction = score_sharpness_factor * jnp.dot(
            weights.astype(jnp.bfloat16), other, preferred_element_type=jnp.float32
        )
        tangent = (
            direction - unit_rows * jnp.sum(unit_rows * direction, axis=-1, keepdims=True)
        ) * inv_length
        sums_ref[tower : tower + 1, :] = jnp.sum(tangent * normed, axis=0, keepdims=True)
        scaled_back = tangent * gain
        gradient = (
            scaled_back
            - jnp.mean(scaled_back, axis=-1, keepdims=True)
            - normed * jnp.mean(scaled_back * normed, axis=-1, keepdims=True)
        ) * inverse
        grad_ref[0] = gradient.astype(grad_ref.dtype)
    first_lane = lax.broadcasted_iota(jnp.int32, (1, width), 1) == 0
    sums_ref[2:3, :] = jnp.where(first_lane, loss_rows[0] / real_count, 0.0)


def group_kernel(image_masks, text_masks, *refs):
    (sharpness_ref, shift_ref, multiplier_ref, counts_ref, picture_gain_ref, caption_gain_ref,
     partner_ref) = refs[:7]
    count = len(image_masks)
    pieces = refs[7 : 7 + 2 * count]
    (image_grad_ref, text_grad_ref, sums_ref, raw_ref, unit_ref, short_ref, normed_ref, inverse_ref,
     length_ref, weights_ref, copy_sems) = refs[7 + 2 * count :]
    block_rows = pieces[0].shape[1]
    group_rows = raw_ref.shape[1]
    width = raw_ref.shape[2]
    arrivals = []
    for position, source in enumerate(pieces):
        tower, slot = divmod(position, count)
        rows = pl.ds(slot * block_rows, block_rows)
        arrival = pltpu.make_async_copy(source.at[0], raw_ref.at[tower, rows, :], copy_sems.at[position])
        arrival.start()
        arrivals.append(arrival)

    own_block = lax.axis_index("blk")
    blocks = counts_ref.shape[1]
    total = counts_ref[0, 0]
    for block in range(1, blocks):
        total = total + counts_ref[0, block]
    real_count = jnp.full((1, 1), total, jnp.int32).astype(jnp.float32)
    score_sharpness_factor = jnp.exp(jnp.full((1, 1), sharpness_ref[0], jnp.float32))
    score_shift_amount = jnp.full((1, 1), shift_ref[0], jnp.float32)
    grad_factor = jnp.full((1, 1), multiplier_ref[0], jnp.float32) / real_count

    def held(masks, shape, dim):
        place = lax.broadcasted_iota(jnp.int32, shape, dim)
        row = jnp.zeros(shape, jnp.int32)
        limit = jnp.zeros(shape, jnp.int32)
        for slot, mask in enumerate(masks):
            block = own_block ^ mask
            here = place // block_rows == slot
            row = jnp.where(here, block * block_rows + place % block_rows, row)
            limit = jnp.where(here, counts_ref[0, block], limit)
        return row, (row % block_rows) < limit

    image_row, image_real = held(image_masks, (group_rows, 1), 0)
    text_row, text_real = held(text_masks, (1, group_rows), 1)
    natural = lax.broadcasted_iota(jnp.int32, (group_rows, group_rows), 1)
    partner_of_image = jnp.sum(
        jnp.where(natural == image_row, partner_ref[...].astype(jnp.float32), 0.0), axis=1, keepdims=True
    ).astype(jnp.int32)

    gains = (picture_gain_ref[...][None, :], caption_gain_ref[...][None, :])
    chunk = min(128, group_rows)
    waited = set()
    for tower in range(2):
        for first in range(0, group_rows, chunk):
            rows = pl.ds(first, chunk)
            for slot in range(first // block_rows, (first + chunk - 1) // block_rows + 1):
                if tower * count + slot not in waited:
                    waited.add(tower * count + slot)
                    arrivals[tower * count + slot].wait()
            values = raw_ref[tower, rows, :].astype(jnp.float32)
            centred = values - jnp.mean(values, axis=-1, keepdims=True)
            inverse = lax.rsqrt(jnp.mean(centred * centred, axis=-1, keepdims=True) + epsilon)
            normed = centred * inverse
            scaled = normed * gains[tower]
            inv_length = lax.rsqrt(jnp.sum(scaled * scaled, axis=-1, keepdims=True) + epsilon)
            unit_rows = scaled * inv_length
            unit_ref[tower, rows, :] = unit_rows
            short_ref[tower, rows, :] = unit_rows.astype(short_ref.dtype)
            normed_ref[tower, rows, :] = normed
            inverse_ref[tower, rows, :] = inverse
            length_ref[tower, rows, :] = inv_length

    loss = jnp.zeros((1, 1), jnp.float32)
    for first in range(0, group_rows, chunk):
        rows = pl.ds(first, chunk)
        scores = lax.dot_general(
            short_ref[0, rows, :], short_ref[1], (((1,), (1,)), ((), ())), preferred_element_type=jnp.float32
        )
        score_similarity_table = score_sharpness_factor * scores + score_shift_amount
        labels = jnp.where(partner_of_image[first : first + chunk] == text_row, 1.0, -1.0)
        kept = image_real[first : first + chunk] & text_real
        margin = -labels * score_similarity_table
        decay = jnp.exp(-jnp.abs(margin))
        softplus = jnp.maximum(margin, 0.0) + jnp.log1p(decay)
        loss = loss + jnp.sum(jnp.where(kept, softplus, 0.0), axis=(0, 1), keepdims=True)
        sigmoid = jnp.where(margin >= 0.0, 1.0, decay) / (1.0 + decay)
        weights = jnp.where(kept, -labels * sigmoid, 0.0) * grad_factor
        weights_ref[rows, :] = weights.astype(weights_ref.dtype)

    for tower, grad_ref in enumerate((image_grad_ref, text_grad_ref)):
        gain_sum = jnp.zeros((1, width), jnp.float32)
        for first in range(0, group_rows, chunk):
            rows = pl.ds(first, chunk)
            if tower == 0:
                pairs = weights_ref[rows, :]
                contract = (((1,), (0,)), ((), ()))
            else:
                pairs = weights_ref[:, rows]
                contract = (((0,), (0,)), ((), ()))
            direction = score_sharpness_factor * lax.dot_general(
                pairs, short_ref[1 - tower], contract, preferred_element_type=jnp.float32
            )
            unit_rows = unit_ref[tower, rows, :]
            normed = normed_ref[tower, rows, :]
            tangent = (
                direction - unit_rows * jnp.sum(unit_rows * direction, axis=-1, keepdims=True)
            ) * length_ref[tower, rows, :]
            gain_sum = gain_sum + jnp.sum(tangent * normed, axis=0, keepdims=True)
            if first == 0:
                own = slice(0, block_rows)
                scaled_back = tangent[own] * gains[tower]
                gradient = (
                    scaled_back
                    - jnp.mean(scaled_back, axis=-1, keepdims=True)
                    - normed[own] * jnp.mean(scaled_back * normed[own], axis=-1, keepdims=True)
                ) * inverse_ref[tower, 0:block_rows, :]
                grad_ref[0] = gradient.astype(grad_ref.dtype)
        sums_ref[tower : tower + 1, :] = gain_sum
    first_lane = lax.broadcasted_iota(jnp.int32, (1, width), 1) == 0
    sums_ref[2:3, :] = jnp.where(first_lane, loss / real_count, 0.0)


def whole_group(
    picture_averaged_features,
    caption_averaged_features,
    picture_rescale_factor,
    caption_rescale_factor,
    exponent_of_sharpness,
    score_shift_term,
    objective_multiplier,
    matching_caption_index,
    genuine_entry_counts,
):
    count = lax.axis_size("blk")
    block_rows, width = picture_averaged_features.shape[1:]
    group_rows = count * block_rows
    pieces, masks, unused = gather_blocks(picture_averaged_features, caption_averaged_features, "blk")
    smem = pltpu.MemorySpace.SMEM
    vmem = pltpu.MemorySpace.VMEM
    grad_shape = jax.ShapeDtypeStruct(picture_averaged_features.shape, jnp.bfloat16)
    full = (2, group_rows, width)
    column = (2, group_rows, 1)
    image_grad, text_grad, sums = pl.pallas_call(
        functools.partial(group_kernel, tuple(masks[:count]), tuple(masks[count:])),
        out_shape=(grad_shape, grad_shape, jax.ShapeDtypeStruct((3, width), jnp.float32)),
        in_specs=[pl.BlockSpec(memory_space=smem)] * 4
        + [pl.BlockSpec(memory_space=vmem)] * 3
        + [pl.BlockSpec(memory_space=pl.ANY)] * len(pieces),
        out_specs=(pl.BlockSpec(memory_space=vmem),) * 3,
        scratch_shapes=[
            pltpu.VMEM(full, jnp.bfloat16),
            pltpu.VMEM(full, jnp.float32),
            pltpu.VMEM(full, jnp.bfloat16),
            pltpu.VMEM(full, jnp.float32),
            pltpu.VMEM(column, jnp.float32),
            pltpu.VMEM(column, jnp.float32),
            pltpu.VMEM((group_rows, group_rows), jnp.bfloat16),
            pltpu.SemaphoreType.DMA((len(pieces),)),
        ],
    )(
        exponent_of_sharpness,
        score_shift_term,
        objective_multiplier,
        genuine_entry_counts,
        picture_rescale_factor,
        caption_rescale_factor,
        matching_caption_index,
        *pieces,
    )
    group_loss = sums[2, 0:1]
    gain_grads = all_sum(sums, "rep", keep=2)
    return (image_grad, text_grad, gain_grads, group_loss)


def shards(
    picture_averaged_features,
    caption_averaged_features,
    picture_rescale_factor,
    caption_rescale_factor,
    exponent_of_sharpness,
    score_shift_term,
    objective_multiplier,
    matching_caption_index,
    genuine_entry_counts,
):
    width = picture_averaged_features.shape[2]
    first, second = embed_both(
        picture_averaged_features, caption_averaged_features, picture_rescale_factor, caption_rescale_factor
    )
    pieces, masks, offsets = gather_blocks(first, second, "blk")

    smem = pltpu.MemorySpace.SMEM
    vmem = pltpu.MemorySpace.VMEM
    grad_shape = jax.ShapeDtypeStruct(picture_averaged_features.shape, jnp.bfloat16)
    image_grad, text_grad, sums = pl.pallas_call(
        functools.partial(grad_kernel, tuple(masks), tuple(offsets)),
        out_shape=(grad_shape, grad_shape, jax.ShapeDtypeStruct((3, width), jnp.float32)),
        in_specs=[pl.BlockSpec(memory_space=smem)] * 4
        + [pl.BlockSpec(memory_space=vmem)] * 5
        + [pl.BlockSpec(memory_space=pl.ANY)] * len(pieces),
        out_specs=(pl.BlockSpec(memory_space=vmem),) * 3,
        scratch_shapes=[
            pltpu.VMEM((2, len(pieces) * pieces[0].shape[1], width), pieces[0].dtype),
            pltpu.SemaphoreType.DMA((len(pieces),)),
        ],
    )(
        exponent_of_sharpness,
        score_shift_term,
        objective_multiplier,
        genuine_entry_counts,
        picture_averaged_features,
        caption_averaged_features,
        picture_rescale_factor,
        caption_rescale_factor,
        matching_caption_index,
        *pieces,
    )

    group_sums = all_sum(sums, "blk")
    group_loss = group_sums[2, 0:1]
    gain_grads = all_sum(group_sums, "rep", keep=2)
    return (image_grad, text_grad, gain_grads, group_loss)


def body(*args):
    group_rows = args[0].shape[1] * lax.axis_size("blk")
    return (whole_group if group_rows <= 512 else shards)(*args)


def solution(mesh):
    placed = (
        P("rep", "blk", None),
        P("rep", "blk", None),
        P(),
        P(),
        P(),
        P(),
        P(),
        P("rep", None),
        P("rep", None),
    )
    return jax.shard_map(
        body,
        mesh=mesh,
        in_specs=placed,
        out_specs=(P("rep", "blk", None), P("rep", "blk", None), P(), P("rep")),
        check_vma=False,
    )
```

```python
import functools

import jax
import jax.numpy as jnp
from jax import lax
from jax.sharding import PartitionSpec as P
from jax.experimental import pallas as pl
from jax.experimental.pallas import tpu as pltpu

epsilon = 1e-06


def xor_swap(value, axis, bit):
    count = lax.axis_size(axis)
    return lax.ppermute(value, axis, [(source, source ^ bit) for source in range(count)])


def power_of_two(count):
    return count > 1 and count & (count - 1) == 0


def gather_blocks(first, second, axis):
    count = lax.axis_size(axis)
    half = first.shape[1]
    if not power_of_two(count) or count < 4:
        own = lax.axis_index(axis)
        pieces = [lax.all_gather(part, axis, axis=1, tiled=False) for part in (first, second)]
        pieces = [
            lax.dynamic_index_in_dim(part, own ^ mask, axis=1, keepdims=False)
            for part in pieces
            for mask in range(count)
        ]
        return pieces, list(range(count)) * 2, [0] * count + [half] * count
    chip_bits = [1 << b for b in range(1, count.bit_length() - 1)]
    orders = (chip_bits, chip_bits[::-1])
    routed = ([first], [second])
    routed_masks = ([0], [0])
    fresh = ([0], [0])
    shared = ([], [])
    shared_masks = ([], [])
    for step in range(len(chip_bits) + 1):
        last = step == len(chip_bits)
        sent = [None, None]
        if not last:
            sent = [xor_swap(tuple(routed[h]), axis, orders[h][step]) for h in range(2)]
        across = [xor_swap(tuple(routed[h][i] for i in fresh[h]), axis, 1) for h in range(2)]
        for h in range(2):
            shared[h].extend(across[h])
            shared_masks[h].extend([routed_masks[h][i] ^ 1 for i in fresh[h]])
            if not last:
                bit = orders[h][step]
                fresh[h][:] = list(range(len(routed[h]), 2 * len(routed[h])))
                routed[h].extend(sent[h])
                routed_masks[h].extend([mask ^ bit for mask in routed_masks[h]])
    gathered = routed[0] + shared[0] + routed[1] + shared[1]
    masks = routed_masks[0] + shared_masks[0] + routed_masks[1] + shared_masks[1]
    offsets = [0] * count + [half] * count
    return gathered, masks, offsets


def all_sum(value, axis, keep=None):
    keep = value.shape[0] if keep is None else keep
    count = lax.axis_size(axis)
    if not power_of_two(count):
        return lax.psum(value, axis)[:keep]
    bit = 1
    while bit < count:
        if bit * 2 < count:
            value = value + xor_swap(value, axis, bit)
        else:
            value = value[:keep] + xor_swap(value, axis, bit)[:keep]
        bit *= 2
    return value


def embed_kernel(picture_ref, caption_ref, picture_gain_ref, caption_gain_ref, first_ref, second_ref):
    half = first_ref.shape[1]
    towers = ((picture_ref, picture_gain_ref), (caption_ref, caption_gain_ref))
    for tower, (pooled_ref, gain_ref) in enumerate(towers):
        values = pooled_ref[0].astype(jnp.float32)
        centred = values - jnp.mean(values, axis=-1, keepdims=True)
        inverse = lax.rsqrt(jnp.mean(centred * centred, axis=-1, keepdims=True) + epsilon)
        scaled = centred * inverse * gain_ref[...][None, :]
        inv_length = lax.rsqrt(jnp.sum(scaled * scaled, axis=-1, keepdims=True) + epsilon)
        unit_rows = (scaled * inv_length).astype(first_ref.dtype)
        first_ref[tower] = unit_rows[:half]
        second_ref[tower] = unit_rows[half:]


def embed_both(picture, caption, picture_gain, caption_gain):
    rows, width = picture.shape[1:]
    vmem = pltpu.MemorySpace.VMEM
    half = jax.ShapeDtypeStruct((2, rows // 2, width), jnp.bfloat16)
    return pl.pallas_call(
        embed_kernel,
        out_shape=(half, half),
        in_specs=[pl.BlockSpec(memory_space=vmem)] * 4,
        out_specs=(pl.BlockSpec(memory_space=vmem), pl.BlockSpec(memory_space=vmem)),
    )(picture, caption, picture_gain, caption_gain)


def grad_kernel(masks, offsets, *refs):
    (sharpness_ref, shift_ref, multiplier_ref, counts_ref, picture_ref, caption_ref, picture_gain_ref,
     caption_gain_ref, partner_ref) = refs[:9]
    pieces = refs[9 : 9 + len(masks)]
    image_grad_ref, text_grad_ref, sums_ref, gathered_ref, copy_sems = refs[9 + len(masks) :]
    piece = pieces[0].shape[1]
    arrivals = [
        pltpu.make_async_copy(
            source, gathered_ref.at[:, position * piece : (position + 1) * piece, :], copy_sems.at[position]
        )
        for position, source in enumerate(pieces)
    ]
    for arrival in arrivals:
        arrival.start()
    blocks = counts_ref.shape[1]
    own_block = lax.axis_index("blk")
    block_rows = picture_ref.shape[1]
    width = picture_ref.shape[2]
    group_rows = gathered_ref.shape[1]
    own_start = own_block * block_rows
    total = counts_ref[0, 0]
    for block in range(1, blocks):
        total = total + counts_ref[0, block]
    real_count = jnp.full((1, 1), total, jnp.int32).astype(jnp.float32)
    score_sharpness_factor = jnp.exp(jnp.full((1, 1), sharpness_ref[0], jnp.float32))
    score_shift_amount = jnp.full((1, 1), shift_ref[0], jnp.float32)
    grad_factor = jnp.full((1, 1), multiplier_ref[0], jnp.float32) / real_count

    lane = lax.broadcasted_iota(jnp.int32, (1, group_rows), 1)
    held_row = jnp.zeros((1, group_rows), jnp.int32)
    limit = jnp.zeros((1, group_rows), jnp.int32)
    for position, (mask, offset) in enumerate(zip(masks, offsets)):
        block = own_block ^ mask
        here = lane // piece == position
        held_row = jnp.where(here, block * block_rows + offset + lane % piece, held_row)
        limit = jnp.where(here, counts_ref[0, block], limit)
    real_group = (held_row % block_rows) < limit
    sub = lax.broadcasted_iota(jnp.int32, (block_rows, 1), 0)
    real_own = sub < counts_ref[0, own_block]
    kept = real_own & real_group

    natural = lax.broadcasted_iota(jnp.int32, (block_rows, group_rows), 1)
    own_index = own_start + lax.broadcasted_iota(jnp.int32, (block_rows, group_rows), 0)
    partner_row = partner_ref[...]
    own_partner = jnp.sum(
        jnp.where(natural == own_index, partner_row.astype(jnp.float32), 0.0), axis=1, keepdims=True
    ).astype(jnp.int32)
    matched_image = jnp.sum(
        jnp.where(partner_row == own_index, natural.astype(jnp.float32), 0.0), axis=1, keepdims=True
    ).astype(jnp.int32)
    positives = (own_partner == held_row, matched_image == held_row)

    start_b = len(masks) // 2 * piece
    for arrival in arrivals:
        arrival.wait()
    loss_rows = []
    towers = ((picture_ref, picture_gain_ref, image_grad_ref), (caption_ref, caption_gain_ref, text_grad_ref))
    for tower, (pooled_ref, gain_ref, grad_ref) in enumerate(towers):
        values = pooled_ref[0].astype(jnp.float32)
        gain = gain_ref[...][None, :]
        centred = values - jnp.mean(values, axis=-1, keepdims=True)
        inverse = lax.rsqrt(jnp.mean(centred * centred, axis=-1, keepdims=True) + epsilon)
        normed = centred * inverse
        scaled = normed * gain
        inv_length = lax.rsqrt(jnp.sum(scaled * scaled, axis=-1, keepdims=True) + epsilon)
        unit_rows = scaled * inv_length

        own = jnp.concatenate(
            [gathered_ref[tower, 0:piece, :], gathered_ref[tower, start_b : start_b + piece, :]], axis=0
        )
        other = gathered_ref[1 - tower]
        scores = lax.dot_general(own, other, (((1,), (1,)), ((), ())), preferred_element_type=jnp.float32)
        score_similarity_table = score_sharpness_factor * scores + score_shift_amount
        labels = jnp.where(positives[tower], 1.0, -1.0)
        margin = -labels * score_similarity_table
        if tower == 0:
            softplus = jnp.maximum(margin, 0.0) + jnp.log1p(jnp.exp(-jnp.abs(margin)))
            loss_rows.append(jnp.sum(jnp.where(kept, softplus, 0.0), axis=(0, 1), keepdims=True))
        weights = jnp.where(kept, -labels * jax.nn.sigmoid(margin), 0.0) * grad_factor
        direction = score_sharpness_factor * jnp.dot(
            weights.astype(jnp.bfloat16), other, preferred_element_type=jnp.float32
        )
        tangent = (
            direction - unit_rows * jnp.sum(unit_rows * direction, axis=-1, keepdims=True)
        ) * inv_length
        sums_ref[tower : tower + 1, :] = jnp.sum(tangent * normed, axis=0, keepdims=True)
        scaled_back = tangent * gain
        gradient = (
            scaled_back
            - jnp.mean(scaled_back, axis=-1, keepdims=True)
            - normed * jnp.mean(scaled_back * normed, axis=-1, keepdims=True)
        ) * inverse
        grad_ref[0] = gradient.astype(grad_ref.dtype)
    first_lane = lax.broadcasted_iota(jnp.int32, (1, width), 1) == 0
    sums_ref[2:3, :] = jnp.where(first_lane, loss_rows[0] / real_count, 0.0)


def group_kernel(image_masks, text_masks, *refs):
    (sharpness_ref, shift_ref, multiplier_ref, counts_ref, picture_gain_ref, caption_gain_ref,
     partner_ref) = refs[:7]
    count = len(image_masks)
    pieces = refs[7 : 7 + 2 * count]
    (image_grad_ref, text_grad_ref, sums_ref, raw_ref, unit_ref, short_ref, normed_ref, inverse_ref,
     length_ref, weights_ref, tangent_ref, copy_sems) = refs[7 + 2 * count :]
    block_rows = pieces[0].shape[1]
    group_rows = raw_ref.shape[1]
    width = raw_ref.shape[2]
    own_block = lax.axis_index("blk")

    def block_of(mask):
        block = own_block
        for bit in range(mask.bit_length()):
            if mask >> bit & 1:
                block = block + (1 - 2 * (own_block // (1 << bit) % 2)) * (1 << bit)
        return block

    arrivals = []
    for position, source in enumerate(pieces):
        tower, slot = divmod(position, count)
        masks = image_masks if tower == 0 else text_masks
        rows = pl.ds(pl.multiple_of(block_of(masks[slot]) * block_rows, block_rows), block_rows)
        arrival = pltpu.make_async_copy(source.at[0], raw_ref.at[tower, rows, :], copy_sems.at[position])
        arrival.start()
        arrivals.append(arrival)

    blocks = counts_ref.shape[1]
    total = counts_ref[0, 0]
    for block in range(1, blocks):
        total = total + counts_ref[0, block]
    real_count = jnp.full((1, 1), total, jnp.int32).astype(jnp.float32)
    score_sharpness_factor = jnp.exp(jnp.full((1, 1), sharpness_ref[0], jnp.float32))
    score_shift_amount = jnp.full((1, 1), shift_ref[0], jnp.float32)
    grad_factor = jnp.full((1, 1), multiplier_ref[0], jnp.float32) / real_count

    def held(shape, dim):
        row = lax.broadcasted_iota(jnp.int32, shape, dim)
        limit = jnp.zeros(shape, jnp.int32)
        for block in range(blocks):
            limit = jnp.where(row // block_rows == block, counts_ref[0, block], limit)
        return row, (row % block_rows) < limit

    image_row, image_real = held((group_rows, 1), 0)
    text_row, text_real = held((1, group_rows), 1)
    natural = lax.broadcasted_iota(jnp.int32, (group_rows, group_rows), 1)
    partner_of_image = jnp.sum(
        jnp.where(natural == image_row, partner_ref[...].astype(jnp.float32), 0.0), axis=1, keepdims=True
    ).astype(jnp.int32)

    for arrival in arrivals:
        arrival.wait()
    gains = (picture_gain_ref[...][None, :], caption_gain_ref[...][None, :])
    chunk = min(128, group_rows)
    for tower in range(2):
        for first in range(0, group_rows, chunk):
            rows = pl.ds(first, chunk)
            values = raw_ref[tower, rows, :].astype(jnp.float32)
            centred = values - jnp.mean(values, axis=-1, keepdims=True)
            inverse = lax.rsqrt(jnp.mean(centred * centred, axis=-1, keepdims=True) + epsilon)
            normed = centred * inverse
            scaled = normed * gains[tower]
            inv_length = lax.rsqrt(jnp.sum(scaled * scaled, axis=-1, keepdims=True) + epsilon)
            unit_rows = scaled * inv_length
            unit_ref[tower, rows, :] = unit_rows
            short_ref[tower, rows, :] = unit_rows.astype(short_ref.dtype)
            normed_ref[tower, rows, :] = normed
            inverse_ref[tower, rows, :] = inverse
            length_ref[tower, rows, :] = inv_length

    loss = jnp.zeros((1, 1), jnp.float32)
    for first in range(0, group_rows, chunk):
        rows = pl.ds(first, chunk)
        scores = lax.dot_general(
            short_ref[0, rows, :], short_ref[1], (((1,), (1,)), ((), ())), preferred_element_type=jnp.float32
        )
        score_similarity_table = score_sharpness_factor * scores + score_shift_amount
        labels = jnp.where(partner_of_image[first : first + chunk] == text_row, 1.0, -1.0)
        kept = image_real[first : first + chunk] & text_real
        margin = -labels * score_similarity_table
        decay = jnp.exp(-jnp.abs(margin))
        softplus = jnp.maximum(margin, 0.0) + jnp.log1p(decay)
        loss = loss + jnp.sum(jnp.where(kept, softplus, 0.0), axis=(0, 1), keepdims=True)
        sigmoid = jnp.where(margin >= 0.0, 1.0, decay) / (1.0 + decay)
        weights = jnp.where(kept, -labels * sigmoid, 0.0) * grad_factor
        weights_ref[rows, :] = weights.astype(weights_ref.dtype)

    for tower, grad_ref in enumerate((image_grad_ref, text_grad_ref)):
        gain_sum = jnp.zeros((1, width), jnp.float32)
        for first in range(0, group_rows, chunk):
            rows = pl.ds(first, chunk)
            if tower == 0:
                pairs = weights_ref[rows, :]
                contract = (((1,), (0,)), ((), ()))
            else:
                pairs = weights_ref[:, rows]
                contract = (((0,), (0,)), ((), ()))
            direction = score_sharpness_factor * lax.dot_general(
                pairs, short_ref[1 - tower], contract, preferred_element_type=jnp.float32
            )
            unit_rows = unit_ref[tower, rows, :]
            normed = normed_ref[tower, rows, :]
            tangent = (
                direction - unit_rows * jnp.sum(unit_rows * direction, axis=-1, keepdims=True)
            ) * length_ref[tower, rows, :]
            gain_sum = gain_sum + jnp.sum(tangent * normed, axis=0, keepdims=True)
            tangent_ref[rows, :] = tangent
        sums_ref[tower : tower + 1, :] = gain_sum
        own = pl.ds(pl.multiple_of(own_block * block_rows, block_rows), block_rows)
        normed = normed_ref[tower, own, :]
        scaled_back = tangent_ref[own, :] * gains[tower]
        gradient = (
            scaled_back
            - jnp.mean(scaled_back, axis=-1, keepdims=True)
            - normed * jnp.mean(scaled_back * normed, axis=-1, keepdims=True)
        ) * inverse_ref[tower, own, :]
        grad_ref[0] = gradient.astype(grad_ref.dtype)
    first_lane = lax.broadcasted_iota(jnp.int32, (1, width), 1) == 0
    sums_ref[2:3, :] = jnp.where(first_lane, loss / real_count, 0.0)


def whole_group(
    picture_averaged_features,
    caption_averaged_features,
    picture_rescale_factor,
    caption_rescale_factor,
    exponent_of_sharpness,
    score_shift_term,
    objective_multiplier,
    matching_caption_index,
    genuine_entry_counts,
):
    count = lax.axis_size("blk")
    block_rows, width = picture_averaged_features.shape[1:]
    group_rows = count * block_rows
    pieces, masks, unused = gather_blocks(picture_averaged_features, caption_averaged_features, "blk")
    smem = pltpu.MemorySpace.SMEM
    vmem = pltpu.MemorySpace.VMEM
    grad_shape = jax.ShapeDtypeStruct(picture_averaged_features.shape, jnp.bfloat16)
    full = (2, group_rows, width)
    column = (2, group_rows, 1)
    image_grad, text_grad, sums = pl.pallas_call(
        functools.partial(group_kernel, tuple(masks[:count]), tuple(masks[count:])),
        out_shape=(grad_shape, grad_shape, jax.ShapeDtypeStruct((3, width), jnp.float32)),
        in_specs=[pl.BlockSpec(memory_space=smem)] * 4
        + [pl.BlockSpec(memory_space=vmem)] * 3
        + [pl.BlockSpec(memory_space=pl.ANY)] * len(pieces),
        out_specs=(pl.BlockSpec(memory_space=vmem),) * 3,
        scratch_shapes=[
            pltpu.VMEM(full, jnp.bfloat16),
            pltpu.VMEM(full, jnp.float32),
            pltpu.VMEM(full, jnp.bfloat16),
            pltpu.VMEM(full, jnp.float32),
            pltpu.VMEM(column, jnp.float32),
            pltpu.VMEM(column, jnp.float32),
            pltpu.VMEM((group_rows, group_rows), jnp.bfloat16),
            pltpu.VMEM((group_rows, width), jnp.float32),
            pltpu.SemaphoreType.DMA((len(pieces),)),
        ],
    )(
        exponent_of_sharpness,
        score_shift_term,
        objective_multiplier,
        genuine_entry_counts,
        picture_rescale_factor,
        caption_rescale_factor,
        matching_caption_index,
        *pieces,
    )
    group_loss = sums[2, 0:1]
    gain_grads = all_sum(sums, "rep", keep=2)
    return (image_grad, text_grad, gain_grads, group_loss)


def shards(
    picture_averaged_features,
    caption_averaged_features,
    picture_rescale_factor,
    caption_rescale_factor,
    exponent_of_sharpness,
    score_shift_term,
    objective_multiplier,
    matching_caption_index,
    genuine_entry_counts,
):
    width = picture_averaged_features.shape[2]
    first, second = embed_both(
        picture_averaged_features, caption_averaged_features, picture_rescale_factor, caption_rescale_factor
    )
    pieces, masks, offsets = gather_blocks(first, second, "blk")

    smem = pltpu.MemorySpace.SMEM
    vmem = pltpu.MemorySpace.VMEM
    grad_shape = jax.ShapeDtypeStruct(picture_averaged_features.shape, jnp.bfloat16)
    image_grad, text_grad, sums = pl.pallas_call(
        functools.partial(grad_kernel, tuple(masks), tuple(offsets)),
        out_shape=(grad_shape, grad_shape, jax.ShapeDtypeStruct((3, width), jnp.float32)),
        in_specs=[pl.BlockSpec(memory_space=smem)] * 4
        + [pl.BlockSpec(memory_space=vmem)] * 5
        + [pl.BlockSpec(memory_space=pl.ANY)] * len(pieces),
        out_specs=(pl.BlockSpec(memory_space=vmem),) * 3,
        scratch_shapes=[
            pltpu.VMEM((2, len(pieces) * pieces[0].shape[1], width), pieces[0].dtype),
            pltpu.SemaphoreType.DMA((len(pieces),)),
        ],
    )(
        exponent_of_sharpness,
        score_shift_term,
        objective_multiplier,
        genuine_entry_counts,
        picture_averaged_features,
        caption_averaged_features,
        picture_rescale_factor,
        caption_rescale_factor,
        matching_caption_index,
        *pieces,
    )

    group_sums = all_sum(sums, "blk")
    group_loss = group_sums[2, 0:1]
    gain_grads = all_sum(group_sums, "rep", keep=2)
    return (image_grad, text_grad, gain_grads, group_loss)


def body(*args):
    group_rows = args[0].shape[1] * lax.axis_size("blk")
    return (whole_group if group_rows <= 512 else shards)(*args)


def solution(mesh):
    placed = (
        P("rep", "blk", None),
        P("rep", "blk", None),
        P(),
        P(),
        P(),
        P(),
        P(),
        P("rep", None),
        P("rep", None),
    )
    return jax.shard_map(
        body,
        mesh=mesh,
        in_specs=placed,
        out_specs=(P("rep", "blk", None), P("rep", "blk", None), P(), P("rep")),
        check_vma=False,
    )
```

```python
import functools

import jax
import jax.numpy as jnp
from jax import lax
from jax.sharding import PartitionSpec as P
from jax.experimental import pallas as pl
from jax.experimental.pallas import tpu as pltpu

epsilon = 1e-06


def xor_swap(value, axis, bit):
    count = lax.axis_size(axis)
    return lax.ppermute(value, axis, [(source, source ^ bit) for source in range(count)])


def power_of_two(count):
    return count > 1 and count & (count - 1) == 0


def gather_blocks(first, second, axis):
    count = lax.axis_size(axis)
    half = first.shape[1]
    if not power_of_two(count) or count < 4:
        own = lax.axis_index(axis)
        pieces = [lax.all_gather(part, axis, axis=1, tiled=False) for part in (first, second)]
        pieces = [
            lax.dynamic_index_in_dim(part, own ^ mask, axis=1, keepdims=False)
            for part in pieces
            for mask in range(count)
        ]
        return pieces, list(range(count)) * 2, [0] * count + [half] * count
    chip_bits = [1 << b for b in range(1, count.bit_length() - 1)]
    orders = (chip_bits, chip_bits[::-1])
    routed = ([first], [second])
    routed_masks = ([0], [0])
    fresh = ([0], [0])
    shared = ([], [])
    shared_masks = ([], [])
    for step in range(len(chip_bits) + 1):
        last = step == len(chip_bits)
        sent = [None, None]
        if not last:
            sent = [xor_swap(tuple(routed[h]), axis, orders[h][step]) for h in range(2)]
        across = [xor_swap(tuple(routed[h][i] for i in fresh[h]), axis, 1) for h in range(2)]
        for h in range(2):
            shared[h].extend(across[h])
            shared_masks[h].extend([routed_masks[h][i] ^ 1 for i in fresh[h]])
            if not last:
                bit = orders[h][step]
                fresh[h][:] = list(range(len(routed[h]), 2 * len(routed[h])))
                routed[h].extend(sent[h])
                routed_masks[h].extend([mask ^ bit for mask in routed_masks[h]])
    gathered = routed[0] + shared[0] + routed[1] + shared[1]
    masks = routed_masks[0] + shared_masks[0] + routed_masks[1] + shared_masks[1]
    offsets = [0] * count + [half] * count
    return gathered, masks, offsets


def all_sum(value, axis, keep=None):
    keep = value.shape[0] if keep is None else keep
    count = lax.axis_size(axis)
    if 1 < count <= 4:
        held = [value[:keep]] + [
            lax.ppermute(value, axis, [(source, (source + shift) % count) for source in range(count)])[:keep]
            for shift in range(1, count)
        ]
        own = lax.axis_index(axis)
        total = None
        for member in range(count):
            shift = (own - member) % count
            part = held[0]
            for other in range(1, count):
                part = jnp.where(shift == other, held[other], part)
            total = part if total is None else total + part
        return total
    if not power_of_two(count):
        return lax.psum(value, axis)[:keep]
    bit = 1
    while bit < count:
        if bit * 2 < count:
            value = value + xor_swap(value, axis, bit)
        else:
            value = value[:keep] + xor_swap(value, axis, bit)[:keep]
        bit *= 2
    return value


def embed_kernel(picture_ref, caption_ref, picture_gain_ref, caption_gain_ref, first_ref, second_ref):
    half = first_ref.shape[1]
    towers = ((picture_ref, picture_gain_ref), (caption_ref, caption_gain_ref))
    for tower, (pooled_ref, gain_ref) in enumerate(towers):
        values = pooled_ref[0].astype(jnp.float32)
        centred = values - jnp.mean(values, axis=-1, keepdims=True)
        inverse = lax.rsqrt(jnp.mean(centred * centred, axis=-1, keepdims=True) + epsilon)
        scaled = centred * inverse * gain_ref[...][None, :]
        inv_length = lax.rsqrt(jnp.sum(scaled * scaled, axis=-1, keepdims=True) + epsilon)
        unit_rows = (scaled * inv_length).astype(first_ref.dtype)
        first_ref[tower] = unit_rows[:half]
        second_ref[tower] = unit_rows[half:]


def embed_both(picture, caption, picture_gain, caption_gain):
    rows, width = picture.shape[1:]
    vmem = pltpu.MemorySpace.VMEM
    half = jax.ShapeDtypeStruct((2, rows // 2, width), jnp.bfloat16)
    return pl.pallas_call(
        embed_kernel,
        out_shape=(half, half),
        in_specs=[pl.BlockSpec(memory_space=vmem)] * 4,
        out_specs=(pl.BlockSpec(memory_space=vmem), pl.BlockSpec(memory_space=vmem)),
    )(picture, caption, picture_gain, caption_gain)


def grad_kernel(masks, offsets, *refs):
    (sharpness_ref, shift_ref, multiplier_ref, counts_ref, picture_ref, caption_ref, picture_gain_ref,
     caption_gain_ref, partner_ref) = refs[:9]
    pieces = refs[9 : 9 + len(masks)]
    image_grad_ref, text_grad_ref, sums_ref, gathered_ref, copy_sems = refs[9 + len(masks) :]
    piece = pieces[0].shape[1]
    arrivals = [
        pltpu.make_async_copy(
            source, gathered_ref.at[:, position * piece : (position + 1) * piece, :], copy_sems.at[position]
        )
        for position, source in enumerate(pieces)
    ]
    for arrival in arrivals:
        arrival.start()
    blocks = counts_ref.shape[1]
    own_block = lax.axis_index("blk")
    block_rows = picture_ref.shape[1]
    width = picture_ref.shape[2]
    group_rows = gathered_ref.shape[1]
    own_start = own_block * block_rows
    total = counts_ref[0, 0]
    for block in range(1, blocks):
        total = total + counts_ref[0, block]
    real_count = jnp.full((1, 1), total, jnp.int32).astype(jnp.float32)
    score_sharpness_factor = jnp.exp(jnp.full((1, 1), sharpness_ref[0], jnp.float32))
    score_shift_amount = jnp.full((1, 1), shift_ref[0], jnp.float32)
    grad_factor = jnp.full((1, 1), multiplier_ref[0], jnp.float32) / real_count

    lane = lax.broadcasted_iota(jnp.int32, (1, group_rows), 1)
    held_row = jnp.zeros((1, group_rows), jnp.int32)
    limit = jnp.zeros((1, group_rows), jnp.int32)
    for position, (mask, offset) in enumerate(zip(masks, offsets)):
        block = own_block ^ mask
        here = lane // piece == position
        held_row = jnp.where(here, block * block_rows + offset + lane % piece, held_row)
        limit = jnp.where(here, counts_ref[0, block], limit)
    real_group = (held_row % block_rows) < limit
    sub = lax.broadcasted_iota(jnp.int32, (block_rows, 1), 0)
    real_own = sub < counts_ref[0, own_block]
    kept = real_own & real_group

    natural = lax.broadcasted_iota(jnp.int32, (block_rows, group_rows), 1)
    own_index = own_start + lax.broadcasted_iota(jnp.int32, (block_rows, group_rows), 0)
    partner_row = partner_ref[...]
    own_partner = jnp.sum(
        jnp.where(natural == own_index, partner_row.astype(jnp.float32), 0.0), axis=1, keepdims=True
    ).astype(jnp.int32)
    matched_image = jnp.sum(
        jnp.where(partner_row == own_index, natural.astype(jnp.float32), 0.0), axis=1, keepdims=True
    ).astype(jnp.int32)
    positives = (own_partner == held_row, matched_image == held_row)

    start_b = len(masks) // 2 * piece
    for arrival in arrivals:
        arrival.wait()
    loss_rows = []
    towers = ((picture_ref, picture_gain_ref, image_grad_ref), (caption_ref, caption_gain_ref, text_grad_ref))
    for tower, (pooled_ref, gain_ref, grad_ref) in enumerate(towers):
        values = pooled_ref[0].astype(jnp.float32)
        gain = gain_ref[...][None, :]
        centred = values - jnp.mean(values, axis=-1, keepdims=True)
        inverse = lax.rsqrt(jnp.mean(centred * centred, axis=-1, keepdims=True) + epsilon)
        normed = centred * inverse
        scaled = normed * gain
        inv_length = lax.rsqrt(jnp.sum(scaled * scaled, axis=-1, keepdims=True) + epsilon)
        unit_rows = scaled * inv_length

        own = jnp.concatenate(
            [gathered_ref[tower, 0:piece, :], gathered_ref[tower, start_b : start_b + piece, :]], axis=0
        )
        other = gathered_ref[1 - tower]
        scores = lax.dot_general(own, other, (((1,), (1,)), ((), ())), preferred_element_type=jnp.float32)
        score_similarity_table = score_sharpness_factor * scores + score_shift_amount
        labels = jnp.where(positives[tower], 1.0, -1.0)
        margin = -labels * score_similarity_table
        if tower == 0:
            softplus = jnp.maximum(margin, 0.0) + jnp.log1p(jnp.exp(-jnp.abs(margin)))
            loss_rows.append(jnp.sum(jnp.where(kept, softplus, 0.0), axis=(0, 1), keepdims=True))
        weights = jnp.where(kept, -labels * jax.nn.sigmoid(margin), 0.0) * grad_factor
        direction = score_sharpness_factor * jnp.dot(
            weights.astype(jnp.bfloat16), other, preferred_element_type=jnp.float32
        )
        tangent = (
            direction - unit_rows * jnp.sum(unit_rows * direction, axis=-1, keepdims=True)
        ) * inv_length
        sums_ref[tower : tower + 1, :] = jnp.sum(tangent * normed, axis=0, keepdims=True)
        scaled_back = tangent * gain
        gradient = (
            scaled_back
            - jnp.mean(scaled_back, axis=-1, keepdims=True)
            - normed * jnp.mean(scaled_back * normed, axis=-1, keepdims=True)
        ) * inverse
        grad_ref[0] = gradient.astype(grad_ref.dtype)
    first_lane = lax.broadcasted_iota(jnp.int32, (1, width), 1) == 0
    sums_ref[2:3, :] = jnp.where(first_lane, loss_rows[0] / real_count, 0.0)


def group_kernel(image_masks, text_masks, *refs):
    (sharpness_ref, shift_ref, multiplier_ref, counts_ref, picture_gain_ref, caption_gain_ref,
     partner_ref) = refs[:7]
    count = len(image_masks)
    pieces = refs[7 : 7 + 2 * count]
    (image_grad_ref, text_grad_ref, sums_ref, raw_ref, unit_ref, short_ref, normed_ref, inverse_ref,
     length_ref, weights_ref, tangent_ref, copy_sems) = refs[7 + 2 * count :]
    block_rows = pieces[0].shape[1]
    group_rows = raw_ref.shape[1]
    width = raw_ref.shape[2]
    own_block = lax.axis_index("blk")

    def block_of(mask):
        block = own_block
        for bit in range(mask.bit_length()):
            if mask >> bit & 1:
                block = block + (1 - 2 * (own_block // (1 << bit) % 2)) * (1 << bit)
        return block

    arrivals = []
    for position, source in enumerate(pieces):
        tower, slot = divmod(position, count)
        masks = image_masks if tower == 0 else text_masks
        rows = pl.ds(pl.multiple_of(block_of(masks[slot]) * block_rows, block_rows), block_rows)
        arrival = pltpu.make_async_copy(source.at[0], raw_ref.at[tower, rows, :], copy_sems.at[position])
        arrival.start()
        arrivals.append(arrival)

    blocks = counts_ref.shape[1]
    total = counts_ref[0, 0]
    for block in range(1, blocks):
        total = total + counts_ref[0, block]
    real_count = jnp.full((1, 1), total, jnp.int32).astype(jnp.float32)
    score_sharpness_factor = jnp.exp(jnp.full((1, 1), sharpness_ref[0], jnp.float32))
    score_shift_amount = jnp.full((1, 1), shift_ref[0], jnp.float32)
    grad_factor = jnp.full((1, 1), multiplier_ref[0], jnp.float32) / real_count

    def held(shape, dim):
        row = lax.broadcasted_iota(jnp.int32, shape, dim)
        limit = jnp.zeros(shape, jnp.int32)
        for block in range(blocks):
            limit = jnp.where(row // block_rows == block, counts_ref[0, block], limit)
        return row, (row % block_rows) < limit

    image_row, image_real = held((group_rows, 1), 0)
    text_row, text_real = held((1, group_rows), 1)
    natural = lax.broadcasted_iota(jnp.int32, (group_rows, group_rows), 1)
    partner_of_image = jnp.sum(
        jnp.where(natural == image_row, partner_ref[...].astype(jnp.float32), 0.0), axis=1, keepdims=True
    ).astype(jnp.int32)

    for arrival in arrivals:
        arrival.wait()
    gains = (picture_gain_ref[...][None, :], caption_gain_ref[...][None, :])
    chunk = min(128, group_rows)
    for tower in range(2):
        for first in range(0, group_rows, chunk):
            rows = pl.ds(first, chunk)
            values = raw_ref[tower, rows, :].astype(jnp.float32)
            centred = values - jnp.mean(values, axis=-1, keepdims=True)
            inverse = lax.rsqrt(jnp.mean(centred * centred, axis=-1, keepdims=True) + epsilon)
            normed = centred * inverse
            scaled = normed * gains[tower]
            inv_length = lax.rsqrt(jnp.sum(scaled * scaled, axis=-1, keepdims=True) + epsilon)
            unit_rows = scaled * inv_length
            unit_ref[tower, rows, :] = unit_rows
            short_ref[tower, rows, :] = unit_rows.astype(short_ref.dtype)
            normed_ref[tower, rows, :] = normed
            inverse_ref[tower, rows, :] = inverse
            length_ref[tower, rows, :] = inv_length

    loss = jnp.zeros((1, 1), jnp.float32)
    for first in range(0, group_rows, chunk):
        rows = pl.ds(first, chunk)
        scores = lax.dot_general(
            short_ref[0, rows, :], short_ref[1], (((1,), (1,)), ((), ())), preferred_element_type=jnp.float32
        )
        score_similarity_table = score_sharpness_factor * scores + score_shift_amount
        labels = jnp.where(partner_of_image[first : first + chunk] == text_row, 1.0, -1.0)
        kept = image_real[first : first + chunk] & text_real
        margin = -labels * score_similarity_table
        decay = jnp.exp(-jnp.abs(margin))
        softplus = jnp.maximum(margin, 0.0) + jnp.log1p(decay)
        loss = loss + jnp.sum(jnp.where(kept, softplus, 0.0), axis=(0, 1), keepdims=True)
        sigmoid = jnp.where(margin >= 0.0, 1.0, decay) / (1.0 + decay)
        weights = jnp.where(kept, -labels * sigmoid, 0.0) * grad_factor
        weights_ref[rows, :] = weights.astype(weights_ref.dtype)

    for tower, grad_ref in enumerate((image_grad_ref, text_grad_ref)):
        gain_sum = jnp.zeros((1, width), jnp.float32)
        for first in range(0, group_rows, chunk):
            rows = pl.ds(first, chunk)
            if tower == 0:
                pairs = weights_ref[rows, :]
                contract = (((1,), (0,)), ((), ()))
            else:
                pairs = weights_ref[:, rows]
                contract = (((0,), (0,)), ((), ()))
            direction = score_sharpness_factor * lax.dot_general(
                pairs, short_ref[1 - tower], contract, preferred_element_type=jnp.float32
            )
            unit_rows = unit_ref[tower, rows, :]
            normed = normed_ref[tower, rows, :]
            tangent = (
                direction - unit_rows * jnp.sum(unit_rows * direction, axis=-1, keepdims=True)
            ) * length_ref[tower, rows, :]
            gain_sum = gain_sum + jnp.sum(tangent * normed, axis=0, keepdims=True)

            @pl.when((own_block * block_rows >= first) & (own_block * block_rows < first + chunk))
            def _():
                tangent_ref[rows, :] = tangent
        sums_ref[tower : tower + 1, :] = gain_sum
        own = pl.ds(pl.multiple_of(own_block * block_rows, block_rows), block_rows)
        normed = normed_ref[tower, own, :]
        scaled_back = tangent_ref[own, :] * gains[tower]
        gradient = (
            scaled_back
            - jnp.mean(scaled_back, axis=-1, keepdims=True)
            - normed * jnp.mean(scaled_back * normed, axis=-1, keepdims=True)
        ) * inverse_ref[tower, own, :]
        grad_ref[0] = gradient.astype(grad_ref.dtype)
    first_lane = lax.broadcasted_iota(jnp.int32, (1, width), 1) == 0
    sums_ref[2:3, :] = jnp.where(first_lane, loss / real_count, 0.0)


def whole_group(
    picture_averaged_features,
    caption_averaged_features,
    picture_rescale_factor,
    caption_rescale_factor,
    exponent_of_sharpness,
    score_shift_term,
    objective_multiplier,
    matching_caption_index,
    genuine_entry_counts,
):
    count = lax.axis_size("blk")
    block_rows, width = picture_averaged_features.shape[1:]
    group_rows = count * block_rows
    pieces, masks, unused = gather_blocks(picture_averaged_features, caption_averaged_features, "blk")
    smem = pltpu.MemorySpace.SMEM
    vmem = pltpu.MemorySpace.VMEM
    grad_shape = jax.ShapeDtypeStruct(picture_averaged_features.shape, jnp.bfloat16)
    full = (2, group_rows, width)
    column = (2, group_rows, 1)
    image_grad, text_grad, sums = pl.pallas_call(
        functools.partial(group_kernel, tuple(masks[:count]), tuple(masks[count:])),
        out_shape=(grad_shape, grad_shape, jax.ShapeDtypeStruct((3, width), jnp.float32)),
        in_specs=[pl.BlockSpec(memory_space=smem)] * 4
        + [pl.BlockSpec(memory_space=vmem)] * 3
        + [pl.BlockSpec(memory_space=pl.ANY)] * len(pieces),
        out_specs=(pl.BlockSpec(memory_space=vmem),) * 3,
        scratch_shapes=[
            pltpu.VMEM(full, jnp.bfloat16),
            pltpu.VMEM(full, jnp.float32),
            pltpu.VMEM(full, jnp.bfloat16),
            pltpu.VMEM(full, jnp.float32),
            pltpu.VMEM(column, jnp.float32),
            pltpu.VMEM(column, jnp.float32),
            pltpu.VMEM((group_rows, group_rows), jnp.bfloat16),
            pltpu.VMEM((group_rows, width), jnp.float32),
            pltpu.SemaphoreType.DMA((len(pieces),)),
        ],
    )(
        exponent_of_sharpness,
        score_shift_term,
        objective_multiplier,
        genuine_entry_counts,
        picture_rescale_factor,
        caption_rescale_factor,
        matching_caption_index,
        *pieces,
    )
    group_loss = sums[2, 0:1]
    gain_grads = all_sum(sums, "rep", keep=2)
    return (image_grad, text_grad, gain_grads, group_loss)


def shards(
    picture_averaged_features,
    caption_averaged_features,
    picture_rescale_factor,
    caption_rescale_factor,
    exponent_of_sharpness,
    score_shift_term,
    objective_multiplier,
    matching_caption_index,
    genuine_entry_counts,
):
    width = picture_averaged_features.shape[2]
    first, second = embed_both(
        picture_averaged_features, caption_averaged_features, picture_rescale_factor, caption_rescale_factor
    )
    pieces, masks, offsets = gather_blocks(first, second, "blk")

    smem = pltpu.MemorySpace.SMEM
    vmem = pltpu.MemorySpace.VMEM
    grad_shape = jax.ShapeDtypeStruct(picture_averaged_features.shape, jnp.bfloat16)
    image_grad, text_grad, sums = pl.pallas_call(
        functools.partial(grad_kernel, tuple(masks), tuple(offsets)),
        out_shape=(grad_shape, grad_shape, jax.ShapeDtypeStruct((3, width), jnp.float32)),
        in_specs=[pl.BlockSpec(memory_space=smem)] * 4
        + [pl.BlockSpec(memory_space=vmem)] * 5
        + [pl.BlockSpec(memory_space=pl.ANY)] * len(pieces),
        out_specs=(pl.BlockSpec(memory_space=vmem),) * 3,
        scratch_shapes=[
            pltpu.VMEM((2, len(pieces) * pieces[0].shape[1], width), pieces[0].dtype),
            pltpu.SemaphoreType.DMA((len(pieces),)),
        ],
    )(
        exponent_of_sharpness,
        score_shift_term,
        objective_multiplier,
        genuine_entry_counts,
        picture_averaged_features,
        caption_averaged_features,
        picture_rescale_factor,
        caption_rescale_factor,
        matching_caption_index,
        *pieces,
    )

    group_sums = all_sum(sums, "blk")
    group_loss = group_sums[2, 0:1]
    gain_grads = all_sum(group_sums, "rep", keep=2)
    return (image_grad, text_grad, gain_grads, group_loss)


def body(*args):
    group_rows = args[0].shape[1] * lax.axis_size("blk")
    return (whole_group if group_rows <= 512 else shards)(*args)


def solution(mesh):
    placed = (
        P("rep", "blk", None),
        P("rep", "blk", None),
        P(),
        P(),
        P(),
        P(),
        P(),
        P("rep", None),
        P("rep", None),
    )
    return jax.shard_map(
        body,
        mesh=mesh,
        in_specs=placed,
        out_specs=(P("rep", "blk", None), P("rep", "blk", None), P(), P("rep")),
        check_vma=False,
    )
```

```python
import functools

import jax
import jax.numpy as jnp
from jax import lax
from jax.sharding import PartitionSpec as P
from jax.experimental import pallas as pl
from jax.experimental.pallas import tpu as pltpu

epsilon = 1e-06


def xor_swap(value, axis, bit):
    count = lax.axis_size(axis)
    return lax.ppermute(value, axis, [(source, source ^ bit) for source in range(count)])


def power_of_two(count):
    return count > 1 and count & (count - 1) == 0


def gather_blocks(first, second, axis):
    count = lax.axis_size(axis)
    half = first.shape[1]
    if not power_of_two(count) or count < 4:
        own = lax.axis_index(axis)
        pieces = [lax.all_gather(part, axis, axis=1, tiled=False) for part in (first, second)]
        pieces = [
            lax.dynamic_index_in_dim(part, own ^ mask, axis=1, keepdims=False)
            for part in pieces
            for mask in range(count)
        ]
        return pieces, list(range(count)) * 2, [0] * count + [half] * count
    chip_bits = [1 << b for b in range(1, count.bit_length() - 1)]
    orders = (chip_bits, chip_bits[::-1])
    routed = ([first], [second])
    routed_masks = ([0], [0])
    fresh = ([0], [0])
    shared = ([], [])
    shared_masks = ([], [])
    for step in range(len(chip_bits) + 1):
        last = step == len(chip_bits)
        sent = [None, None]
        if not last:
            sent = [xor_swap(tuple(routed[h]), axis, orders[h][step]) for h in range(2)]
        across = [xor_swap(tuple(routed[h][i] for i in fresh[h]), axis, 1) for h in range(2)]
        for h in range(2):
            shared[h].extend(across[h])
            shared_masks[h].extend([routed_masks[h][i] ^ 1 for i in fresh[h]])
            if not last:
                bit = orders[h][step]
                fresh[h][:] = list(range(len(routed[h]), 2 * len(routed[h])))
                routed[h].extend(sent[h])
                routed_masks[h].extend([mask ^ bit for mask in routed_masks[h]])
    gathered = routed[0] + shared[0] + routed[1] + shared[1]
    masks = routed_masks[0] + shared_masks[0] + routed_masks[1] + shared_masks[1]
    offsets = [0] * count + [half] * count
    return gathered, masks, offsets


def all_sum(value, axis, keep=None):
    keep = value.shape[0] if keep is None else keep
    count = lax.axis_size(axis)
    if not power_of_two(count):
        return lax.psum(value, axis)[:keep]
    bit = 1
    while bit < count:
        if bit * 2 < count:
            value = value + xor_swap(value, axis, bit)
        else:
            value = value[:keep] + xor_swap(value, axis, bit)[:keep]
        bit *= 2
    return value


def embed_kernel(picture_ref, caption_ref, picture_gain_ref, caption_gain_ref, first_ref, second_ref):
    half = first_ref.shape[1]
    towers = ((picture_ref, picture_gain_ref), (caption_ref, caption_gain_ref))
    for tower, (pooled_ref, gain_ref) in enumerate(towers):
        values = pooled_ref[0].astype(jnp.float32)
        centred = values - jnp.mean(values, axis=-1, keepdims=True)
        inverse = lax.rsqrt(jnp.mean(centred * centred, axis=-1, keepdims=True) + epsilon)
        scaled = centred * inverse * gain_ref[...][None, :]
        inv_length = lax.rsqrt(jnp.sum(scaled * scaled, axis=-1, keepdims=True) + epsilon)
        unit_rows = (scaled * inv_length).astype(first_ref.dtype)
        first_ref[tower] = unit_rows[:half]
        second_ref[tower] = unit_rows[half:]


def embed_both(picture, caption, picture_gain, caption_gain):
    rows, width = picture.shape[1:]
    vmem = pltpu.MemorySpace.VMEM
    half = jax.ShapeDtypeStruct((2, rows // 2, width), jnp.bfloat16)
    return pl.pallas_call(
        embed_kernel,
        out_shape=(half, half),
        in_specs=[pl.BlockSpec(memory_space=vmem)] * 4,
        out_specs=(pl.BlockSpec(memory_space=vmem), pl.BlockSpec(memory_space=vmem)),
    )(picture, caption, picture_gain, caption_gain)


def grad_kernel(masks, offsets, *refs):
    (sharpness_ref, shift_ref, multiplier_ref, counts_ref, picture_ref, caption_ref, picture_gain_ref,
     caption_gain_ref, partner_ref) = refs[:9]
    pieces = refs[9 : 9 + len(masks)]
    image_grad_ref, text_grad_ref, sums_ref, gathered_ref, copy_sems = refs[9 + len(masks) :]
    piece = pieces[0].shape[1]
    arrivals = [
        pltpu.make_async_copy(
            source, gathered_ref.at[:, position * piece : (position + 1) * piece, :], copy_sems.at[position]
        )
        for position, source in enumerate(pieces)
    ]
    for arrival in arrivals:
        arrival.start()
    blocks = counts_ref.shape[1]
    own_block = lax.axis_index("blk")
    block_rows = picture_ref.shape[1]
    width = picture_ref.shape[2]
    group_rows = gathered_ref.shape[1]
    own_start = own_block * block_rows
    total = counts_ref[0, 0]
    for block in range(1, blocks):
        total = total + counts_ref[0, block]
    real_count = jnp.full((1, 1), total, jnp.int32).astype(jnp.float32)
    score_sharpness_factor = jnp.exp(jnp.full((1, 1), sharpness_ref[0], jnp.float32))
    score_shift_amount = jnp.full((1, 1), shift_ref[0], jnp.float32)
    grad_factor = jnp.full((1, 1), multiplier_ref[0], jnp.float32) / real_count

    lane = lax.broadcasted_iota(jnp.int32, (1, group_rows), 1)
    held_row = jnp.zeros((1, group_rows), jnp.int32)
    limit = jnp.zeros((1, group_rows), jnp.int32)
    for position, (mask, offset) in enumerate(zip(masks, offsets)):
        block = own_block ^ mask
        here = lane // piece == position
        held_row = jnp.where(here, block * block_rows + offset + lane % piece, held_row)
        limit = jnp.where(here, counts_ref[0, block], limit)
    real_group = (held_row % block_rows) < limit
    sub = lax.broadcasted_iota(jnp.int32, (block_rows, 1), 0)
    real_own = sub < counts_ref[0, own_block]
    kept = real_own & real_group

    natural = lax.broadcasted_iota(jnp.int32, (block_rows, group_rows), 1)
    own_index = own_start + lax.broadcasted_iota(jnp.int32, (block_rows, group_rows), 0)
    partner_row = partner_ref[...]
    own_partner = jnp.sum(
        jnp.where(natural == own_index, partner_row.astype(jnp.float32), 0.0), axis=1, keepdims=True
    ).astype(jnp.int32)
    matched_image = jnp.sum(
        jnp.where(partner_row == own_index, natural.astype(jnp.float32), 0.0), axis=1, keepdims=True
    ).astype(jnp.int32)
    positives = (own_partner == held_row, matched_image == held_row)

    start_b = len(masks) // 2 * piece
    for arrival in arrivals:
        arrival.wait()
    loss_rows = []
    towers = ((picture_ref, picture_gain_ref, image_grad_ref), (caption_ref, caption_gain_ref, text_grad_ref))
    for tower, (pooled_ref, gain_ref, grad_ref) in enumerate(towers):
        values = pooled_ref[0].astype(jnp.float32)
        gain = gain_ref[...][None, :]
        centred = values - jnp.mean(values, axis=-1, keepdims=True)
        inverse = lax.rsqrt(jnp.mean(centred * centred, axis=-1, keepdims=True) + epsilon)
        normed = centred * inverse
        scaled = normed * gain
        inv_length = lax.rsqrt(jnp.sum(scaled * scaled, axis=-1, keepdims=True) + epsilon)
        unit_rows = scaled * inv_length

        own = jnp.concatenate(
            [gathered_ref[tower, 0:piece, :], gathered_ref[tower, start_b : start_b + piece, :]], axis=0
        )
        other = gathered_ref[1 - tower]
        scores = lax.dot_general(own, other, (((1,), (1,)), ((), ())), preferred_element_type=jnp.float32)
        score_similarity_table = score_sharpness_factor * scores + score_shift_amount
        labels = jnp.where(positives[tower], 1.0, -1.0)
        margin = -labels * score_similarity_table
        if tower == 0:
            softplus = jnp.maximum(margin, 0.0) + jnp.log1p(jnp.exp(-jnp.abs(margin)))
            loss_rows.append(jnp.sum(jnp.where(kept, softplus, 0.0), axis=(0, 1), keepdims=True))
        weights = jnp.where(kept, -labels * jax.nn.sigmoid(margin), 0.0) * grad_factor
        direction = score_sharpness_factor * jnp.dot(
            weights.astype(jnp.bfloat16), other, preferred_element_type=jnp.float32
        )
        tangent = (
            direction - unit_rows * jnp.sum(unit_rows * direction, axis=-1, keepdims=True)
        ) * inv_length
        sums_ref[tower : tower + 1, :] = jnp.sum(tangent * normed, axis=0, keepdims=True)
        scaled_back = tangent * gain
        gradient = (
            scaled_back
            - jnp.mean(scaled_back, axis=-1, keepdims=True)
            - normed * jnp.mean(scaled_back * normed, axis=-1, keepdims=True)
        ) * inverse
        grad_ref[0] = gradient.astype(grad_ref.dtype)
    first_lane = lax.broadcasted_iota(jnp.int32, (1, width), 1) == 0
    sums_ref[2:3, :] = jnp.where(first_lane, loss_rows[0] / real_count, 0.0)


def group_kernel(image_masks, text_masks, *refs):
    (sharpness_ref, shift_ref, multiplier_ref, counts_ref, picture_gain_ref, caption_gain_ref,
     partner_ref) = refs[:7]
    count = len(image_masks)
    pieces = refs[7 : 7 + 2 * count]
    (image_grad_ref, text_grad_ref, sums_ref, raw_ref, unit_ref, short_ref, normed_ref, inverse_ref,
     length_ref, weights_ref, tangent_ref, copy_sems) = refs[7 + 2 * count :]
    block_rows = pieces[0].shape[1]
    group_rows = raw_ref.shape[1]
    width = raw_ref.shape[2]
    own_block = lax.axis_index("blk")

    def block_of(mask):
        block = own_block
        for bit in range(mask.bit_length()):
            if mask >> bit & 1:
                block = block + (1 - 2 * (own_block // (1 << bit) % 2)) * (1 << bit)
        return block

    arrivals = []
    for position, source in enumerate(pieces):
        tower, slot = divmod(position, count)
        masks = image_masks if tower == 0 else text_masks
        rows = pl.ds(pl.multiple_of(block_of(masks[slot]) * block_rows, block_rows), block_rows)
        arrival = pltpu.make_async_copy(source.at[0], raw_ref.at[tower, rows, :], copy_sems.at[position])
        arrival.start()
        arrivals.append(arrival)

    blocks = counts_ref.shape[1]
    total = counts_ref[0, 0]
    for block in range(1, blocks):
        total = total + counts_ref[0, block]
    real_count = jnp.full((1, 1), total, jnp.int32).astype(jnp.float32)
    score_sharpness_factor = jnp.exp(jnp.full((1, 1), sharpness_ref[0], jnp.float32))
    score_shift_amount = jnp.full((1, 1), shift_ref[0], jnp.float32)
    grad_factor = jnp.full((1, 1), multiplier_ref[0], jnp.float32) / real_count

    def held(shape, dim):
        row = lax.broadcasted_iota(jnp.int32, shape, dim)
        limit = jnp.zeros(shape, jnp.int32)
        for block in range(blocks):
            limit = jnp.where(row // block_rows == block, counts_ref[0, block], limit)
        return row, (row % block_rows) < limit

    image_row, image_real = held((group_rows, 1), 0)
    text_row, text_real = held((1, group_rows), 1)
    natural = lax.broadcasted_iota(jnp.int32, (group_rows, group_rows), 1)
    partner_of_image = jnp.sum(
        jnp.where(natural == image_row, partner_ref[...].astype(jnp.float32), 0.0), axis=1, keepdims=True
    ).astype(jnp.int32)

    for arrival in arrivals:
        arrival.wait()
    gains = (picture_gain_ref[...][None, :], caption_gain_ref[...][None, :])
    chunk = min(128, group_rows)
    for tower in range(2):
        for first in range(0, group_rows, chunk):
            rows = pl.ds(first, chunk)
            values = raw_ref[tower, rows, :].astype(jnp.float32)
            centred = values - jnp.mean(values, axis=-1, keepdims=True)
            inverse = lax.rsqrt(jnp.mean(centred * centred, axis=-1, keepdims=True) + epsilon)
            normed = centred * inverse
            scaled = normed * gains[tower]
            inv_length = lax.rsqrt(jnp.sum(scaled * scaled, axis=-1, keepdims=True) + epsilon)
            unit_rows = scaled * inv_length
            unit_ref[tower, rows, :] = unit_rows
            short_ref[tower, rows, :] = unit_rows.astype(short_ref.dtype)
            normed_ref[tower, rows, :] = normed
            inverse_ref[tower, rows, :] = inverse
            length_ref[tower, rows, :] = inv_length

    loss = jnp.zeros((1, 1), jnp.float32)
    for first in range(0, group_rows, chunk):
        rows = pl.ds(first, chunk)
        scores = lax.dot_general(
            short_ref[0, rows, :], short_ref[1], (((1,), (1,)), ((), ())), preferred_element_type=jnp.float32
        )
        score_similarity_table = score_sharpness_factor * scores + score_shift_amount
        labels = jnp.where(partner_of_image[first : first + chunk] == text_row, 1.0, -1.0)
        kept = image_real[first : first + chunk] & text_real
        margin = -labels * score_similarity_table
        decay = jnp.exp(-jnp.abs(margin))
        softplus = jnp.maximum(margin, 0.0) + jnp.log1p(decay)
        loss = loss + jnp.sum(jnp.where(kept, softplus, 0.0), axis=(0, 1), keepdims=True)
        sigmoid = jnp.where(margin >= 0.0, 1.0, decay) / (1.0 + decay)
        weights = jnp.where(kept, -labels * sigmoid, 0.0) * grad_factor
        weights_ref[rows, :] = weights.astype(weights_ref.dtype)

    for tower, grad_ref in enumerate((image_grad_ref, text_grad_ref)):
        gain_sum = jnp.zeros((1, width), jnp.float32)
        for first in range(0, group_rows, chunk):
            rows = pl.ds(first, chunk)
            if tower == 0:
                pairs = weights_ref[rows, :]
                contract = (((1,), (0,)), ((), ()))
            else:
                pairs = weights_ref[:, rows]
                contract = (((0,), (0,)), ((), ()))
            direction = score_sharpness_factor * lax.dot_general(
                pairs, short_ref[1 - tower], contract, preferred_element_type=jnp.float32
            )
            unit_rows = unit_ref[tower, rows, :]
            normed = normed_ref[tower, rows, :]
            tangent = (
                direction - unit_rows * jnp.sum(unit_rows * direction, axis=-1, keepdims=True)
            ) * length_ref[tower, rows, :]
            gain_sum = gain_sum + jnp.sum(tangent * normed, axis=0, keepdims=True)
            tangent_ref[rows, :] = tangent
        sums_ref[tower : tower + 1, :] = gain_sum
        own = pl.ds(pl.multiple_of(own_block * block_rows, block_rows), block_rows)
        normed = normed_ref[tower, own, :]
        scaled_back = tangent_ref[own, :] * gains[tower]
        gradient = (
            scaled_back
            - jnp.mean(scaled_back, axis=-1, keepdims=True)
            - normed * jnp.mean(scaled_back * normed, axis=-1, keepdims=True)
        ) * inverse_ref[tower, own, :]
        grad_ref[0] = gradient.astype(grad_ref.dtype)
    first_lane = lax.broadcasted_iota(jnp.int32, (1, width), 1) == 0
    sums_ref[2:3, :] = jnp.where(first_lane, loss / real_count, 0.0)


def whole_group(
    picture_averaged_features,
    caption_averaged_features,
    picture_rescale_factor,
    caption_rescale_factor,
    exponent_of_sharpness,
    score_shift_term,
    objective_multiplier,
    matching_caption_index,
    genuine_entry_counts,
):
    count = lax.axis_size("blk")
    block_rows, width = picture_averaged_features.shape[1:]
    group_rows = count * block_rows
    pieces, masks, unused = gather_blocks(picture_averaged_features, caption_averaged_features, "blk")
    smem = pltpu.MemorySpace.SMEM
    vmem = pltpu.MemorySpace.VMEM
    grad_shape = jax.ShapeDtypeStruct(picture_averaged_features.shape, jnp.bfloat16)
    full = (2, group_rows, width)
    column = (2, group_rows, 1)
    image_grad, text_grad, sums = pl.pallas_call(
        functools.partial(group_kernel, tuple(masks[:count]), tuple(masks[count:])),
        out_shape=(grad_shape, grad_shape, jax.ShapeDtypeStruct((3, width), jnp.float32)),
        in_specs=[pl.BlockSpec(memory_space=smem)] * 4
        + [pl.BlockSpec(memory_space=vmem)] * 3
        + [pl.BlockSpec(memory_space=pl.ANY)] * len(pieces),
        out_specs=(pl.BlockSpec(memory_space=vmem),) * 3,
        scratch_shapes=[
            pltpu.VMEM(full, jnp.bfloat16),
            pltpu.VMEM(full, jnp.float32),
            pltpu.VMEM(full, jnp.bfloat16),
            pltpu.VMEM(full, jnp.float32),
            pltpu.VMEM(column, jnp.float32),
            pltpu.VMEM(column, jnp.float32),
            pltpu.VMEM((group_rows, group_rows), jnp.bfloat16),
            pltpu.VMEM((group_rows, width), jnp.float32),
            pltpu.SemaphoreType.DMA((len(pieces),)),
        ],
    )(
        exponent_of_sharpness,
        score_shift_term,
        objective_multiplier,
        genuine_entry_counts,
        picture_rescale_factor,
        caption_rescale_factor,
        matching_caption_index,
        *[pltpu.with_memory_space_constraint(piece, pltpu.VMEM) for piece in pieces],
    )
    group_loss = sums[2, 0:1]
    gain_grads = all_sum(sums, "rep", keep=2)
    return (image_grad, text_grad, gain_grads, group_loss)


def shards(
    picture_averaged_features,
    caption_averaged_features,
    picture_rescale_factor,
    caption_rescale_factor,
    exponent_of_sharpness,
    score_shift_term,
    objective_multiplier,
    matching_caption_index,
    genuine_entry_counts,
):
    width = picture_averaged_features.shape[2]
    first, second = embed_both(
        picture_averaged_features, caption_averaged_features, picture_rescale_factor, caption_rescale_factor
    )
    pieces, masks, offsets = gather_blocks(first, second, "blk")

    smem = pltpu.MemorySpace.SMEM
    vmem = pltpu.MemorySpace.VMEM
    grad_shape = jax.ShapeDtypeStruct(picture_averaged_features.shape, jnp.bfloat16)
    image_grad, text_grad, sums = pl.pallas_call(
        functools.partial(grad_kernel, tuple(masks), tuple(offsets)),
        out_shape=(grad_shape, grad_shape, jax.ShapeDtypeStruct((3, width), jnp.float32)),
        in_specs=[pl.BlockSpec(memory_space=smem)] * 4
        + [pl.BlockSpec(memory_space=vmem)] * 5
        + [pl.BlockSpec(memory_space=pl.ANY)] * len(pieces),
        out_specs=(pl.BlockSpec(memory_space=vmem),) * 3,
        scratch_shapes=[
            pltpu.VMEM((2, len(pieces) * pieces[0].shape[1], width), pieces[0].dtype),
            pltpu.SemaphoreType.DMA((len(pieces),)),
        ],
    )(
        exponent_of_sharpness,
        score_shift_term,
        objective_multiplier,
        genuine_entry_counts,
        picture_averaged_features,
        caption_averaged_features,
        picture_rescale_factor,
        caption_rescale_factor,
        matching_caption_index,
        *pieces,
    )

    group_sums = all_sum(sums, "blk")
    group_loss = group_sums[2, 0:1]
    gain_grads = all_sum(group_sums, "rep", keep=2)
    return (image_grad, text_grad, gain_grads, group_loss)


def body(*args):
    group_rows = args[0].shape[1] * lax.axis_size("blk")
    return (whole_group if group_rows <= 512 else shards)(*args)


def solution(mesh):
    placed = (
        P("rep", "blk", None),
        P("rep", "blk", None),
        P(),
        P(),
        P(),
        P(),
        P(),
        P("rep", None),
        P("rep", None),
    )
    return jax.shard_map(
        body,
        mesh=mesh,
        in_specs=placed,
        out_specs=(P("rep", "blk", None), P("rep", "blk", None), P(), P("rep")),
        check_vma=False,
    )
```

```python
import functools

import jax
import jax.numpy as jnp
from jax import lax
from jax.sharding import PartitionSpec as P
from jax.experimental import pallas as pl
from jax.experimental.pallas import tpu as pltpu

epsilon = 1e-06


def xor_swap(value, axis, bit):
    count = lax.axis_size(axis)
    return lax.ppermute(value, axis, [(source, source ^ bit) for source in range(count)])


def power_of_two(count):
    return count > 1 and count & (count - 1) == 0


def gather_blocks(first, second, axis):
    count = lax.axis_size(axis)
    half = first.shape[1]
    if not power_of_two(count) or count < 4:
        own = lax.axis_index(axis)
        pieces = [lax.all_gather(part, axis, axis=1, tiled=False) for part in (first, second)]
        pieces = [
            lax.dynamic_index_in_dim(part, own ^ mask, axis=1, keepdims=False)
            for part in pieces
            for mask in range(count)
        ]
        return pieces, list(range(count)) * 2, [0] * count + [half] * count
    chip_bits = [1 << b for b in range(1, count.bit_length() - 1)]
    orders = (chip_bits, chip_bits[::-1])
    routed = ([first], [second])
    routed_masks = ([0], [0])
    fresh = ([0], [0])
    shared = ([], [])
    shared_masks = ([], [])
    for step in range(len(chip_bits) + 1):
        last = step == len(chip_bits)
        sent = [None, None]
        if not last:
            sent = [xor_swap(tuple(routed[h]), axis, orders[h][step]) for h in range(2)]
        across = [xor_swap(tuple(routed[h][i] for i in fresh[h]), axis, 1) for h in range(2)]
        for h in range(2):
            shared[h].extend(across[h])
            shared_masks[h].extend([routed_masks[h][i] ^ 1 for i in fresh[h]])
            if not last:
                bit = orders[h][step]
                fresh[h][:] = list(range(len(routed[h]), 2 * len(routed[h])))
                routed[h].extend(sent[h])
                routed_masks[h].extend([mask ^ bit for mask in routed_masks[h]])
    gathered = routed[0] + shared[0] + routed[1] + shared[1]
    masks = routed_masks[0] + shared_masks[0] + routed_masks[1] + shared_masks[1]
    offsets = [0] * count + [half] * count
    return gathered, masks, offsets


def all_sum(value, axis, keep=None):
    keep = value.shape[0] if keep is None else keep
    count = lax.axis_size(axis)
    if not power_of_two(count):
        return lax.psum(value, axis)[:keep]
    bit = 1
    while bit < count:
        if bit * 2 < count:
            value = value + xor_swap(value, axis, bit)
        else:
            value = value[:keep] + xor_swap(value, axis, bit)[:keep]
        bit *= 2
    return value


def embed_kernel(picture_ref, caption_ref, picture_gain_ref, caption_gain_ref, first_ref, second_ref):
    half = first_ref.shape[1]
    towers = ((picture_ref, picture_gain_ref), (caption_ref, caption_gain_ref))
    for tower, (pooled_ref, gain_ref) in enumerate(towers):
        values = pooled_ref[0].astype(jnp.float32)
        centred = values - jnp.mean(values, axis=-1, keepdims=True)
        inverse = lax.rsqrt(jnp.mean(centred * centred, axis=-1, keepdims=True) + epsilon)
        scaled = centred * inverse * gain_ref[...][None, :]
        inv_length = lax.rsqrt(jnp.sum(scaled * scaled, axis=-1, keepdims=True) + epsilon)
        unit_rows = (scaled * inv_length).astype(first_ref.dtype)
        first_ref[tower] = unit_rows[:half]
        second_ref[tower] = unit_rows[half:]


def embed_both(picture, caption, picture_gain, caption_gain):
    rows, width = picture.shape[1:]
    vmem = pltpu.MemorySpace.VMEM
    half = jax.ShapeDtypeStruct((2, rows // 2, width), jnp.bfloat16)
    return pl.pallas_call(
        embed_kernel,
        out_shape=(half, half),
        in_specs=[pl.BlockSpec(memory_space=vmem)] * 4,
        out_specs=(pl.BlockSpec(memory_space=vmem), pl.BlockSpec(memory_space=vmem)),
    )(picture, caption, picture_gain, caption_gain)


def grad_kernel(masks, offsets, *refs):
    (sharpness_ref, shift_ref, multiplier_ref, counts_ref, picture_ref, caption_ref, picture_gain_ref,
     caption_gain_ref, partner_ref) = refs[:9]
    pieces = refs[9 : 9 + len(masks)]
    image_grad_ref, text_grad_ref, sums_ref, gathered_ref, copy_sems = refs[9 + len(masks) :]
    piece = pieces[0].shape[1]
    arrivals = [
        pltpu.make_async_copy(
            source, gathered_ref.at[:, position * piece : (position + 1) * piece, :], copy_sems.at[position]
        )
        for position, source in enumerate(pieces)
    ]
    for arrival in arrivals:
        arrival.start()
    blocks = counts_ref.shape[1]
    own_block = lax.axis_index("blk")
    block_rows = picture_ref.shape[1]
    width = picture_ref.shape[2]
    group_rows = gathered_ref.shape[1]
    own_start = own_block * block_rows
    total = counts_ref[0, 0]
    for block in range(1, blocks):
        total = total + counts_ref[0, block]
    real_count = jnp.full((1, 1), total, jnp.int32).astype(jnp.float32)
    score_sharpness_factor = jnp.exp(jnp.full((1, 1), sharpness_ref[0], jnp.float32))
    score_shift_amount = jnp.full((1, 1), shift_ref[0], jnp.float32)
    grad_factor = jnp.full((1, 1), multiplier_ref[0], jnp.float32) / real_count

    lane = lax.broadcasted_iota(jnp.int32, (1, group_rows), 1)
    held_row = jnp.zeros((1, group_rows), jnp.int32)
    limit = jnp.zeros((1, group_rows), jnp.int32)
    for position, (mask, offset) in enumerate(zip(masks, offsets)):
        block = own_block ^ mask
        here = lane // piece == position
        held_row = jnp.where(here, block * block_rows + offset + lane % piece, held_row)
        limit = jnp.where(here, counts_ref[0, block], limit)
    real_group = (held_row % block_rows) < limit
    sub = lax.broadcasted_iota(jnp.int32, (block_rows, 1), 0)
    real_own = sub < counts_ref[0, own_block]
    kept = real_own & real_group

    natural = lax.broadcasted_iota(jnp.int32, (block_rows, group_rows), 1)
    own_index = own_start + lax.broadcasted_iota(jnp.int32, (block_rows, group_rows), 0)
    partner_row = partner_ref[...]
    own_partner = jnp.sum(
        jnp.where(natural == own_index, partner_row.astype(jnp.float32), 0.0), axis=1, keepdims=True
    ).astype(jnp.int32)
    matched_image = jnp.sum(
        jnp.where(partner_row == own_index, natural.astype(jnp.float32), 0.0), axis=1, keepdims=True
    ).astype(jnp.int32)
    positives = (own_partner == held_row, matched_image == held_row)

    start_b = len(masks) // 2 * piece
    for arrival in arrivals:
        arrival.wait()
    loss_rows = []
    towers = ((picture_ref, picture_gain_ref, image_grad_ref), (caption_ref, caption_gain_ref, text_grad_ref))
    for tower, (pooled_ref, gain_ref, grad_ref) in enumerate(towers):
        values = pooled_ref[0].astype(jnp.float32)
        gain = gain_ref[...][None, :]
        centred = values - jnp.mean(values, axis=-1, keepdims=True)
        inverse = lax.rsqrt(jnp.mean(centred * centred, axis=-1, keepdims=True) + epsilon)
        normed = centred * inverse
        scaled = normed * gain
        inv_length = lax.rsqrt(jnp.sum(scaled * scaled, axis=-1, keepdims=True) + epsilon)
        unit_rows = scaled * inv_length

        own = jnp.concatenate(
            [gathered_ref[tower, 0:piece, :], gathered_ref[tower, start_b : start_b + piece, :]], axis=0
        )
        other = gathered_ref[1 - tower]
        scores = lax.dot_general(own, other, (((1,), (1,)), ((), ())), preferred_element_type=jnp.float32)
        score_similarity_table = score_sharpness_factor * scores + score_shift_amount
        labels = jnp.where(positives[tower], 1.0, -1.0)
        margin = -labels * score_similarity_table
        if tower == 0:
            softplus = jnp.maximum(margin, 0.0) + jnp.log1p(jnp.exp(-jnp.abs(margin)))
            loss_rows.append(jnp.sum(jnp.where(kept, softplus, 0.0), axis=(0, 1), keepdims=True))
        weights = jnp.where(kept, -labels * jax.nn.sigmoid(margin), 0.0) * grad_factor
        direction = score_sharpness_factor * jnp.dot(
            weights.astype(jnp.bfloat16), other, preferred_element_type=jnp.float32
        )
        tangent = (
            direction - unit_rows * jnp.sum(unit_rows * direction, axis=-1, keepdims=True)
        ) * inv_length
        sums_ref[tower : tower + 1, :] = jnp.sum(tangent * normed, axis=0, keepdims=True)
        scaled_back = tangent * gain
        gradient = (
            scaled_back
            - jnp.mean(scaled_back, axis=-1, keepdims=True)
            - normed * jnp.mean(scaled_back * normed, axis=-1, keepdims=True)
        ) * inverse
        grad_ref[0] = gradient.astype(grad_ref.dtype)
    first_lane = lax.broadcasted_iota(jnp.int32, (1, width), 1) == 0
    sums_ref[2:3, :] = jnp.where(first_lane, loss_rows[0] / real_count, 0.0)


def group_kernel(image_masks, text_masks, *refs):
    (sharpness_ref, shift_ref, multiplier_ref, counts_ref, picture_gain_ref, caption_gain_ref,
     partner_ref) = refs[:7]
    count = len(image_masks)
    pieces = refs[7 : 7 + 2 * count]
    (image_grad_ref, text_grad_ref, sums_ref, raw_ref, unit_ref, short_ref, normed_ref, inverse_ref,
     length_ref, weights_ref, tangent_ref, copy_sems) = refs[7 + 2 * count :]
    block_rows = pieces[0].shape[1]
    group_rows = count * block_rows
    width = pieces[0].shape[2]
    own_block = lax.axis_index("blk")

    def block_of(mask):
        block = own_block
        for bit in range(mask.bit_length()):
            if mask >> bit & 1:
                block = block + (1 - 2 * (own_block // (1 << bit) % 2)) * (1 << bit)
        return block


    blocks = counts_ref.shape[1]
    total = counts_ref[0, 0]
    for block in range(1, blocks):
        total = total + counts_ref[0, block]
    real_count = jnp.full((1, 1), total, jnp.int32).astype(jnp.float32)
    score_sharpness_factor = jnp.exp(jnp.full((1, 1), sharpness_ref[0], jnp.float32))
    score_shift_amount = jnp.full((1, 1), shift_ref[0], jnp.float32)
    grad_factor = jnp.full((1, 1), multiplier_ref[0], jnp.float32) / real_count

    def held(shape, dim):
        row = lax.broadcasted_iota(jnp.int32, shape, dim)
        limit = jnp.zeros(shape, jnp.int32)
        for block in range(blocks):
            limit = jnp.where(row // block_rows == block, counts_ref[0, block], limit)
        return row, (row % block_rows) < limit

    image_row, image_real = held((group_rows, 1), 0)
    text_row, text_real = held((1, group_rows), 1)
    natural = lax.broadcasted_iota(jnp.int32, (group_rows, group_rows), 1)
    partner_of_image = jnp.sum(
        jnp.where(natural == image_row, partner_ref[...].astype(jnp.float32), 0.0), axis=1, keepdims=True
    ).astype(jnp.int32)

    gains = (picture_gain_ref[...][None, :], caption_gain_ref[...][None, :])
    chunk = min(128, group_rows)
    for position, source in enumerate(pieces):
        tower, slot = divmod(position, count)
        masks = image_masks if tower == 0 else text_masks
        rows = pl.ds(pl.multiple_of(block_of(masks[slot]) * block_rows, block_rows), block_rows)
        if source is not None:
            values = source[0].astype(jnp.float32)
            centred = values - jnp.mean(values, axis=-1, keepdims=True)
            inverse = lax.rsqrt(jnp.mean(centred * centred, axis=-1, keepdims=True) + epsilon)
            normed = centred * inverse
            scaled = normed * gains[tower]
            inv_length = lax.rsqrt(jnp.sum(scaled * scaled, axis=-1, keepdims=True) + epsilon)
            unit_rows = scaled * inv_length
            unit_ref[tower, rows, :] = unit_rows
            short_ref[tower, rows, :] = unit_rows.astype(short_ref.dtype)
            normed_ref[tower, rows, :] = normed
            inverse_ref[tower, rows, :] = inverse
            length_ref[tower, rows, :] = inv_length

    loss = jnp.zeros((1, 1), jnp.float32)
    for first in range(0, group_rows, chunk):
        rows = pl.ds(first, chunk)
        scores = lax.dot_general(
            short_ref[0, rows, :], short_ref[1], (((1,), (1,)), ((), ())), preferred_element_type=jnp.float32
        )
        score_similarity_table = score_sharpness_factor * scores + score_shift_amount
        labels = jnp.where(partner_of_image[first : first + chunk] == text_row, 1.0, -1.0)
        kept = image_real[first : first + chunk] & text_real
        margin = -labels * score_similarity_table
        decay = jnp.exp(-jnp.abs(margin))
        softplus = jnp.maximum(margin, 0.0) + jnp.log1p(decay)
        loss = loss + jnp.sum(jnp.where(kept, softplus, 0.0), axis=(0, 1), keepdims=True)
        sigmoid = jnp.where(margin >= 0.0, 1.0, decay) / (1.0 + decay)
        weights = jnp.where(kept, -labels * sigmoid, 0.0) * grad_factor
        weights_ref[rows, :] = weights.astype(weights_ref.dtype)

    for tower, grad_ref in enumerate((image_grad_ref, text_grad_ref)):
        gain_sum = jnp.zeros((1, width), jnp.float32)
        for first in range(0, group_rows, chunk):
            rows = pl.ds(first, chunk)
            if tower == 0:
                pairs = weights_ref[rows, :]
                contract = (((1,), (0,)), ((), ()))
            else:
                pairs = weights_ref[:, rows]
                contract = (((0,), (0,)), ((), ()))
            direction = score_sharpness_factor * lax.dot_general(
                pairs, short_ref[1 - tower], contract, preferred_element_type=jnp.float32
            )
            unit_rows = unit_ref[tower, rows, :]
            normed = normed_ref[tower, rows, :]
            tangent = (
                direction - unit_rows * jnp.sum(unit_rows * direction, axis=-1, keepdims=True)
            ) * length_ref[tower, rows, :]
            gain_sum = gain_sum + jnp.sum(tangent * normed, axis=0, keepdims=True)
            tangent_ref[rows, :] = tangent
        sums_ref[tower : tower + 1, :] = gain_sum
        own = pl.ds(pl.multiple_of(own_block * block_rows, block_rows), block_rows)
        normed = normed_ref[tower, own, :]
        scaled_back = tangent_ref[own, :] * gains[tower]
        gradient = (
            scaled_back
            - jnp.mean(scaled_back, axis=-1, keepdims=True)
            - normed * jnp.mean(scaled_back * normed, axis=-1, keepdims=True)
        ) * inverse_ref[tower, own, :]
        grad_ref[0] = gradient.astype(grad_ref.dtype)
    first_lane = lax.broadcasted_iota(jnp.int32, (1, width), 1) == 0
    sums_ref[2:3, :] = jnp.where(first_lane, loss / real_count, 0.0)


def whole_group(
    picture_averaged_features,
    caption_averaged_features,
    picture_rescale_factor,
    caption_rescale_factor,
    exponent_of_sharpness,
    score_shift_term,
    objective_multiplier,
    matching_caption_index,
    genuine_entry_counts,
):
    count = lax.axis_size("blk")
    block_rows, width = picture_averaged_features.shape[1:]
    group_rows = count * block_rows
    pieces, masks, unused = gather_blocks(picture_averaged_features, caption_averaged_features, "blk")
    smem = pltpu.MemorySpace.SMEM
    vmem = pltpu.MemorySpace.VMEM
    grad_shape = jax.ShapeDtypeStruct(picture_averaged_features.shape, jnp.bfloat16)
    full = (2, group_rows, width)
    column = (2, group_rows, 1)
    image_grad, text_grad, sums = pl.pallas_call(
        functools.partial(group_kernel, tuple(masks[:count]), tuple(masks[count:])),
        out_shape=(grad_shape, grad_shape, jax.ShapeDtypeStruct((3, width), jnp.float32)),
        in_specs=[pl.BlockSpec(memory_space=smem)] * 4
        + [pl.BlockSpec(memory_space=vmem)] * 3
        + [pl.BlockSpec(memory_space=vmem)] * len(pieces),
        out_specs=(pl.BlockSpec(memory_space=vmem),) * 3,
        scratch_shapes=[
            pltpu.VMEM(full, jnp.bfloat16),
            pltpu.VMEM(full, jnp.float32),
            pltpu.VMEM(full, jnp.bfloat16),
            pltpu.VMEM(full, jnp.float32),
            pltpu.VMEM(column, jnp.float32),
            pltpu.VMEM(column, jnp.float32),
            pltpu.VMEM((group_rows, group_rows), jnp.bfloat16),
            pltpu.VMEM((group_rows, width), jnp.float32),
            pltpu.SemaphoreType.DMA((len(pieces),)),
        ],
    )(
        exponent_of_sharpness,
        score_shift_term,
        objective_multiplier,
        genuine_entry_counts,
        picture_rescale_factor,
        caption_rescale_factor,
        matching_caption_index,
        *[pltpu.with_memory_space_constraint(piece, pltpu.VMEM) for piece in pieces],
    )
    group_loss = sums[2, 0:1]
    gain_grads = all_sum(sums, "rep", keep=2)
    return (image_grad, text_grad, gain_grads, group_loss)


def shards(
    picture_averaged_features,
    caption_averaged_features,
    picture_rescale_factor,
    caption_rescale_factor,
    exponent_of_sharpness,
    score_shift_term,
    objective_multiplier,
    matching_caption_index,
    genuine_entry_counts,
):
    width = picture_averaged_features.shape[2]
    first, second = embed_both(
        picture_averaged_features, caption_averaged_features, picture_rescale_factor, caption_rescale_factor
    )
    pieces, masks, offsets = gather_blocks(first, second, "blk")

    smem = pltpu.MemorySpace.SMEM
    vmem = pltpu.MemorySpace.VMEM
    grad_shape = jax.ShapeDtypeStruct(picture_averaged_features.shape, jnp.bfloat16)
    image_grad, text_grad, sums = pl.pallas_call(
        functools.partial(grad_kernel, tuple(masks), tuple(offsets)),
        out_shape=(grad_shape, grad_shape, jax.ShapeDtypeStruct((3, width), jnp.float32)),
        in_specs=[pl.BlockSpec(memory_space=smem)] * 4
        + [pl.BlockSpec(memory_space=vmem)] * 5
        + [pl.BlockSpec(memory_space=pl.ANY)] * len(pieces),
        out_specs=(pl.BlockSpec(memory_space=vmem),) * 3,
        scratch_shapes=[
            pltpu.VMEM((2, len(pieces) * pieces[0].shape[1], width), pieces[0].dtype),
            pltpu.SemaphoreType.DMA((len(pieces),)),
        ],
    )(
        exponent_of_sharpness,
        score_shift_term,
        objective_multiplier,
        genuine_entry_counts,
        picture_averaged_features,
        caption_averaged_features,
        picture_rescale_factor,
        caption_rescale_factor,
        matching_caption_index,
        *pieces,
    )

    group_sums = all_sum(sums, "blk")
    group_loss = group_sums[2, 0:1]
    gain_grads = all_sum(group_sums, "rep", keep=2)
    return (image_grad, text_grad, gain_grads, group_loss)


def body(*args):
    group_rows = args[0].shape[1] * lax.axis_size("blk")
    return (whole_group if group_rows <= 512 else shards)(*args)


def solution(mesh):
    placed = (
        P("rep", "blk", None),
        P("rep", "blk", None),
        P(),
        P(),
        P(),
        P(),
        P(),
        P("rep", None),
        P("rep", None),
    )
    return jax.shard_map(
        body,
        mesh=mesh,
        in_specs=placed,
        out_specs=(P("rep", "blk", None), P("rep", "blk", None), P(), P("rep")),
        check_vma=False,
    )
```

```python
import functools

import jax
import jax.numpy as jnp
from jax import lax
from jax.sharding import PartitionSpec as P
from jax.experimental import pallas as pl
from jax.experimental.pallas import tpu as pltpu

epsilon = 1e-06


def xor_swap(value, axis, bit):
    count = lax.axis_size(axis)
    return lax.ppermute(value, axis, [(source, source ^ bit) for source in range(count)])


def power_of_two(count):
    return count > 1 and count & (count - 1) == 0


def gather_blocks(first, second, axis):
    count = lax.axis_size(axis)
    half = first.shape[1]
    if not power_of_two(count) or count < 4:
        own = lax.axis_index(axis)
        pieces = [lax.all_gather(part, axis, axis=1, tiled=False) for part in (first, second)]
        pieces = [
            lax.dynamic_index_in_dim(part, own ^ mask, axis=1, keepdims=False)
            for part in pieces
            for mask in range(count)
        ]
        return pieces, list(range(count)) * 2, [0] * count + [half] * count
    chip_bits = [1 << b for b in range(1, count.bit_length() - 1)]
    orders = (chip_bits, chip_bits[::-1])
    routed = ([first], [second])
    routed_masks = ([0], [0])
    fresh = ([0], [0])
    shared = ([], [])
    shared_masks = ([], [])
    for step in range(len(chip_bits) + 1):
        last = step == len(chip_bits)
        sent = [None, None]
        if not last:
            sent = [xor_swap(tuple(routed[h]), axis, orders[h][step]) for h in range(2)]
        across = [xor_swap(tuple(routed[h][i] for i in fresh[h]), axis, 1) for h in range(2)]
        for h in range(2):
            shared[h].extend(across[h])
            shared_masks[h].extend([routed_masks[h][i] ^ 1 for i in fresh[h]])
            if not last:
                bit = orders[h][step]
                fresh[h][:] = list(range(len(routed[h]), 2 * len(routed[h])))
                routed[h].extend(sent[h])
                routed_masks[h].extend([mask ^ bit for mask in routed_masks[h]])
    gathered = routed[0] + shared[0] + routed[1] + shared[1]
    masks = routed_masks[0] + shared_masks[0] + routed_masks[1] + shared_masks[1]
    offsets = [0] * count + [half] * count
    return gathered, masks, offsets


def all_sum(value, axis, keep=None):
    keep = value.shape[0] if keep is None else keep
    count = lax.axis_size(axis)
    if not power_of_two(count):
        return lax.psum(value, axis)[:keep]
    bit = 1
    while bit < count:
        if bit * 2 < count:
            value = value + xor_swap(value, axis, bit)
        else:
            value = value[:keep] + xor_swap(value, axis, bit)[:keep]
        bit *= 2
    return value


def embed_kernel(picture_ref, caption_ref, picture_gain_ref, caption_gain_ref, first_ref, second_ref):
    half = first_ref.shape[1]
    towers = ((picture_ref, picture_gain_ref), (caption_ref, caption_gain_ref))
    for tower, (pooled_ref, gain_ref) in enumerate(towers):
        values = pooled_ref[0].astype(jnp.float32)
        centred = values - jnp.mean(values, axis=-1, keepdims=True)
        inverse = lax.rsqrt(jnp.mean(centred * centred, axis=-1, keepdims=True) + epsilon)
        scaled = centred * inverse * gain_ref[...][None, :]
        inv_length = lax.rsqrt(jnp.sum(scaled * scaled, axis=-1, keepdims=True) + epsilon)
        unit_rows = (scaled * inv_length).astype(first_ref.dtype)
        first_ref[tower] = unit_rows[:half]
        second_ref[tower] = unit_rows[half:]


def embed_both(picture, caption, picture_gain, caption_gain):
    rows, width = picture.shape[1:]
    vmem = pltpu.MemorySpace.VMEM
    half = jax.ShapeDtypeStruct((2, rows // 2, width), jnp.bfloat16)
    return pl.pallas_call(
        embed_kernel,
        out_shape=(half, half),
        in_specs=[pl.BlockSpec(memory_space=vmem)] * 4,
        out_specs=(pl.BlockSpec(memory_space=vmem), pl.BlockSpec(memory_space=vmem)),
    )(picture, caption, picture_gain, caption_gain)


def grad_kernel(masks, offsets, *refs):
    (sharpness_ref, shift_ref, multiplier_ref, counts_ref, picture_ref, caption_ref, picture_gain_ref,
     caption_gain_ref, partner_ref) = refs[:9]
    pieces = refs[9 : 9 + len(masks)]
    image_grad_ref, text_grad_ref, sums_ref, gathered_ref, copy_sems = refs[9 + len(masks) :]
    piece = pieces[0].shape[1]
    arrivals = [
        pltpu.make_async_copy(
            source, gathered_ref.at[:, position * piece : (position + 1) * piece, :], copy_sems.at[position]
        )
        for position, source in enumerate(pieces)
    ]
    for arrival in arrivals:
        arrival.start()
    blocks = counts_ref.shape[1]
    own_block = lax.axis_index("blk")
    block_rows = picture_ref.shape[1]
    width = picture_ref.shape[2]
    group_rows = gathered_ref.shape[1]
    own_start = own_block * block_rows
    total = counts_ref[0, 0]
    for block in range(1, blocks):
        total = total + counts_ref[0, block]
    real_count = jnp.full((1, 1), total, jnp.int32).astype(jnp.float32)
    score_sharpness_factor = jnp.exp(jnp.full((1, 1), sharpness_ref[0], jnp.float32))
    score_shift_amount = jnp.full((1, 1), shift_ref[0], jnp.float32)
    grad_factor = jnp.full((1, 1), multiplier_ref[0], jnp.float32) / real_count

    lane = lax.broadcasted_iota(jnp.int32, (1, group_rows), 1)
    held_row = jnp.zeros((1, group_rows), jnp.int32)
    limit = jnp.zeros((1, group_rows), jnp.int32)
    for position, (mask, offset) in enumerate(zip(masks, offsets)):
        block = own_block ^ mask
        here = lane // piece == position
        held_row = jnp.where(here, block * block_rows + offset + lane % piece, held_row)
        limit = jnp.where(here, counts_ref[0, block], limit)
    real_group = (held_row % block_rows) < limit
    sub = lax.broadcasted_iota(jnp.int32, (block_rows, 1), 0)
    real_own = sub < counts_ref[0, own_block]
    kept = real_own & real_group

    natural = lax.broadcasted_iota(jnp.int32, (block_rows, group_rows), 1)
    own_index = own_start + lax.broadcasted_iota(jnp.int32, (block_rows, group_rows), 0)
    partner_row = partner_ref[...]
    own_partner = jnp.sum(
        jnp.where(natural == own_index, partner_row.astype(jnp.float32), 0.0), axis=1, keepdims=True
    ).astype(jnp.int32)
    matched_image = jnp.sum(
        jnp.where(partner_row == own_index, natural.astype(jnp.float32), 0.0), axis=1, keepdims=True
    ).astype(jnp.int32)
    positives = (own_partner == held_row, matched_image == held_row)

    start_b = len(masks) // 2 * piece
    for arrival in arrivals:
        arrival.wait()
    loss_rows = []
    towers = ((picture_ref, picture_gain_ref, image_grad_ref), (caption_ref, caption_gain_ref, text_grad_ref))
    for tower, (pooled_ref, gain_ref, grad_ref) in enumerate(towers):
        values = pooled_ref[0].astype(jnp.float32)
        gain = gain_ref[...][None, :]
        centred = values - jnp.mean(values, axis=-1, keepdims=True)
        inverse = lax.rsqrt(jnp.mean(centred * centred, axis=-1, keepdims=True) + epsilon)
        normed = centred * inverse
        scaled = normed * gain
        inv_length = lax.rsqrt(jnp.sum(scaled * scaled, axis=-1, keepdims=True) + epsilon)
        unit_rows = scaled * inv_length

        own = jnp.concatenate(
            [gathered_ref[tower, 0:piece, :], gathered_ref[tower, start_b : start_b + piece, :]], axis=0
        )
        other = gathered_ref[1 - tower]
        scores = lax.dot_general(own, other, (((1,), (1,)), ((), ())), preferred_element_type=jnp.float32)
        score_similarity_table = score_sharpness_factor * scores + score_shift_amount
        labels = jnp.where(positives[tower], 1.0, -1.0)
        margin = -labels * score_similarity_table
        if tower == 0:
            softplus = jnp.maximum(margin, 0.0) + jnp.log1p(jnp.exp(-jnp.abs(margin)))
            loss_rows.append(jnp.sum(jnp.where(kept, softplus, 0.0), axis=(0, 1), keepdims=True))
        weights = jnp.where(kept, -labels * jax.nn.sigmoid(margin), 0.0) * grad_factor
        direction = score_sharpness_factor * jnp.dot(
            weights.astype(jnp.bfloat16), other, preferred_element_type=jnp.float32
        )
        tangent = (
            direction - unit_rows * jnp.sum(unit_rows * direction, axis=-1, keepdims=True)
        ) * inv_length
        sums_ref[tower : tower + 1, :] = jnp.sum(tangent * normed, axis=0, keepdims=True)
        scaled_back = tangent * gain
        gradient = (
            scaled_back
            - jnp.mean(scaled_back, axis=-1, keepdims=True)
            - normed * jnp.mean(scaled_back * normed, axis=-1, keepdims=True)
        ) * inverse
        grad_ref[0] = gradient.astype(grad_ref.dtype)
    first_lane = lax.broadcasted_iota(jnp.int32, (1, width), 1) == 0
    sums_ref[2:3, :] = jnp.where(first_lane, loss_rows[0] / real_count, 0.0)


def group_kernel(image_masks, text_masks, *refs):
    (sharpness_ref, shift_ref, multiplier_ref, counts_ref, picture_gain_ref, caption_gain_ref,
     partner_ref) = refs[:7]
    count = len(image_masks)
    pieces = refs[7 : 7 + 2 * count]
    (image_grad_ref, text_grad_ref, sums_ref, raw_ref, unit_ref, short_ref, normed_ref, inverse_ref,
     length_ref, weights_ref, tangent_ref, copy_sems) = refs[7 + 2 * count :]
    block_rows = pieces[0].shape[1]
    group_rows = count * block_rows
    width = pieces[0].shape[2]
    own_block = lax.axis_index("blk")

    def block_of(mask):
        block = own_block
        for bit in range(mask.bit_length()):
            if mask >> bit & 1:
                block = block + (1 - 2 * (own_block // (1 << bit) % 2)) * (1 << bit)
        return block


    blocks = counts_ref.shape[1]
    total = counts_ref[0, 0]
    for block in range(1, blocks):
        total = total + counts_ref[0, block]
    real_count = jnp.full((1, 1), total, jnp.int32).astype(jnp.float32)
    score_sharpness_factor = jnp.exp(jnp.full((1, 1), sharpness_ref[0], jnp.float32))
    score_shift_amount = jnp.full((1, 1), shift_ref[0], jnp.float32)
    grad_factor = jnp.full((1, 1), multiplier_ref[0], jnp.float32) / real_count

    def held(shape, dim):
        row = lax.broadcasted_iota(jnp.int32, shape, dim)
        limit = jnp.zeros(shape, jnp.int32)
        for block in range(blocks):
            limit = jnp.where(row // block_rows == block, counts_ref[0, block], limit)
        return row, (row % block_rows) < limit

    image_row, image_real = held((group_rows, 1), 0)
    text_row, text_real = held((1, group_rows), 1)
    natural = lax.broadcasted_iota(jnp.int32, (group_rows, group_rows), 1)
    partner_of_image = jnp.sum(
        jnp.where(natural == image_row, partner_ref[...].astype(jnp.float32), 0.0), axis=1, keepdims=True
    ).astype(jnp.int32)

    gains = (picture_gain_ref[...][None, :], caption_gain_ref[...][None, :])
    chunk = min(128, group_rows)
    for position, source in enumerate(pieces):
        tower, slot = divmod(position, count)
        masks = image_masks if tower == 0 else text_masks
        rows = pl.ds(pl.multiple_of(block_of(masks[slot]) * block_rows, block_rows), block_rows)
        if source is not None:
            values = source[0].astype(jnp.float32)
            centred = values - jnp.mean(values, axis=-1, keepdims=True)
            inverse = lax.rsqrt(jnp.mean(centred * centred, axis=-1, keepdims=True) + epsilon)
            normed = centred * inverse
            scaled = normed * gains[tower]
            inv_length = lax.rsqrt(jnp.sum(scaled * scaled, axis=-1, keepdims=True) + epsilon)
            unit_rows = scaled * inv_length
            unit_ref[tower, rows, :] = unit_rows
            short_ref[tower, rows, :] = unit_rows.astype(short_ref.dtype)
            normed_ref[tower, rows, :] = normed
            inverse_ref[tower, rows, :] = inverse
            length_ref[tower, rows, :] = inv_length

    loss = jnp.zeros((1, 1), jnp.float32)
    for first in range(0, group_rows, chunk):
        rows = pl.ds(first, chunk)
        scores = lax.dot_general(
            short_ref[0, rows, :], short_ref[1], (((1,), (1,)), ((), ())), preferred_element_type=jnp.float32
        )
        score_similarity_table = score_sharpness_factor * scores + score_shift_amount
        labels = jnp.where(partner_of_image[first : first + chunk] == text_row, 1.0, -1.0)
        kept = image_real[first : first + chunk] & text_real
        margin = -labels * score_similarity_table
        decay = jnp.exp(-jnp.abs(margin))
        softplus = jnp.maximum(margin, 0.0) + jnp.log1p(decay)
        loss = loss + jnp.sum(jnp.where(kept, softplus, 0.0), axis=(0, 1), keepdims=True)
        sigmoid = jnp.where(margin >= 0.0, 1.0, decay) / (1.0 + decay)
        weights = jnp.where(kept, -labels * sigmoid, 0.0) * grad_factor
        weights_ref[rows, :] = weights.astype(weights_ref.dtype)

    for tower, grad_ref in enumerate((image_grad_ref, text_grad_ref)):
        gain_sum = jnp.zeros((1, width), jnp.float32)
        for first in range(0, group_rows, chunk):
            rows = pl.ds(first, chunk)
            if tower == 0:
                pairs = weights_ref[rows, :]
                contract = (((1,), (0,)), ((), ()))
            else:
                pairs = weights_ref[:, rows]
                contract = (((0,), (0,)), ((), ()))
            direction = score_sharpness_factor * lax.dot_general(
                pairs, short_ref[1 - tower], contract, preferred_element_type=jnp.float32
            )
            unit_rows = unit_ref[tower, rows, :]
            normed = normed_ref[tower, rows, :]
            tangent = (
                direction - unit_rows * jnp.sum(unit_rows * direction, axis=-1, keepdims=True)
            ) * length_ref[tower, rows, :]
            gain_sum = gain_sum + jnp.sum(tangent * normed, axis=0, keepdims=True)
            tangent_ref[rows, :] = tangent
        sums_ref[tower : tower + 1, :] = gain_sum
        own = pl.ds(pl.multiple_of(own_block * block_rows, block_rows), block_rows)
        normed = normed_ref[tower, own, :]
        scaled_back = tangent_ref[own, :] * gains[tower]
        gradient = (
            scaled_back
            - jnp.mean(scaled_back, axis=-1, keepdims=True)
            - normed * jnp.mean(scaled_back * normed, axis=-1, keepdims=True)
        ) * inverse_ref[tower, own, :]
        grad_ref[0] = gradient.astype(grad_ref.dtype)
    first_lane = lax.broadcasted_iota(jnp.int32, (1, width), 1) == 0
    sums_ref[2:3, :] = jnp.where(first_lane, loss / real_count, 0.0)


def whole_group(
    picture_averaged_features,
    caption_averaged_features,
    picture_rescale_factor,
    caption_rescale_factor,
    exponent_of_sharpness,
    score_shift_term,
    objective_multiplier,
    matching_caption_index,
    genuine_entry_counts,
):
    count = lax.axis_size("blk")
    block_rows, width = picture_averaged_features.shape[1:]
    group_rows = count * block_rows
    pieces, masks, unused = gather_blocks(picture_averaged_features, caption_averaged_features, "blk")
    smem = pltpu.MemorySpace.SMEM
    vmem = pltpu.MemorySpace.VMEM
    grad_shape = jax.ShapeDtypeStruct(picture_averaged_features.shape, jnp.bfloat16)
    full = (2, group_rows, width)
    column = (2, group_rows, 1)
    image_grad, text_grad, sums = pl.pallas_call(
        functools.partial(group_kernel, tuple(masks[:count]), tuple(masks[count:])),
        out_shape=(grad_shape, grad_shape, jax.ShapeDtypeStruct((3, width), jnp.float32)),
        in_specs=[pl.BlockSpec(memory_space=smem)] * 4
        + [pl.BlockSpec(memory_space=vmem)] * 3
        + [pl.BlockSpec(memory_space=vmem)] * len(pieces),
        out_specs=(pl.BlockSpec(memory_space=vmem),) * 3,
        scratch_shapes=[
            pltpu.VMEM(full, jnp.bfloat16),
            pltpu.VMEM(full, jnp.float32),
            pltpu.VMEM(full, jnp.bfloat16),
            pltpu.VMEM(full, jnp.float32),
            pltpu.VMEM(column, jnp.float32),
            pltpu.VMEM(column, jnp.float32),
            pltpu.VMEM((group_rows, group_rows), jnp.bfloat16),
            pltpu.VMEM((group_rows, width), jnp.float32),
            pltpu.SemaphoreType.DMA((len(pieces),)),
        ],
    )(
        exponent_of_sharpness,
        score_shift_term,
        objective_multiplier,
        genuine_entry_counts,
        picture_rescale_factor,
        caption_rescale_factor,
        matching_caption_index,
        *[piece if slot % count == 0 else pltpu.with_memory_space_constraint(piece, pltpu.VMEM) for slot, piece in enumerate(pieces)],
    )
    group_loss = sums[2, 0:1]
    gain_grads = all_sum(sums, "rep", keep=2)
    return (image_grad, text_grad, gain_grads, group_loss)


def shards(
    picture_averaged_features,
    caption_averaged_features,
    picture_rescale_factor,
    caption_rescale_factor,
    exponent_of_sharpness,
    score_shift_term,
    objective_multiplier,
    matching_caption_index,
    genuine_entry_counts,
):
    width = picture_averaged_features.shape[2]
    first, second = embed_both(
        picture_averaged_features, caption_averaged_features, picture_rescale_factor, caption_rescale_factor
    )
    pieces, masks, offsets = gather_blocks(first, second, "blk")

    smem = pltpu.MemorySpace.SMEM
    vmem = pltpu.MemorySpace.VMEM
    grad_shape = jax.ShapeDtypeStruct(picture_averaged_features.shape, jnp.bfloat16)
    image_grad, text_grad, sums = pl.pallas_call(
        functools.partial(grad_kernel, tuple(masks), tuple(offsets)),
        out_shape=(grad_shape, grad_shape, jax.ShapeDtypeStruct((3, width), jnp.float32)),
        in_specs=[pl.BlockSpec(memory_space=smem)] * 4
        + [pl.BlockSpec(memory_space=vmem)] * 5
        + [pl.BlockSpec(memory_space=pl.ANY)] * len(pieces),
        out_specs=(pl.BlockSpec(memory_space=vmem),) * 3,
        scratch_shapes=[
            pltpu.VMEM((2, len(pieces) * pieces[0].shape[1], width), pieces[0].dtype),
            pltpu.SemaphoreType.DMA((len(pieces),)),
        ],
    )(
        exponent_of_sharpness,
        score_shift_term,
        objective_multiplier,
        genuine_entry_counts,
        picture_averaged_features,
        caption_averaged_features,
        picture_rescale_factor,
        caption_rescale_factor,
        matching_caption_index,
        *pieces,
    )

    group_sums = all_sum(sums, "blk")
    group_loss = group_sums[2, 0:1]
    gain_grads = all_sum(group_sums, "rep", keep=2)
    return (image_grad, text_grad, gain_grads, group_loss)


def body(*args):
    group_rows = args[0].shape[1] * lax.axis_size("blk")
    return (whole_group if group_rows <= 512 else shards)(*args)


def solution(mesh):
    placed = (
        P("rep", "blk", None),
        P("rep", "blk", None),
        P(),
        P(),
        P(),
        P(),
        P(),
        P("rep", None),
        P("rep", None),
    )
    return jax.shard_map(
        body,
        mesh=mesh,
        in_specs=placed,
        out_specs=(P("rep", "blk", None), P("rep", "blk", None), P(), P("rep")),
        check_vma=False,
    )
```

```python
import functools

import jax
import jax.numpy as jnp
from jax import lax
from jax.sharding import PartitionSpec as P
from jax.experimental import pallas as pl
from jax.experimental.pallas import tpu as pltpu

epsilon = 1e-06


def xor_swap(value, axis, bit):
    count = lax.axis_size(axis)
    return lax.ppermute(value, axis, [(source, source ^ bit) for source in range(count)])


def power_of_two(count):
    return count > 1 and count & (count - 1) == 0


def gather_blocks(first, second, axis):
    count = lax.axis_size(axis)
    half = first.shape[1]
    if not power_of_two(count) or count < 4:
        own = lax.axis_index(axis)
        pieces = [lax.all_gather(part, axis, axis=1, tiled=False) for part in (first, second)]
        pieces = [
            lax.dynamic_index_in_dim(part, own ^ mask, axis=1, keepdims=False)
            for part in pieces
            for mask in range(count)
        ]
        return pieces, list(range(count)) * 2, [0] * count + [half] * count
    chip_bits = [1 << b for b in range(1, count.bit_length() - 1)]
    orders = (chip_bits, chip_bits[::-1])
    routed = ([first], [second])
    routed_masks = ([0], [0])
    fresh = ([0], [0])
    shared = ([], [])
    shared_masks = ([], [])
    for step in range(len(chip_bits) + 1):
        last = step == len(chip_bits)
        sent = [None, None]
        if not last:
            sent = [xor_swap(tuple(routed[h]), axis, orders[h][step]) for h in range(2)]
        across = [xor_swap(tuple(routed[h][i] for i in fresh[h]), axis, 1) for h in range(2)]
        for h in range(2):
            shared[h].extend(across[h])
            shared_masks[h].extend([routed_masks[h][i] ^ 1 for i in fresh[h]])
            if not last:
                bit = orders[h][step]
                fresh[h][:] = list(range(len(routed[h]), 2 * len(routed[h])))
                routed[h].extend(sent[h])
                routed_masks[h].extend([mask ^ bit for mask in routed_masks[h]])
    gathered = routed[0] + shared[0] + routed[1] + shared[1]
    masks = routed_masks[0] + shared_masks[0] + routed_masks[1] + shared_masks[1]
    offsets = [0] * count + [half] * count
    return gathered, masks, offsets


def all_sum(value, axis, keep=None):
    keep = value.shape[0] if keep is None else keep
    count = lax.axis_size(axis)
    if not power_of_two(count):
        return lax.psum(value, axis)[:keep]
    bit = 1
    while bit < count:
        if bit * 2 < count:
            value = value + xor_swap(value, axis, bit)
        else:
            value = value[:keep] + xor_swap(value, axis, bit)[:keep]
        bit *= 2
    return value


def embed_kernel(picture_ref, caption_ref, picture_gain_ref, caption_gain_ref, first_ref, second_ref):
    half = first_ref.shape[1]
    towers = ((picture_ref, picture_gain_ref), (caption_ref, caption_gain_ref))
    for tower, (pooled_ref, gain_ref) in enumerate(towers):
        values = pooled_ref[0].astype(jnp.float32)
        centred = values - jnp.mean(values, axis=-1, keepdims=True)
        inverse = lax.rsqrt(jnp.mean(centred * centred, axis=-1, keepdims=True) + epsilon)
        scaled = centred * inverse * gain_ref[...][None, :]
        inv_length = lax.rsqrt(jnp.sum(scaled * scaled, axis=-1, keepdims=True) + epsilon)
        unit_rows = (scaled * inv_length).astype(first_ref.dtype)
        first_ref[tower] = unit_rows[:half]
        second_ref[tower] = unit_rows[half:]


def embed_both(picture, caption, picture_gain, caption_gain):
    rows, width = picture.shape[1:]
    vmem = pltpu.MemorySpace.VMEM
    half = jax.ShapeDtypeStruct((2, rows // 2, width), jnp.bfloat16)
    return pl.pallas_call(
        embed_kernel,
        out_shape=(half, half),
        in_specs=[pl.BlockSpec(memory_space=vmem)] * 4,
        out_specs=(pl.BlockSpec(memory_space=vmem), pl.BlockSpec(memory_space=vmem)),
    )(picture, caption, picture_gain, caption_gain)


def grad_kernel(masks, offsets, *refs):
    (sharpness_ref, shift_ref, multiplier_ref, counts_ref, picture_ref, caption_ref, picture_gain_ref,
     caption_gain_ref, partner_ref) = refs[:9]
    pieces = refs[9 : 9 + len(masks)]
    image_grad_ref, text_grad_ref, sums_ref, gathered_ref, copy_sems = refs[9 + len(masks) :]
    piece = pieces[0].shape[1]
    arrivals = [
        pltpu.make_async_copy(
            source, gathered_ref.at[:, position * piece : (position + 1) * piece, :], copy_sems.at[position]
        )
        for position, source in enumerate(pieces)
    ]
    for arrival in arrivals:
        arrival.start()
    blocks = counts_ref.shape[1]
    own_block = lax.axis_index("blk")
    block_rows = picture_ref.shape[1]
    width = picture_ref.shape[2]
    group_rows = gathered_ref.shape[1]
    own_start = own_block * block_rows
    total = counts_ref[0, 0]
    for block in range(1, blocks):
        total = total + counts_ref[0, block]
    real_count = jnp.full((1, 1), total, jnp.int32).astype(jnp.float32)
    score_sharpness_factor = jnp.exp(jnp.full((1, 1), sharpness_ref[0], jnp.float32))
    score_shift_amount = jnp.full((1, 1), shift_ref[0], jnp.float32)
    grad_factor = jnp.full((1, 1), multiplier_ref[0], jnp.float32) / real_count

    lane = lax.broadcasted_iota(jnp.int32, (1, group_rows), 1)
    held_row = jnp.zeros((1, group_rows), jnp.int32)
    limit = jnp.zeros((1, group_rows), jnp.int32)
    for position, (mask, offset) in enumerate(zip(masks, offsets)):
        block = own_block ^ mask
        here = lane // piece == position
        held_row = jnp.where(here, block * block_rows + offset + lane % piece, held_row)
        limit = jnp.where(here, counts_ref[0, block], limit)
    real_group = (held_row % block_rows) < limit
    sub = lax.broadcasted_iota(jnp.int32, (block_rows, 1), 0)
    real_own = sub < counts_ref[0, own_block]
    kept = real_own & real_group

    natural = lax.broadcasted_iota(jnp.int32, (block_rows, group_rows), 1)
    own_index = own_start + lax.broadcasted_iota(jnp.int32, (block_rows, group_rows), 0)
    partner_row = partner_ref[...]
    own_partner = jnp.sum(
        jnp.where(natural == own_index, partner_row.astype(jnp.float32), 0.0), axis=1, keepdims=True
    ).astype(jnp.int32)
    matched_image = jnp.sum(
        jnp.where(partner_row == own_index, natural.astype(jnp.float32), 0.0), axis=1, keepdims=True
    ).astype(jnp.int32)
    positives = (own_partner == held_row, matched_image == held_row)

    start_b = len(masks) // 2 * piece
    for arrival in arrivals:
        arrival.wait()
    loss_rows = []
    towers = ((picture_ref, picture_gain_ref, image_grad_ref), (caption_ref, caption_gain_ref, text_grad_ref))
    for tower, (pooled_ref, gain_ref, grad_ref) in enumerate(towers):
        values = pooled_ref[0].astype(jnp.float32)
        gain = gain_ref[...][None, :]
        centred = values - jnp.mean(values, axis=-1, keepdims=True)
        inverse = lax.rsqrt(jnp.mean(centred * centred, axis=-1, keepdims=True) + epsilon)
        normed = centred * inverse
        scaled = normed * gain
        inv_length = lax.rsqrt(jnp.sum(scaled * scaled, axis=-1, keepdims=True) + epsilon)
        unit_rows = scaled * inv_length

        own = jnp.concatenate(
            [gathered_ref[tower, 0:piece, :], gathered_ref[tower, start_b : start_b + piece, :]], axis=0
        )
        other = gathered_ref[1 - tower]
        scores = lax.dot_general(own, other, (((1,), (1,)), ((), ())), preferred_element_type=jnp.float32)
        score_similarity_table = score_sharpness_factor * scores + score_shift_amount
        labels = jnp.where(positives[tower], 1.0, -1.0)
        margin = -labels * score_similarity_table
        if tower == 0:
            softplus = jnp.maximum(margin, 0.0) + jnp.log1p(jnp.exp(-jnp.abs(margin)))
            loss_rows.append(jnp.sum(jnp.where(kept, softplus, 0.0), axis=(0, 1), keepdims=True))
        weights = jnp.where(kept, -labels * jax.nn.sigmoid(margin), 0.0) * grad_factor
        direction = score_sharpness_factor * jnp.dot(
            weights.astype(jnp.bfloat16), other, preferred_element_type=jnp.float32
        )
        tangent = (
            direction - unit_rows * jnp.sum(unit_rows * direction, axis=-1, keepdims=True)
        ) * inv_length
        sums_ref[tower : tower + 1, :] = jnp.sum(tangent * normed, axis=0, keepdims=True)
        scaled_back = tangent * gain
        gradient = (
            scaled_back
            - jnp.mean(scaled_back, axis=-1, keepdims=True)
            - normed * jnp.mean(scaled_back * normed, axis=-1, keepdims=True)
        ) * inverse
        grad_ref[0] = gradient.astype(grad_ref.dtype)
    first_lane = lax.broadcasted_iota(jnp.int32, (1, width), 1) == 0
    sums_ref[2:3, :] = jnp.where(first_lane, loss_rows[0] / real_count, 0.0)


def group_kernel(image_masks, text_masks, *refs):
    (sharpness_ref, shift_ref, multiplier_ref, counts_ref, picture_gain_ref, caption_gain_ref,
     partner_ref) = refs[:7]
    count = len(image_masks)
    pieces = refs[7 : 7 + 2 * count]
    (image_grad_ref, text_grad_ref, sums_ref, raw_ref, unit_ref, short_ref, normed_ref, inverse_ref,
     length_ref, weights_ref, tangent_ref, copy_sems) = refs[7 + 2 * count :]
    block_rows = pieces[0].shape[1]
    group_rows = count * block_rows
    width = pieces[0].shape[2]
    own_block = lax.axis_index("blk")

    def block_of(mask):
        block = own_block
        for bit in range(mask.bit_length()):
            if mask >> bit & 1:
                block = block + (1 - 2 * (own_block // (1 << bit) % 2)) * (1 << bit)
        return block


    blocks = counts_ref.shape[1]
    total = counts_ref[0, 0]
    for block in range(1, blocks):
        total = total + counts_ref[0, block]
    real_count = jnp.full((1, 1), total, jnp.int32).astype(jnp.float32)
    score_sharpness_factor = jnp.exp(jnp.full((1, 1), sharpness_ref[0], jnp.float32))
    score_shift_amount = jnp.full((1, 1), shift_ref[0], jnp.float32)
    grad_factor = jnp.full((1, 1), multiplier_ref[0], jnp.float32) / real_count

    def held(shape, dim):
        row = lax.broadcasted_iota(jnp.int32, shape, dim)
        limit = jnp.zeros(shape, jnp.int32)
        for block in range(blocks):
            limit = jnp.where(row // block_rows == block, counts_ref[0, block], limit)
        return row, (row % block_rows) < limit

    image_row, image_real = held((group_rows, 1), 0)
    text_row, text_real = held((1, group_rows), 1)
    natural = lax.broadcasted_iota(jnp.int32, (group_rows, group_rows), 1)
    partner_of_image = jnp.sum(
        jnp.where(natural == image_row, partner_ref[...].astype(jnp.float32), 0.0), axis=1, keepdims=True
    ).astype(jnp.int32)

    gains = (picture_gain_ref[...][None, :], caption_gain_ref[...][None, :])
    chunk = min(256, group_rows)
    for position, source in enumerate(pieces):
        tower, slot = divmod(position, count)
        masks = image_masks if tower == 0 else text_masks
        rows = pl.ds(pl.multiple_of(block_of(masks[slot]) * block_rows, block_rows), block_rows)
        if source is not None:
            values = source[0].astype(jnp.float32)
            centred = values - jnp.mean(values, axis=-1, keepdims=True)
            inverse = lax.rsqrt(jnp.mean(centred * centred, axis=-1, keepdims=True) + epsilon)
            normed = centred * inverse
            scaled = normed * gains[tower]
            inv_length = lax.rsqrt(jnp.sum(scaled * scaled, axis=-1, keepdims=True) + epsilon)
            unit_rows = scaled * inv_length
            unit_ref[tower, rows, :] = unit_rows
            short_ref[tower, rows, :] = unit_rows.astype(short_ref.dtype)
            normed_ref[tower, rows, :] = normed
            inverse_ref[tower, rows, :] = inverse
            length_ref[tower, rows, :] = inv_length

    loss = jnp.zeros((1, 1), jnp.float32)
    for first in range(0, group_rows, chunk):
        rows = pl.ds(first, chunk)
        scores = lax.dot_general(
            short_ref[0, rows, :], short_ref[1], (((1,), (1,)), ((), ())), preferred_element_type=jnp.float32
        )
        score_similarity_table = score_sharpness_factor * scores + score_shift_amount
        labels = jnp.where(partner_of_image[first : first + chunk] == text_row, 1.0, -1.0)
        kept = image_real[first : first + chunk] & text_real
        margin = -labels * score_similarity_table
        decay = jnp.exp(-jnp.abs(margin))
        softplus = jnp.maximum(margin, 0.0) + jnp.log1p(decay)
        loss = loss + jnp.sum(jnp.where(kept, softplus, 0.0), axis=(0, 1), keepdims=True)
        sigmoid = jnp.where(margin >= 0.0, 1.0, decay) / (1.0 + decay)
        weights = jnp.where(kept, -labels * sigmoid, 0.0) * grad_factor
        weights_ref[rows, :] = weights.astype(weights_ref.dtype)

    for tower, grad_ref in enumerate((image_grad_ref, text_grad_ref)):
        gain_sum = jnp.zeros((1, width), jnp.float32)
        for first in range(0, group_rows, chunk):
            rows = pl.ds(first, chunk)
            if tower == 0:
                pairs = weights_ref[rows, :]
                contract = (((1,), (0,)), ((), ()))
            else:
                pairs = weights_ref[:, rows]
                contract = (((0,), (0,)), ((), ()))
            direction = score_sharpness_factor * lax.dot_general(
                pairs, short_ref[1 - tower], contract, preferred_element_type=jnp.float32
            )
            unit_rows = unit_ref[tower, rows, :]
            normed = normed_ref[tower, rows, :]
            tangent = (
                direction - unit_rows * jnp.sum(unit_rows * direction, axis=-1, keepdims=True)
            ) * length_ref[tower, rows, :]
            gain_sum = gain_sum + jnp.sum(tangent * normed, axis=0, keepdims=True)
            tangent_ref[rows, :] = tangent
        sums_ref[tower : tower + 1, :] = gain_sum
        own = pl.ds(pl.multiple_of(own_block * block_rows, block_rows), block_rows)
        normed = normed_ref[tower, own, :]
        scaled_back = tangent_ref[own, :] * gains[tower]
        gradient = (
            scaled_back
            - jnp.mean(scaled_back, axis=-1, keepdims=True)
            - normed * jnp.mean(scaled_back * normed, axis=-1, keepdims=True)
        ) * inverse_ref[tower, own, :]
        grad_ref[0] = gradient.astype(grad_ref.dtype)
    first_lane = lax.broadcasted_iota(jnp.int32, (1, width), 1) == 0
    sums_ref[2:3, :] = jnp.where(first_lane, loss / real_count, 0.0)


def whole_group(
    picture_averaged_features,
    caption_averaged_features,
    picture_rescale_factor,
    caption_rescale_factor,
    exponent_of_sharpness,
    score_shift_term,
    objective_multiplier,
    matching_caption_index,
    genuine_entry_counts,
):
    count = lax.axis_size("blk")
    block_rows, width = picture_averaged_features.shape[1:]
    group_rows = count * block_rows
    pieces, masks, unused = gather_blocks(picture_averaged_features, caption_averaged_features, "blk")
    smem = pltpu.MemorySpace.SMEM
    vmem = pltpu.MemorySpace.VMEM
    grad_shape = jax.ShapeDtypeStruct(picture_averaged_features.shape, jnp.bfloat16)
    full = (2, group_rows, width)
    column = (2, group_rows, 1)
    image_grad, text_grad, sums = pl.pallas_call(
        functools.partial(group_kernel, tuple(masks[:count]), tuple(masks[count:])),
        out_shape=(grad_shape, grad_shape, jax.ShapeDtypeStruct((3, width), jnp.float32)),
        in_specs=[pl.BlockSpec(memory_space=smem)] * 4
        + [pl.BlockSpec(memory_space=vmem)] * 3
        + [pl.BlockSpec(memory_space=vmem)] * len(pieces),
        out_specs=(pl.BlockSpec(memory_space=vmem),) * 3,
        scratch_shapes=[
            pltpu.VMEM(full, jnp.bfloat16),
            pltpu.VMEM(full, jnp.float32),
            pltpu.VMEM(full, jnp.bfloat16),
            pltpu.VMEM(full, jnp.float32),
            pltpu.VMEM(column, jnp.float32),
            pltpu.VMEM(column, jnp.float32),
            pltpu.VMEM((group_rows, group_rows), jnp.bfloat16),
            pltpu.VMEM((group_rows, width), jnp.float32),
            pltpu.SemaphoreType.DMA((len(pieces),)),
        ],
    )(
        exponent_of_sharpness,
        score_shift_term,
        objective_multiplier,
        genuine_entry_counts,
        picture_rescale_factor,
        caption_rescale_factor,
        matching_caption_index,
        *[piece if slot % count == 0 else pltpu.with_memory_space_constraint(piece, pltpu.VMEM) for slot, piece in enumerate(pieces)],
    )
    group_loss = sums[2, 0:1]
    gain_grads = all_sum(sums, "rep", keep=2)
    return (image_grad, text_grad, gain_grads, group_loss)


def shards(
    picture_averaged_features,
    caption_averaged_features,
    picture_rescale_factor,
    caption_rescale_factor,
    exponent_of_sharpness,
    score_shift_term,
    objective_multiplier,
    matching_caption_index,
    genuine_entry_counts,
):
    width = picture_averaged_features.shape[2]
    first, second = embed_both(
        picture_averaged_features, caption_averaged_features, picture_rescale_factor, caption_rescale_factor
    )
    pieces, masks, offsets = gather_blocks(first, second, "blk")

    smem = pltpu.MemorySpace.SMEM
    vmem = pltpu.MemorySpace.VMEM
    grad_shape = jax.ShapeDtypeStruct(picture_averaged_features.shape, jnp.bfloat16)
    image_grad, text_grad, sums = pl.pallas_call(
        functools.partial(grad_kernel, tuple(masks), tuple(offsets)),
        out_shape=(grad_shape, grad_shape, jax.ShapeDtypeStruct((3, width), jnp.float32)),
        in_specs=[pl.BlockSpec(memory_space=smem)] * 4
        + [pl.BlockSpec(memory_space=vmem)] * 5
        + [pl.BlockSpec(memory_space=pl.ANY)] * len(pieces),
        out_specs=(pl.BlockSpec(memory_space=vmem),) * 3,
        scratch_shapes=[
            pltpu.VMEM((2, len(pieces) * pieces[0].shape[1], width), pieces[0].dtype),
            pltpu.SemaphoreType.DMA((len(pieces),)),
        ],
    )(
        exponent_of_sharpness,
        score_shift_term,
        objective_multiplier,
        genuine_entry_counts,
        picture_averaged_features,
        caption_averaged_features,
        picture_rescale_factor,
        caption_rescale_factor,
        matching_caption_index,
        *pieces,
    )

    group_sums = all_sum(sums, "blk")
    group_loss = group_sums[2, 0:1]
    gain_grads = all_sum(group_sums, "rep", keep=2)
    return (image_grad, text_grad, gain_grads, group_loss)


def body(*args):
    group_rows = args[0].shape[1] * lax.axis_size("blk")
    return (whole_group if group_rows <= 512 else shards)(*args)


def solution(mesh):
    placed = (
        P("rep", "blk", None),
        P("rep", "blk", None),
        P(),
        P(),
        P(),
        P(),
        P(),
        P("rep", None),
        P("rep", None),
    )
    return jax.shard_map(
        body,
        mesh=mesh,
        in_specs=placed,
        out_specs=(P("rep", "blk", None), P("rep", "blk", None), P(), P("rep")),
        check_vma=False,
    )
```
